32 devices in a mesh: chan: 8 (over y, x, core), win: 4 (over z).
Axes of the slice: x: 2, y: 2, z: 4, core: 2. Of those that a mesh axis runs over, the one named last changes fastest.
Arguments:
- record: bfloat16 [3, 1024, 32768], P(None, 'chan', 'win'), may hold values from -6 to 6
- chan_taps: float32 [33], replicated, may hold values from -1 to 1
- time_taps: float32 [65], replicated, may hold values from -0.75 to 0.75
- sources: int32 [3, 4], replicated, may hold values from 0 to 1023
Outputs:
- stacked: float32 [3, 4, 129, 1024], P(None, None, None, 'chan')
The draws below stay inside these ranges and needn't reach their ends.
Inputs may be any that keep to these rules, and one draw needn't show every extreme that they name: `sources`: channel numbers of the fibre.
All inputs are finite; a program needn't handle non-finite values.
Results may differ from the reference program's by a relative error of at most 0.006.
Values may be sent and summed in bfloat16 or wider, within the bound.
No kernel may reach another device: no remote copies, remote signals or barrier semaphores. Data moves between devices by JAX's collectives and lax.ppermute only.
A program may use at most 128 MiB of HBM per device.

```python
import math
import jax
import jax.numpy as jnp
from jax import lax

SAMP = 8192
STEPS = 3
SRC = 4
LAG = 64
CH_HALF = 16
TM_HALF = 32
CHANNELS = 1024
WINDOWS = 4


def with_ends(entries, stream_key, smallest, high):
    longest = entries.shape.index(max(entries.shape))
    spots = []
    for shift in (0, 1):
        where = [jax.random.randint(jax.random.fold_in(stream_key, axis), (), 0, length) for axis, length in enumerate(entries.shape)]
        where[longest] = (where[longest] + shift) % entries.shape[longest]
        spots.append(tuple(where))
    return entries.at[spots[0]].set(smallest).at[spots[1]].set(high)


def steps_of(rng, shape, split, low, top_value):
    loudness, own = 1.0, jax.random.fold_in(rng, 6)
    for position, parts in split:
        steps = jnp.exp(jax.random.uniform(jax.random.fold_in(own, position), (parts,), jnp.float32, low / len(split), top_value / len(split)))
        loudness = loudness * jnp.repeat(steps, shape[position] // parts).reshape([-1 if axis == position else 1 for axis in range(len(shape))])
    return loudness


def noise(stream_key, extent, width, reach, shards=(), kind=jnp.bfloat16):
    values = jax.random.normal(stream_key, extent, jnp.float32) * width
    if len(shards) > 0:
        values = steps_of(stream_key, extent, shards, -0.22, 0.18) * values
    return jnp.clip(values, min=-reach, max=reach).astype(kind)


def setup_inputs(seed: int = 0) -> dict:
    streams_of = jax.random.split(jax.random.key(seed), 5)
    return {
        "record": noise(streams_of[0], (STEPS, CHANNELS, WINDOWS * SAMP), 1.0, 6.0, ((1, 8), (2, 4))),
        "chan_taps": noise(streams_of[1], (2 * CH_HALF + 1,), (2 * CH_HALF + 1) ** -0.5, 1.0, (), jnp.float32),
        "time_taps": noise(streams_of[2], (2 * TM_HALF + 1,), (2 * TM_HALF + 1) ** -0.5, 0.75, (), jnp.float32),
        "sources": with_ends(jax.random.randint(streams_of[3], (STEPS, SRC), 0, CHANNELS), jax.random.fold_in(streams_of[3], 1), 0, CHANNELS - 1).astype(jnp.int32),
    }


def time_filter(chan_pass, tap_table):
    channels_here, samples = chan_pass.shape
    half = (tap_table.shape[0] - 1) // 2
    blocks = chan_pass.reshape(channels_here, samples // 128, 128)
    zeros_block = jnp.zeros_like(blocks[:, :1])
    earlier = jnp.concatenate([zeros_block, blocks[:, :-1]], axis=1)
    later = jnp.concatenate([blocks[:, 1:], zeros_block], axis=1)
    extended = jnp.concatenate([earlier, blocks, later], axis=2)
    offset = lax.iota(jnp.int32, 384)[:, None] - 128 - lax.iota(jnp.int32, 128)[None, :] + half
    inside = (offset >= 0) & (offset <= 2 * half)
    weights = jnp.where(inside, tap_table[jnp.clip(offset, 0, 2 * half)], jnp.zeros((), tap_table.dtype))
    result = jnp.einsum('cbr,rt->cbt', extended.astype(jnp.float32), weights.astype(jnp.float32))
    return result.reshape(channels_here, samples)

def whiten(time_pass):
    power = lax.optimization_barrier(jnp.mean(time_pass * time_pass, axis=-1, keepdims=True))
    return (time_pass * lax.rsqrt(power + 1e-06)).astype(jnp.bfloat16)

def correlate(whitened, panel):
    samples = whitened.shape[1]
    padded = jnp.pad(panel, ((0, 0), (LAG, LAG)))
    shifted = jnp.stack([padded[:, 2 * LAG - j:2 * LAG - j + samples] for j in range(2 * LAG + 1)], axis=-1)
    return jnp.einsum('cu,kuj->kjc', whitened.astype(jnp.float32), shifted.astype(jnp.float32))

def reference(record, chan_taps, time_taps, sources):
    chan_table = chan_taps.astype(jnp.bfloat16).astype(jnp.float32)
    time_table = time_taps.astype(jnp.bfloat16)
    half = (chan_taps.shape[0] - 1) // 2
    channels = record.shape[1]
    normalizer = 1.0 / math.sqrt(SAMP * WINDOWS)
    results = []
    for section in range(record.shape[0]):
        chosen = sources[section].astype(jnp.int32)

        def one_window(piece):
            padded = jnp.pad(piece.astype(jnp.float32), ((half, half), (0, 0)))
            total = jnp.zeros((channels, piece.shape[1]), jnp.float32)
            for k in range(2 * half + 1):
                total = total + chan_table[k] * padded[k:k + channels]
            chan_pass = total.astype(jnp.bfloat16)
            whitened = whiten(time_filter(chan_pass, time_table))
            panel = jnp.take(whitened, chosen, axis=0)
            return correlate(whitened, panel)
        pieces = record[section].reshape(channels, WINDOWS, SAMP).transpose(1, 0, 2)
        summed = lax.optimization_barrier(jnp.sum(lax.map(one_window, pieces), axis=0))
        results.append(summed * normalizer)
    return jnp.stack(results)
```

```python
import functools
import math

import jax
import jax.numpy as jnp
from jax import lax
from jax.experimental import pallas as pl
from jax.experimental.pallas import tpu as pltpu
from jax.sharding import PartitionSpec as P

LAG = 64


def padded_2(cells, sides, width):
    for axis, dim in sides:
        count = lax.axis_size(axis)
        ends = count - 1
        head = lax.slice_in_dim(cells, 0, width, axis=dim)
        tail = lax.slice_in_dim(cells, cells.shape[dim] - width, cells.shape[dim], axis=dim)
        cells = jnp.concatenate(
            [
                lax.ppermute(tail, axis, [(i, (i + 1) % count) for i in range(ends)]),
                cells,
                lax.ppermute(head, axis, [((i + 1) % count, i) for i in range(ends)]),
            ],
            axis=dim,
        )
    return cells


def tap_lookup(offset, tap_table):
    count_taps = tap_table.shape[0]
    marks = offset[..., None] == lax.iota(jnp.int32, count_taps)
    picked = jnp.where(marks, tap_table.astype(jnp.float32), jnp.zeros((), jnp.float32))
    return jnp.sum(picked, axis=-1).astype(tap_table.dtype)


def band_matrix(tap_table, height, breadth):
    offset = lax.iota(jnp.int32, breadth)[None, :] - lax.iota(jnp.int32, height)[:, None]
    return tap_lookup(offset, tap_table)


def time_filter(chan_pass, tap_table):
    channels_here, samples = chan_pass.shape
    half = (tap_table.shape[0] - 1) // 2
    blocks = chan_pass.reshape(channels_here, samples // 128, 128)
    zeros_block = jnp.zeros_like(blocks[:, :1])
    earlier = jnp.concatenate([zeros_block, blocks[:, :-1]], axis=1)
    later = jnp.concatenate([blocks[:, 1:], zeros_block], axis=1)
    extended = jnp.concatenate([earlier, blocks, later], axis=2)
    offset = lax.iota(jnp.int32, 384)[:, None] - 128 - lax.iota(jnp.int32, 128)[None, :] + half
    weights = tap_lookup(offset, tap_table)
    result = jnp.einsum("cbr,rt->cbt", extended, weights, preferred_element_type=jnp.float32)
    return result.reshape(channels_here, samples)


def whiten(time_pass):
    power = jnp.mean(time_pass * time_pass, axis=-1, keepdims=True)
    return (time_pass * lax.rsqrt(power + 1e-06)).astype(jnp.bfloat16)


def corr_body(nb, rows, w_ref, p_ref, o_ref, s_ref):
    n = pl.program_id(0)
    k_count = p_ref.shape[0]
    lanes = 128

    @pl.when(n == 0)
    def _():
        o_ref[...] = jnp.zeros_like(o_ref)

    j_idx = lax.broadcasted_iota(jnp.int32, (rows, lanes), 0)
    r_idx = lax.broadcasted_iota(jnp.int32, (rows, lanes), 1)
    upper = r_idx >= j_idx
    for k in range(k_count):
        rolled = []
        for b in range(nb + 1):
            start = pl.multiple_of((n * nb + b) * lanes, lanes)
            chunk = p_ref[pl.ds(k, 1), pl.ds(start, lanes)]
            wide = jnp.broadcast_to(chunk, (rows, lanes))
            rolled.append(pltpu.roll(wide, 0, 1, stride=1, stride_axis=0))
        for b in range(nb):
            piece = jnp.where(upper, rolled[b + 1], rolled[b])
            s_ref[pl.ds(k * rows, rows), pl.ds(b * lanes, lanes)] = piece.astype(s_ref.dtype)
    o_ref[...] += lax.dot_general(
        s_ref[...], w_ref[...], (((1,), (1,)), ((), ())),
        preferred_element_type=jnp.float32)


def correlate_kernel(whitened, panel, nb=8):
    chans, samples = whitened.shape
    k_count = panel.shape[0]
    lanes = 128
    rows = 136
    padded = jnp.pad(panel.astype(jnp.float32), ((0, 0), (LAG, LAG)))
    grid = samples // (nb * lanes)
    out = pl.pallas_call(
        functools.partial(corr_body, nb, rows),
        grid=(grid,),
        in_specs=[
            pl.BlockSpec((chans, nb * lanes), lambda n: (0, n)),
            pl.BlockSpec((k_count, samples + 2 * LAG), lambda n: (0, 0)),
        ],
        out_specs=pl.BlockSpec((k_count * rows, chans), lambda n: (0, 0)),
        out_shape=jax.ShapeDtypeStruct((k_count * rows, chans), jnp.float32),
        scratch_shapes=[pltpu.VMEM((k_count * rows, nb * lanes), jnp.bfloat16)],
        compiler_params=pltpu.CompilerParams(dimension_semantics=("arbitrary",)),
    )(whitened, padded)
    return out.reshape(k_count, rows, chans)[:, : 2 * LAG + 1, :]


def chan_filter(piece, tap_table):
    channels_here = piece.shape[0]
    half = (tap_table.shape[0] - 1) // 2
    widened = padded_2(piece, (("chan", 0),), half)
    total = jnp.dot(
        band_matrix(tap_table, channels_here, channels_here + 2 * half),
        widened,
        preferred_element_type=jnp.float32,
    )
    return total.astype(jnp.bfloat16)


def xor_sum(x, axis):
    count = lax.axis_size(axis)
    if count & (count - 1):
        return lax.psum(x, axis)
    step = 1
    while step < count:
        x = x + lax.ppermute(x, axis, [(i, i ^ step) for i in range(count)])
        step *= 2
    return x


def body(record, chan_taps, time_taps, sources):
    count_steps = record.shape[0]
    channels_here = record.shape[1]
    samples = record.shape[2]
    chan_table = chan_taps.astype(jnp.bfloat16)
    time_table = time_taps.astype(jnp.bfloat16)
    first_chan = lax.axis_index("chan") * channels_here
    selector = (
        (sources - first_chan)[:, :, None] == lax.iota(jnp.int32, channels_here)[None, None, :]
    ).astype(jnp.bfloat16)
    normalizer = 1.0 / math.sqrt(samples * lax.axis_size("win"))

    results = []
    for section in range(count_steps):
        whitened = whiten(time_filter(chan_filter(record[section], chan_table), time_table))
        term = jnp.dot(selector[section], whitened, preferred_element_type=jnp.float32)
        panel = xor_sum(term.astype(jnp.bfloat16), "chan")
        partial_corr = correlate_kernel(whitened, panel)
        results.append(xor_sum(partial_corr, "win"))
    return jnp.stack(results) * normalizer


def solution(mesh):
    in_specs = (P(None, "chan", "win"), P(), P(), P())
    out_specs = P(None, None, None, "chan")
    return jax.shard_map(body, mesh=mesh, in_specs=in_specs, out_specs=out_specs, check_vma=False)
```

```python
import functools
import math

import jax
import jax.numpy as jnp
from jax import lax
from jax.experimental import pallas as pl
from jax.experimental.pallas import tpu as pltpu
from jax.sharding import PartitionSpec as P

LAG = 64


def padded_2(cells, sides, width):
    for axis, dim in sides:
        count = lax.axis_size(axis)
        ends = count - 1
        head = lax.slice_in_dim(cells, 0, width, axis=dim)
        tail = lax.slice_in_dim(cells, cells.shape[dim] - width, cells.shape[dim], axis=dim)
        cells = jnp.concatenate(
            [
                lax.ppermute(tail, axis, [(i, (i + 1) % count) for i in range(ends)]),
                cells,
                lax.ppermute(head, axis, [((i + 1) % count, i) for i in range(ends)]),
            ],
            axis=dim,
        )
    return cells


def tap_lookup(offset, tap_table):
    count_taps = tap_table.shape[0]
    marks = offset[..., None] == lax.iota(jnp.int32, count_taps)
    picked = jnp.where(marks, tap_table.astype(jnp.float32), jnp.zeros((), jnp.float32))
    return jnp.sum(picked, axis=-1).astype(tap_table.dtype)


def band_matrix(tap_table, height, breadth):
    offset = lax.iota(jnp.int32, breadth)[None, :] - lax.iota(jnp.int32, height)[:, None]
    return tap_lookup(offset, tap_table)


def time_filter(chan_pass, tap_table):
    channels_here, samples = chan_pass.shape
    half = (tap_table.shape[0] - 1) // 2
    blocks = chan_pass.reshape(channels_here, samples // 128, 128)
    zeros_block = jnp.zeros_like(blocks[:, :1])
    earlier = jnp.concatenate([zeros_block, blocks[:, :-1]], axis=1)
    later = jnp.concatenate([blocks[:, 1:], zeros_block], axis=1)
    extended = jnp.concatenate([earlier, blocks, later], axis=2)
    offset = lax.iota(jnp.int32, 384)[:, None] - 128 - lax.iota(jnp.int32, 128)[None, :] + half
    weights = tap_lookup(offset, tap_table)
    result = jnp.einsum("cbr,rt->cbt", extended, weights, preferred_element_type=jnp.float32)
    return result.reshape(channels_here, samples)


def whiten(time_pass):
    power = jnp.mean(time_pass * time_pass, axis=-1, keepdims=True)
    return (time_pass * lax.rsqrt(power + 1e-06)).astype(jnp.bfloat16)


def corr_body(nb, rows, w_ref, p_ref, o_ref, s_ref):
    n = pl.program_id(0)
    k_count = p_ref.shape[0]
    lanes = 128

    @pl.when(n == 0)
    def _():
        o_ref[...] = jnp.zeros_like(o_ref)

    j_idx = lax.broadcasted_iota(jnp.int32, (rows, lanes), 0)
    r_idx = lax.broadcasted_iota(jnp.int32, (rows, lanes), 1)
    upper = r_idx >= j_idx
    for k in range(k_count):
        rolled = []
        for b in range(nb + 1):
            start = pl.multiple_of((n * nb + b) * lanes, lanes)
            chunk = p_ref[pl.ds(k, 1), pl.ds(start, lanes)]
            wide = jnp.broadcast_to(chunk, (rows, lanes))
            rolled.append(pltpu.roll(wide, 0, 1, stride=1, stride_axis=0))
        for b in range(nb):
            piece = jnp.where(upper, rolled[b + 1], rolled[b])
            s_ref[pl.ds(k * rows, rows), pl.ds(b * lanes, lanes)] = piece.astype(s_ref.dtype)
    o_ref[...] += lax.dot_general(
        s_ref[...], w_ref[...], (((1,), (1,)), ((), ())),
        preferred_element_type=jnp.float32)


def correlate_kernel(whitened, panel, nb=8):
    chans, samples = whitened.shape
    k_count = panel.shape[0]
    lanes = 128
    rows = 136
    padded = jnp.pad(panel.astype(jnp.float32), ((0, 0), (LAG, LAG)))
    grid = samples // (nb * lanes)
    out = pl.pallas_call(
        functools.partial(corr_body, nb, rows),
        grid=(grid,),
        in_specs=[
            pl.BlockSpec((chans, nb * lanes), lambda n: (0, n)),
            pl.BlockSpec((k_count, samples + 2 * LAG), lambda n: (0, 0)),
        ],
        out_specs=pl.BlockSpec((k_count * rows, chans), lambda n: (0, 0)),
        out_shape=jax.ShapeDtypeStruct((k_count * rows, chans), jnp.float32),
        scratch_shapes=[pltpu.VMEM((k_count * rows, nb * lanes), jnp.bfloat16)],
        compiler_params=pltpu.CompilerParams(dimension_semantics=("arbitrary",)),
        cost_estimate=pl.CostEstimate(
            flops=2 * k_count * rows * samples * chans,
            bytes_accessed=2 * chans * samples + 4 * k_count * (samples + rows * chans),
            transcendentals=0,
        ),
    )(whitened, padded)
    return out.reshape(k_count, rows, chans)[:, : 2 * LAG + 1, :]


def chan_filter(piece, tap_table):
    channels_here = piece.shape[0]
    half = (tap_table.shape[0] - 1) // 2
    widened = padded_2(piece, (("chan", 0),), half)
    total = jnp.dot(
        band_matrix(tap_table, channels_here, channels_here + 2 * half),
        widened,
        preferred_element_type=jnp.float32,
    )
    return total.astype(jnp.bfloat16)


def xor_sum(x, axis):
    count = lax.axis_size(axis)
    if count & (count - 1):
        return lax.psum(x, axis)
    step = 1
    while step < count:
        x = x + lax.ppermute(x, axis, [(i, i ^ step) for i in range(count)])
        step *= 2
    return x


def body(record, chan_taps, time_taps, sources):
    count_steps = record.shape[0]
    channels_here = record.shape[1]
    samples = record.shape[2]
    chan_table = chan_taps.astype(jnp.bfloat16)
    time_table = time_taps.astype(jnp.bfloat16)
    first_chan = lax.axis_index("chan") * channels_here
    selector = (
        (sources - first_chan)[:, :, None] == lax.iota(jnp.int32, channels_here)[None, None, :]
    ).astype(jnp.bfloat16)
    normalizer = 1.0 / math.sqrt(samples * lax.axis_size("win"))

    def prepare(piece, section):
        whitened = whiten(time_filter(chan_filter(piece, chan_table), time_table))
        term = jnp.dot(selector[section], whitened, preferred_element_type=jnp.float32)
        return whitened, xor_sum(term.astype(jnp.bfloat16), "chan")

    pieces = [record[section] for section in range(count_steps)]
    results = []
    pending = prepare(pieces[0], 0)
    for section in range(count_steps):
        upcoming = None
        if section + 1 < count_steps:
            upcoming = prepare(pieces[section + 1], section + 1)
        whitened, panel = pending
        if section >= 2:
            whitened, panel, results[section - 2] = lax.optimization_barrier(
                (whitened, panel, results[section - 2])
            )
        if section + 1 < count_steps:
            partial_corr = correlate_kernel(whitened, panel)
            if section + 2 < count_steps:
                pieces[section + 2], partial_corr = lax.optimization_barrier(
                    (pieces[section + 2], partial_corr)
                )
            results.append(xor_sum(partial_corr, "win"))
        else:
            half = panel.shape[0] // 2
            parts = [
                xor_sum(correlate_kernel(whitened, panel[:half]), "win"),
                xor_sum(correlate_kernel(whitened, panel[half:]), "win"),
            ]
            results.append(jnp.concatenate(parts, axis=0))
        pending = upcoming
    return jnp.stack(results) * normalizer


def solution(mesh):
    in_specs = (P(None, "chan", "win"), P(), P(), P())
    out_specs = P(None, None, None, "chan")
    return jax.shard_map(body, mesh=mesh, in_specs=in_specs, out_specs=out_specs, check_vma=False)
```

```python
import functools
import math

import jax
import jax.numpy as jnp
from jax import lax
from jax.experimental import pallas as pl
from jax.experimental.pallas import tpu as pltpu
from jax.sharding import PartitionSpec as P

LAG = 64


def padded_2(cells, sides, width):
    for axis, dim in sides:
        count = lax.axis_size(axis)
        ends = count - 1
        head = lax.slice_in_dim(cells, 0, width, axis=dim)
        tail = lax.slice_in_dim(cells, cells.shape[dim] - width, cells.shape[dim], axis=dim)
        cells = jnp.concatenate(
            [
                lax.ppermute(tail, axis, [(i, (i + 1) % count) for i in range(ends)]),
                cells,
                lax.ppermute(head, axis, [((i + 1) % count, i) for i in range(ends)]),
            ],
            axis=dim,
        )
    return cells


def tap_lookup(offset, tap_table):
    count_taps = tap_table.shape[0]
    marks = offset[..., None] == lax.iota(jnp.int32, count_taps)
    picked = jnp.where(marks, tap_table.astype(jnp.float32), jnp.zeros((), jnp.float32))
    return jnp.sum(picked, axis=-1).astype(tap_table.dtype)


def band_matrix(tap_table, height, breadth):
    offset = lax.iota(jnp.int32, breadth)[None, :] - lax.iota(jnp.int32, height)[:, None]
    return tap_lookup(offset, tap_table)


def time_filter(chan_pass, tap_table):
    channels_here, samples = chan_pass.shape
    half = (tap_table.shape[0] - 1) // 2
    blocks = chan_pass.reshape(channels_here, samples // 128, 128)
    zeros_block = jnp.zeros_like(blocks[:, :1])
    earlier = jnp.concatenate([zeros_block, blocks[:, :-1]], axis=1)
    later = jnp.concatenate([blocks[:, 1:], zeros_block], axis=1)
    extended = jnp.concatenate([earlier, blocks, later], axis=2)
    offset = lax.iota(jnp.int32, 384)[:, None] - 128 - lax.iota(jnp.int32, 128)[None, :] + half
    weights = tap_lookup(offset, tap_table)
    result = jnp.einsum("cbr,rt->cbt", extended, weights, preferred_element_type=jnp.float32)
    return result.reshape(channels_here, samples)


def whiten(time_pass):
    power = jnp.mean(time_pass * time_pass, axis=-1, keepdims=True)
    return (time_pass * lax.rsqrt(power + 1e-06)).astype(jnp.bfloat16)


def corr_body(nb, rows, w_ref, p_ref, o_ref, s_ref):
    n = pl.program_id(0)
    k_count = p_ref.shape[0]
    lanes = 128

    @pl.when(n == 0)
    def _():
        o_ref[...] = jnp.zeros_like(o_ref)

    j_idx = lax.broadcasted_iota(jnp.int32, (rows, lanes), 0)
    r_idx = lax.broadcasted_iota(jnp.int32, (rows, lanes), 1)
    upper = r_idx >= j_idx
    for k in range(k_count):
        rolled = []
        for b in range(nb + 1):
            start = pl.multiple_of((n * nb + b) * lanes, lanes)
            chunk = p_ref[pl.ds(k, 1), pl.ds(start, lanes)]
            wide = jnp.broadcast_to(chunk, (rows, lanes))
            rolled.append(pltpu.roll(wide, 0, 1, stride=1, stride_axis=0))
        for b in range(nb):
            piece = jnp.where(upper, rolled[b + 1], rolled[b])
            s_ref[pl.ds(k * rows, rows), pl.ds(b * lanes, lanes)] = piece.astype(s_ref.dtype)
    o_ref[...] += lax.dot_general(
        s_ref[...], w_ref[...], (((1,), (1,)), ((), ())),
        preferred_element_type=jnp.float32)


def correlate_kernel(whitened, panel, nb=8):
    chans, samples = whitened.shape
    k_count = panel.shape[0]
    lanes = 128
    rows = 136
    padded = jnp.pad(panel.astype(jnp.float32), ((0, 0), (LAG, LAG)))
    grid = samples // (nb * lanes)
    out = pl.pallas_call(
        functools.partial(corr_body, nb, rows),
        grid=(grid,),
        in_specs=[
            pl.BlockSpec((chans, nb * lanes), lambda n: (0, n)),
            pl.BlockSpec((k_count, samples + 2 * LAG), lambda n: (0, 0)),
        ],
        out_specs=pl.BlockSpec((k_count * rows, chans), lambda n: (0, 0)),
        out_shape=jax.ShapeDtypeStruct((k_count * rows, chans), jnp.float32),
        scratch_shapes=[pltpu.VMEM((k_count * rows, nb * lanes), jnp.bfloat16)],
        compiler_params=pltpu.CompilerParams(dimension_semantics=("arbitrary",)),
        cost_estimate=pl.CostEstimate(
            flops=2 * k_count * rows * samples * chans,
            bytes_accessed=2 * chans * samples + 4 * k_count * (samples + rows * chans),
            transcendentals=0,
        ),
    )(whitened, padded)
    return out.reshape(k_count, rows, chans)[:, : 2 * LAG + 1, :]


def chan_filter(piece, tap_table):
    channels_here = piece.shape[0]
    half = (tap_table.shape[0] - 1) // 2
    widened = padded_2(piece, (("chan", 0),), half)
    total = jnp.dot(
        band_matrix(tap_table, channels_here, channels_here + 2 * half),
        widened,
        preferred_element_type=jnp.float32,
    )
    return total.astype(jnp.bfloat16)


def prep_body(section_chunk, rec_ref, lo_ref, hi_ref, blo_ref, bmid_ref, bhi_ref, tw_ref, o_ref, cp_ref, tp_ref):
    chans, samples = o_ref.shape
    lanes = 128
    cp_ref[:, pl.ds(0, lanes)] = jnp.zeros((chans, lanes), cp_ref.dtype)
    cp_ref[:, pl.ds(samples + lanes, lanes)] = jnp.zeros((chans, lanes), cp_ref.dtype)
    chunk = section_chunk

    def chan_step(i, carry):
        off = pl.multiple_of(i * chunk, chunk)
        total = jnp.dot(bmid_ref[...], rec_ref[0, :, pl.ds(off, chunk)], preferred_element_type=jnp.float32)
        total += jnp.dot(blo_ref[...], lo_ref[:, pl.ds(off, chunk)], preferred_element_type=jnp.float32)
        total += jnp.dot(bhi_ref[...], hi_ref[:, pl.ds(off, chunk)], preferred_element_type=jnp.float32)
        cp_ref[:, pl.ds(pl.multiple_of(off + lanes, lanes), chunk)] = total.astype(cp_ref.dtype)
        return carry

    lax.fori_loop(0, samples // chunk, chan_step, 0)

    def time_step(b, acc):
        off = pl.multiple_of(b * lanes, lanes)
        y = jnp.dot(cp_ref[:, pl.ds(off, 3 * lanes)], tw_ref[...], preferred_element_type=jnp.float32)
        tp_ref[:, pl.ds(off, lanes)] = y
        return acc + y * y

    acc = lax.fori_loop(0, samples // lanes, time_step, jnp.zeros((chans, lanes), jnp.float32))
    power = jnp.sum(acc, axis=1, keepdims=True) / samples
    scale = lax.rsqrt(power + 1e-06)

    def white_step(i, carry):
        off = pl.multiple_of(i * chunk, chunk)
        o_ref[:, pl.ds(off, chunk)] = (tp_ref[:, pl.ds(off, chunk)] * scale).astype(o_ref.dtype)
        return carry

    lax.fori_loop(0, samples // chunk, white_step, 0)


def prepare_kernel(record, section, lo, hi, band, time_weights):
    count_steps, chans, samples = record.shape
    half = lo.shape[0]
    lanes = 128
    chunk = 512
    blo, bmid, bhi = band[:, :half], band[:, half:half + chans], band[:, half + chans:]
    full = lambda i: (0, 0)
    return pl.pallas_call(
        functools.partial(prep_body, chunk),
        grid=(1,),
        in_specs=[
            pl.BlockSpec((1, chans, samples), lambda i: (section, 0, 0)),
            pl.BlockSpec((half, samples), full),
            pl.BlockSpec((half, samples), full),
            pl.BlockSpec((chans, half), full),
            pl.BlockSpec((chans, chans), full),
            pl.BlockSpec((chans, half), full),
            pl.BlockSpec(time_weights.shape, full),
        ],
        out_specs=pl.BlockSpec((chans, samples), full),
        out_shape=jax.ShapeDtypeStruct((chans, samples), jnp.bfloat16),
        scratch_shapes=[
            pltpu.VMEM((chans, samples + 2 * lanes), jnp.bfloat16),
            pltpu.VMEM((chans, samples), jnp.float32),
        ],
        compiler_params=pltpu.CompilerParams(vmem_limit_bytes=48 * 1024 * 1024),
        cost_estimate=pl.CostEstimate(
            flops=2 * chans * samples * (chans + 2 * half + 3 * lanes),
            bytes_accessed=2 * samples * (2 * chans + 2 * half),
            transcendentals=chans,
        ),
    )(record, lo, hi, blo, bmid, bhi, time_weights)


def xor_sum(x, axis):
    count = lax.axis_size(axis)
    if count & (count - 1):
        return lax.psum(x, axis)
    step = 1
    while step < count:
        x = x + lax.ppermute(x, axis, [(i, i ^ step) for i in range(count)])
        step *= 2
    return x


def body(record, chan_taps, time_taps, sources):
    count_steps = record.shape[0]
    channels_here = record.shape[1]
    samples = record.shape[2]
    chan_table = chan_taps.astype(jnp.bfloat16)
    time_table = time_taps.astype(jnp.bfloat16)
    first_chan = lax.axis_index("chan") * channels_here
    selector = (
        (sources - first_chan)[:, :, None] == lax.iota(jnp.int32, channels_here)[None, None, :]
    ).astype(jnp.bfloat16)
    normalizer = 1.0 / math.sqrt(samples * lax.axis_size("win"))

    half = (chan_table.shape[0] - 1) // 2
    count = lax.axis_size("chan")
    band = band_matrix(chan_table, channels_here, channels_here + 2 * half)
    offset = lax.iota(jnp.int32, 384)[:, None] - 128 - lax.iota(jnp.int32, 128)[None, :]
    time_weights = tap_lookup(offset + (time_table.shape[0] - 1) // 2, time_table)

    def prepare(whole, section):
        head = whole[section, :half]
        tail = whole[section, channels_here - half :]
        lower = lax.ppermute(tail, "chan", [(i, i + 1) for i in range(count - 1)])
        upper = lax.ppermute(head, "chan", [(i + 1, i) for i in range(count - 1)])
        whitened = prepare_kernel(whole, section, lower, upper, band, time_weights)
        term = jnp.dot(selector[section], whitened, preferred_element_type=jnp.float32)
        return whitened, xor_sum(term.astype(jnp.bfloat16), "chan")

    pieces = [record] * count_steps
    results = []
    pending = prepare(pieces[0], 0)
    for section in range(count_steps):
        upcoming = None
        if section + 1 < count_steps:
            upcoming = prepare(pieces[section + 1], section + 1)
        whitened, panel = pending
        if section >= 2:
            whitened, panel, results[section - 2] = lax.optimization_barrier(
                (whitened, panel, results[section - 2])
            )
        if section + 1 < count_steps:
            partial_corr = correlate_kernel(whitened, panel)
            if section + 2 < count_steps:
                pieces[section + 2], partial_corr = lax.optimization_barrier(
                    (pieces[section + 2], partial_corr)
                )
            results.append(xor_sum(partial_corr, "win"))
        else:
            half = panel.shape[0] // 2
            parts = [
                xor_sum(correlate_kernel(whitened, panel[:half]), "win"),
                xor_sum(correlate_kernel(whitened, panel[half:]), "win"),
            ]
            results.append(jnp.concatenate(parts, axis=0))
        pending = upcoming
    return jnp.stack(results) * normalizer


def solution(mesh):
    in_specs = (P(None, "chan", "win"), P(), P(), P())
    out_specs = P(None, None, None, "chan")
    return jax.shard_map(body, mesh=mesh, in_specs=in_specs, out_specs=out_specs, check_vma=False)
```

```python
import functools
import math

import jax
import jax.numpy as jnp
from jax import lax
from jax.experimental import pallas as pl
from jax.experimental.pallas import tpu as pltpu
from jax.sharding import PartitionSpec as P

LAG = 64


def padded_2(cells, sides, width):
    for axis, dim in sides:
        count = lax.axis_size(axis)
        ends = count - 1
        head = lax.slice_in_dim(cells, 0, width, axis=dim)
        tail = lax.slice_in_dim(cells, cells.shape[dim] - width, cells.shape[dim], axis=dim)
        cells = jnp.concatenate(
            [
                lax.ppermute(tail, axis, [(i, (i + 1) % count) for i in range(ends)]),
                cells,
                lax.ppermute(head, axis, [((i + 1) % count, i) for i in range(ends)]),
            ],
            axis=dim,
        )
    return cells


def tap_lookup(offset, tap_table):
    count_taps = tap_table.shape[0]
    marks = offset[..., None] == lax.iota(jnp.int32, count_taps)
    picked = jnp.where(marks, tap_table.astype(jnp.float32), jnp.zeros((), jnp.float32))
    return jnp.sum(picked, axis=-1).astype(tap_table.dtype)


def band_matrix(tap_table, height, breadth):
    offset = lax.iota(jnp.int32, breadth)[None, :] - lax.iota(jnp.int32, height)[:, None]
    return tap_lookup(offset, tap_table)


def time_filter(chan_pass, tap_table):
    channels_here, samples = chan_pass.shape
    half = (tap_table.shape[0] - 1) // 2
    blocks = chan_pass.reshape(channels_here, samples // 128, 128)
    zeros_block = jnp.zeros_like(blocks[:, :1])
    earlier = jnp.concatenate([zeros_block, blocks[:, :-1]], axis=1)
    later = jnp.concatenate([blocks[:, 1:], zeros_block], axis=1)
    extended = jnp.concatenate([earlier, blocks, later], axis=2)
    offset = lax.iota(jnp.int32, 384)[:, None] - 128 - lax.iota(jnp.int32, 128)[None, :] + half
    weights = tap_lookup(offset, tap_table)
    result = jnp.einsum("cbr,rt->cbt", extended, weights, preferred_element_type=jnp.float32)
    return result.reshape(channels_here, samples)


def whiten(time_pass):
    power = jnp.mean(time_pass * time_pass, axis=-1, keepdims=True)
    return (time_pass * lax.rsqrt(power + 1e-06)).astype(jnp.bfloat16)


def corr_body(nb, rows, w_ref, p_ref, o_ref, s_ref):
    n = pl.program_id(0)
    k_count = p_ref.shape[0]
    lanes = 128

    @pl.when(n == 0)
    def _():
        o_ref[...] = jnp.zeros_like(o_ref)

    j_idx = lax.broadcasted_iota(jnp.int32, (rows, lanes), 0)
    r_idx = lax.broadcasted_iota(jnp.int32, (rows, lanes), 1)
    upper = r_idx >= j_idx
    for k in range(k_count):
        rolled = []
        for b in range(nb + 1):
            start = pl.multiple_of((n * nb + b) * lanes, lanes)
            chunk = p_ref[pl.ds(k, 1), pl.ds(start, lanes)]
            wide = jnp.broadcast_to(chunk, (rows, lanes))
            rolled.append(pltpu.roll(wide, 0, 1, stride=1, stride_axis=0))
        for b in range(nb):
            piece = jnp.where(upper, rolled[b + 1], rolled[b])
            s_ref[pl.ds(k * rows, rows), pl.ds(b * lanes, lanes)] = piece.astype(s_ref.dtype)
    o_ref[...] += lax.dot_general(
        s_ref[...], w_ref[...], (((1,), (1,)), ((), ())),
        preferred_element_type=jnp.float32)


def correlate_kernel(whitened, panel, nb=8):
    chans, samples = whitened.shape
    k_count = panel.shape[0]
    lanes = 128
    rows = 136
    padded = jnp.pad(panel.astype(jnp.float32), ((0, 0), (LAG, LAG)))
    grid = samples // (nb * lanes)
    out = pl.pallas_call(
        functools.partial(corr_body, nb, rows),
        grid=(grid,),
        in_specs=[
            pl.BlockSpec((chans, nb * lanes), lambda n: (0, n)),
            pl.BlockSpec((k_count, samples + 2 * LAG), lambda n: (0, 0)),
        ],
        out_specs=pl.BlockSpec((k_count * rows, chans), lambda n: (0, 0)),
        out_shape=jax.ShapeDtypeStruct((k_count * rows, chans), jnp.float32),
        scratch_shapes=[pltpu.VMEM((k_count * rows, nb * lanes), jnp.bfloat16)],
        compiler_params=pltpu.CompilerParams(dimension_semantics=("arbitrary",)),
        cost_estimate=pl.CostEstimate(
            flops=2 * k_count * rows * samples * chans,
            bytes_accessed=2 * chans * samples + 4 * k_count * (samples + rows * chans),
            transcendentals=0,
        ),
    )(whitened, padded)
    return out.reshape(k_count, rows, chans)[:, : 2 * LAG + 1, :]


def chan_filter(piece, tap_table):
    channels_here = piece.shape[0]
    half = (tap_table.shape[0] - 1) // 2
    widened = padded_2(piece, (("chan", 0),), half)
    total = jnp.dot(
        band_matrix(tap_table, channels_here, channels_here + 2 * half),
        widened,
        preferred_element_type=jnp.float32,
    )
    return total.astype(jnp.bfloat16)


def prep_body(section_chunk, rec_ref, lo_ref, hi_ref, blo_ref, bmid_ref, bhi_ref, tw_ref, o_ref, cp_ref, tp_ref):
    chans, samples = o_ref.shape
    lanes = 128
    cp_ref[:, pl.ds(0, lanes)] = jnp.zeros((chans, lanes), cp_ref.dtype)
    cp_ref[:, pl.ds(samples + lanes, lanes)] = jnp.zeros((chans, lanes), cp_ref.dtype)
    chunk = section_chunk

    def chan_step(i, carry):
        off = pl.multiple_of(i * chunk, chunk)
        total = jnp.dot(bmid_ref[...], rec_ref[0, :, pl.ds(off, chunk)], preferred_element_type=jnp.float32)
        total += jnp.dot(blo_ref[...], lo_ref[:, pl.ds(off, chunk)], preferred_element_type=jnp.float32)
        total += jnp.dot(bhi_ref[...], hi_ref[:, pl.ds(off, chunk)], preferred_element_type=jnp.float32)
        cp_ref[:, pl.ds(pl.multiple_of(off + lanes, lanes), chunk)] = total.astype(cp_ref.dtype)
        return carry

    lax.fori_loop(0, samples // chunk, chan_step, 0)

    group = 8

    def time_step(g, acc):
        base = g * group
        windows = [
            cp_ref[:, pl.ds(pl.multiple_of((base + q) * lanes, lanes), 3 * lanes)]
            for q in range(group)
        ]
        y = jnp.dot(jnp.concatenate(windows, axis=0), tw_ref[...], preferred_element_type=jnp.float32)
        for q in range(group):
            part = y[q * chans : (q + 1) * chans]
            tp_ref[:, pl.ds(pl.multiple_of((base + q) * lanes, lanes), lanes)] = part
            acc = acc + part * part
        return acc

    acc = lax.fori_loop(0, samples // (lanes * group), time_step, jnp.zeros((chans, lanes), jnp.float32))
    power = jnp.sum(acc, axis=1, keepdims=True) / samples
    scale = lax.rsqrt(power + 1e-06)

    def white_step(i, carry):
        off = pl.multiple_of(i * chunk, chunk)
        o_ref[:, pl.ds(off, chunk)] = (tp_ref[:, pl.ds(off, chunk)] * scale).astype(o_ref.dtype)
        return carry

    lax.fori_loop(0, samples // chunk, white_step, 0)


def prepare_kernel(record, section, lo, hi, band, time_weights):
    count_steps, chans, samples = record.shape
    half = lo.shape[0]
    lanes = 128
    chunk = 512
    blo, bmid, bhi = band[:, :half], band[:, half:half + chans], band[:, half + chans:]
    full = lambda i: (0, 0)
    return pl.pallas_call(
        functools.partial(prep_body, chunk),
        grid=(1,),
        in_specs=[
            pl.BlockSpec((1, chans, samples), lambda i: (section, 0, 0)),
            pl.BlockSpec((half, samples), full),
            pl.BlockSpec((half, samples), full),
            pl.BlockSpec((chans, half), full),
            pl.BlockSpec((chans, chans), full),
            pl.BlockSpec((chans, half), full),
            pl.BlockSpec(time_weights.shape, full),
        ],
        out_specs=pl.BlockSpec((chans, samples), full),
        out_shape=jax.ShapeDtypeStruct((chans, samples), jnp.bfloat16),
        scratch_shapes=[
            pltpu.VMEM((chans, samples + 2 * lanes), jnp.bfloat16),
            pltpu.VMEM((chans, samples), jnp.float32),
        ],
        compiler_params=pltpu.CompilerParams(vmem_limit_bytes=48 * 1024 * 1024),
        cost_estimate=pl.CostEstimate(
            flops=2 * chans * samples * (chans + 2 * half + 3 * lanes),
            bytes_accessed=2 * samples * (2 * chans + 2 * half),
            transcendentals=chans,
        ),
    )(record, lo, hi, blo, bmid, bhi, time_weights)


def xor_sum(x, axis):
    count = lax.axis_size(axis)
    if count & (count - 1):
        return lax.psum(x, axis)
    step = 1
    while step < count:
        x = x + lax.ppermute(x, axis, [(i, i ^ step) for i in range(count)])
        step *= 2
    return x


def spread_sum(x, axis):
    count = lax.axis_size(axis)
    me = lax.axis_index(axis)
    got = [x] + [
        lax.ppermute(x, axis, [(i, (i + shift) % count) for i in range(count)])
        for shift in range(1, count)
    ]
    stacked = jnp.stack(got)
    terms = [lax.dynamic_index_in_dim(stacked, (me - src) % count, keepdims=False) for src in range(count)]
    while len(terms) > 1:
        terms = [terms[i] + terms[i + 1] for i in range(0, len(terms) - 1, 2)] + (
            [terms[-1]] if len(terms) % 2 else []
        )
    return terms[0]


def one_hot_sum(x, axis):
    count = lax.axis_size(axis)
    total = x
    for shift in range(1, count):
        total = total + lax.ppermute(x, axis, [(i, (i + shift) % count) for i in range(count)])
    return total


def body(record, chan_taps, time_taps, sources):
    count_steps = record.shape[0]
    channels_here = record.shape[1]
    samples = record.shape[2]
    chan_table = chan_taps.astype(jnp.bfloat16)
    time_table = time_taps.astype(jnp.bfloat16)
    first_chan = lax.axis_index("chan") * channels_here
    selector = (
        (sources - first_chan)[:, :, None] == lax.iota(jnp.int32, channels_here)[None, None, :]
    ).astype(jnp.bfloat16)
    normalizer = 1.0 / math.sqrt(samples * lax.axis_size("win"))

    half = (chan_table.shape[0] - 1) // 2
    count = lax.axis_size("chan")
    band = band_matrix(chan_table, channels_here, channels_here + 2 * half)
    offset = lax.iota(jnp.int32, 384)[:, None] - 128 - lax.iota(jnp.int32, 128)[None, :]
    time_weights = tap_lookup(offset + (time_table.shape[0] - 1) // 2, time_table)

    def prepare(whole, section):
        head = whole[section, :half]
        tail = whole[section, channels_here - half :]
        lower = lax.ppermute(tail, "chan", [(i, i + 1) for i in range(count - 1)])
        upper = lax.ppermute(head, "chan", [(i + 1, i) for i in range(count - 1)])
        whitened = prepare_kernel(whole, section, lower, upper, band, time_weights)
        term = jnp.dot(selector[section], whitened, preferred_element_type=jnp.float32)
        return whitened, one_hot_sum(term.astype(jnp.bfloat16), "chan")

    pieces = [record] * count_steps
    results = []
    pending = prepare(pieces[0], 0)
    for section in range(count_steps):
        upcoming = None
        if section + 1 < count_steps:
            upcoming = prepare(pieces[section + 1], section + 1)
        whitened, panel = pending
        if section >= 2:
            whitened, panel, results[section - 2] = lax.optimization_barrier(
                (whitened, panel, results[section - 2])
            )
        if section + 1 < count_steps:
            partial_corr = correlate_kernel(whitened, panel)
            if section + 2 < count_steps:
                pieces[section + 2], partial_corr = lax.optimization_barrier(
                    (pieces[section + 2], partial_corr)
                )
            results.append(spread_sum(partial_corr, "win"))
        else:
            half = panel.shape[0] // 2
            parts = [
                spread_sum(correlate_kernel(whitened, panel[:half]), "win"),
                spread_sum(correlate_kernel(whitened, panel[half:]), "win"),
            ]
            results.append(jnp.concatenate(parts, axis=0))
        pending = upcoming
    return jnp.stack(results) * normalizer


def solution(mesh):
    in_specs = (P(None, "chan", "win"), P(), P(), P())
    out_specs = P(None, None, None, "chan")
    return jax.shard_map(body, mesh=mesh, in_specs=in_specs, out_specs=out_specs, check_vma=False)
```

```python
import functools
import math

import jax
import jax.numpy as jnp
from jax import lax
from jax.experimental import pallas as pl
from jax.experimental.pallas import tpu as pltpu
from jax.sharding import PartitionSpec as P

LAG = 64


def padded_2(cells, sides, width):
    for axis, dim in sides:
        count = lax.axis_size(axis)
        ends = count - 1
        head = lax.slice_in_dim(cells, 0, width, axis=dim)
        tail = lax.slice_in_dim(cells, cells.shape[dim] - width, cells.shape[dim], axis=dim)
        cells = jnp.concatenate(
            [
                lax.ppermute(tail, axis, [(i, (i + 1) % count) for i in range(ends)]),
                cells,
                lax.ppermute(head, axis, [((i + 1) % count, i) for i in range(ends)]),
            ],
            axis=dim,
        )
    return cells


def tap_lookup(offset, tap_table):
    count_taps = tap_table.shape[0]
    marks = offset[..., None] == lax.iota(jnp.int32, count_taps)
    picked = jnp.where(marks, tap_table.astype(jnp.float32), jnp.zeros((), jnp.float32))
    return jnp.sum(picked, axis=-1).astype(tap_table.dtype)


def band_matrix(tap_table, height, breadth):
    offset = lax.iota(jnp.int32, breadth)[None, :] - lax.iota(jnp.int32, height)[:, None]
    return tap_lookup(offset, tap_table)


def time_filter(chan_pass, tap_table):
    channels_here, samples = chan_pass.shape
    half = (tap_table.shape[0] - 1) // 2
    blocks = chan_pass.reshape(channels_here, samples // 128, 128)
    zeros_block = jnp.zeros_like(blocks[:, :1])
    earlier = jnp.concatenate([zeros_block, blocks[:, :-1]], axis=1)
    later = jnp.concatenate([blocks[:, 1:], zeros_block], axis=1)
    extended = jnp.concatenate([earlier, blocks, later], axis=2)
    offset = lax.iota(jnp.int32, 384)[:, None] - 128 - lax.iota(jnp.int32, 128)[None, :] + half
    weights = tap_lookup(offset, tap_table)
    result = jnp.einsum("cbr,rt->cbt", extended, weights, preferred_element_type=jnp.float32)
    return result.reshape(channels_here, samples)


def whiten(time_pass):
    power = jnp.mean(time_pass * time_pass, axis=-1, keepdims=True)
    return (time_pass * lax.rsqrt(power + 1e-06)).astype(jnp.bfloat16)


def corr_body(nb, rows, w_ref, p_ref, o_ref, s_ref):
    n = pl.program_id(0)
    k_count = p_ref.shape[0]
    lanes = 128

    @pl.when(n == 0)
    def _():
        o_ref[...] = jnp.zeros_like(o_ref)

    j_idx = lax.broadcasted_iota(jnp.int32, (rows, lanes), 0)
    r_idx = lax.broadcasted_iota(jnp.int32, (rows, lanes), 1)
    upper = r_idx >= j_idx
    for k in range(k_count):
        rolled = []
        for b in range(nb + 1):
            start = pl.multiple_of((n * nb + b) * lanes, lanes)
            chunk = p_ref[pl.ds(k, 1), pl.ds(start, lanes)]
            wide = jnp.broadcast_to(chunk, (rows, lanes))
            rolled.append(pltpu.roll(wide, 0, 1, stride=1, stride_axis=0))
        for b in range(nb):
            piece = jnp.where(upper, rolled[b + 1], rolled[b])
            s_ref[pl.ds(k * rows, rows), pl.ds(b * lanes, lanes)] = piece.astype(s_ref.dtype)
    o_ref[...] += lax.dot_general(
        s_ref[...], w_ref[...], (((1,), (1,)), ((), ())),
        preferred_element_type=jnp.float32)


def correlate_kernel(whitened, panel, nb=8):
    chans, samples = whitened.shape
    k_count = panel.shape[0]
    lanes = 128
    rows = 136
    padded = jnp.pad(panel.astype(jnp.float32), ((0, 0), (LAG, LAG)))
    grid = samples // (nb * lanes)
    out = pl.pallas_call(
        functools.partial(corr_body, nb, rows),
        grid=(grid,),
        in_specs=[
            pl.BlockSpec((chans, nb * lanes), lambda n: (0, n)),
            pl.BlockSpec((k_count, samples + 2 * LAG), lambda n: (0, 0)),
        ],
        out_specs=pl.BlockSpec((k_count * rows, chans), lambda n: (0, 0)),
        out_shape=jax.ShapeDtypeStruct((k_count * rows, chans), jnp.float32),
        scratch_shapes=[pltpu.VMEM((k_count * rows, nb * lanes), jnp.bfloat16)],
        compiler_params=pltpu.CompilerParams(dimension_semantics=("arbitrary",)),
        cost_estimate=pl.CostEstimate(
            flops=2 * k_count * rows * samples * chans,
            bytes_accessed=2 * chans * samples + 4 * k_count * (samples + rows * chans),
            transcendentals=0,
        ),
    )(whitened, padded)
    return out.reshape(k_count, rows, chans)[:, : 2 * LAG + 1, :]


def chan_filter(piece, tap_table):
    channels_here = piece.shape[0]
    half = (tap_table.shape[0] - 1) // 2
    widened = padded_2(piece, (("chan", 0),), half)
    total = jnp.dot(
        band_matrix(tap_table, channels_here, channels_here + 2 * half),
        widened,
        preferred_element_type=jnp.float32,
    )
    return total.astype(jnp.bfloat16)


def prep_body(section_chunk, rec_ref, lo_ref, hi_ref, blo_ref, bmid_ref, bhi_ref, tw_ref, o_ref, cp_ref, tp_ref):
    chans, samples = o_ref.shape
    lanes = 128
    cp_ref[:, pl.ds(0, lanes)] = jnp.zeros((chans, lanes), cp_ref.dtype)
    cp_ref[:, pl.ds(samples + lanes, lanes)] = jnp.zeros((chans, lanes), cp_ref.dtype)
    chunk = section_chunk

    def chan_step(i, carry):
        off = pl.multiple_of(i * chunk, chunk)
        total = jnp.dot(bmid_ref[...], rec_ref[0, :, pl.ds(off, chunk)], preferred_element_type=jnp.float32)
        total += jnp.dot(blo_ref[...], lo_ref[:, pl.ds(off, chunk)], preferred_element_type=jnp.float32)
        total += jnp.dot(bhi_ref[...], hi_ref[:, pl.ds(off, chunk)], preferred_element_type=jnp.float32)
        cp_ref[:, pl.ds(pl.multiple_of(off + lanes, lanes), chunk)] = total.astype(cp_ref.dtype)
        return carry

    lax.fori_loop(0, samples // chunk, chan_step, 0)

    group = 8

    def time_step(g, acc):
        base = g * group
        windows = [
            cp_ref[:, pl.ds(pl.multiple_of((base + q) * lanes, lanes), 3 * lanes)]
            for q in range(group)
        ]
        y = jnp.dot(jnp.concatenate(windows, axis=0), tw_ref[...], preferred_element_type=jnp.float32)
        for q in range(group):
            part = y[q * chans : (q + 1) * chans]
            tp_ref[:, pl.ds(pl.multiple_of((base + q) * lanes, lanes), lanes)] = part
            acc = acc + part * part
        return acc

    acc = lax.fori_loop(0, samples // (lanes * group), time_step, jnp.zeros((chans, lanes), jnp.float32))
    power = jnp.sum(acc, axis=1, keepdims=True) / samples
    scale = lax.rsqrt(power + 1e-06)

    def white_step(i, carry):
        off = pl.multiple_of(i * chunk, chunk)
        o_ref[:, pl.ds(off, chunk)] = (tp_ref[:, pl.ds(off, chunk)] * scale).astype(o_ref.dtype)
        return carry

    lax.fori_loop(0, samples // chunk, white_step, 0)


def prepare_kernel(record, section, lo, hi, band, time_weights):
    count_steps, chans, samples = record.shape
    half = lo.shape[0]
    lanes = 128
    chunk = 512
    blo, bmid, bhi = band[:, :half], band[:, half:half + chans], band[:, half + chans:]
    full = lambda i: (0, 0)
    return pl.pallas_call(
        functools.partial(prep_body, chunk),
        grid=(1,),
        in_specs=[
            pl.BlockSpec((1, chans, samples), lambda i: (section, 0, 0)),
            pl.BlockSpec((half, samples), full),
            pl.BlockSpec((half, samples), full),
            pl.BlockSpec((chans, half), full),
            pl.BlockSpec((chans, chans), full),
            pl.BlockSpec((chans, half), full),
            pl.BlockSpec(time_weights.shape, full),
        ],
        out_specs=pl.BlockSpec((chans, samples), full),
        out_shape=jax.ShapeDtypeStruct((chans, samples), jnp.bfloat16),
        scratch_shapes=[
            pltpu.VMEM((chans, samples + 2 * lanes), jnp.bfloat16),
            pltpu.VMEM((chans, samples), jnp.float32),
        ],
        compiler_params=pltpu.CompilerParams(vmem_limit_bytes=48 * 1024 * 1024),
        cost_estimate=pl.CostEstimate(
            flops=2 * chans * samples * (chans + 2 * half + 3 * lanes),
            bytes_accessed=2 * samples * (2 * chans + 2 * half),
            transcendentals=chans,
        ),
    )(record, lo, hi, blo, bmid, bhi, time_weights)


def xor_sum(x, axis):
    count = lax.axis_size(axis)
    if count & (count - 1):
        return lax.psum(x, axis)
    step = 1
    while step < count:
        x = x + lax.ppermute(x, axis, [(i, i ^ step) for i in range(count)])
        step *= 2
    return x


def spread_sum(x, axis):
    count = lax.axis_size(axis)
    me = lax.axis_index(axis)
    got = [x] + [
        lax.ppermute(x, axis, [(i, (i + shift) % count) for i in range(count)])
        for shift in range(1, count)
    ]
    stacked = jnp.stack(got)
    terms = [lax.dynamic_index_in_dim(stacked, (me - src) % count, keepdims=False) for src in range(count)]
    while len(terms) > 1:
        terms = [terms[i] + terms[i + 1] for i in range(0, len(terms) - 1, 2)] + (
            [terms[-1]] if len(terms) % 2 else []
        )
    return terms[0]


def one_hot_sum(x, axis):
    count = lax.axis_size(axis)
    total = x
    for shift in range(1, count):
        total = total + lax.ppermute(x, axis, [(i, (i + shift) % count) for i in range(count)])
    return total


def body(record, chan_taps, time_taps, sources):
    count_steps = record.shape[0]
    channels_here = record.shape[1]
    samples = record.shape[2]
    chan_table = chan_taps.astype(jnp.bfloat16)
    time_table = time_taps.astype(jnp.bfloat16)
    first_chan = lax.axis_index("chan") * channels_here
    selector = (
        (sources - first_chan)[:, :, None] == lax.iota(jnp.int32, channels_here)[None, None, :]
    ).astype(jnp.bfloat16)
    normalizer = 1.0 / math.sqrt(samples * lax.axis_size("win"))

    half = (chan_table.shape[0] - 1) // 2
    count = lax.axis_size("chan")
    band = band_matrix(chan_table, channels_here, channels_here + 2 * half)
    offset = lax.iota(jnp.int32, 384)[:, None] - 128 - lax.iota(jnp.int32, 128)[None, :]
    time_weights = tap_lookup(offset + (time_table.shape[0] - 1) // 2, time_table)

    heads = record[:, :half]
    tails = record[:, channels_here - half :]
    lowers = lax.ppermute(tails, "chan", [(i, i + 1) for i in range(count - 1)])
    uppers = lax.ppermute(heads, "chan", [(i + 1, i) for i in range(count - 1)])

    whitened = []
    terms = []
    source = record
    for section in range(count_steps):
        if section == count_steps - 1:
            source, early_terms = lax.optimization_barrier((record, jnp.stack(terms)))
        piece = prepare_kernel(source, section, lowers[section], uppers[section], band, time_weights)
        whitened.append(piece)
        term = jnp.dot(selector[section], piece, preferred_element_type=jnp.float32)
        terms.append(term.astype(jnp.bfloat16))
    early = one_hot_sum(early_terms, "chan")
    early_white = whitened[:-1]
    early_white, early, last_term = lax.optimization_barrier((early_white, early, terms[-1]))
    last_panel = one_hot_sum(last_term, "chan")
    corrs = [correlate_kernel(early_white[section], early[section]) for section in range(count_steps - 1)]
    early_corr = jnp.stack(corrs)
    last_white, last_panel, early_corr = lax.optimization_barrier((whitened[-1], last_panel, early_corr))
    early_sum = spread_sum(early_corr, "win")
    results = [early_sum[section] for section in range(count_steps - 1)]
    results.append(spread_sum(correlate_kernel(last_white, last_panel), "win"))
    return jnp.stack(results) * normalizer


def solution(mesh):
    in_specs = (P(None, "chan", "win"), P(), P(), P())
    out_specs = P(None, None, None, "chan")
    return jax.shard_map(body, mesh=mesh, in_specs=in_specs, out_specs=out_specs, check_vma=False)
```

```python
import functools
import math

import jax
import jax.numpy as jnp
from jax import lax
from jax.experimental import pallas as pl
from jax.experimental.pallas import tpu as pltpu
from jax.sharding import PartitionSpec as P

LAG = 64
CORR_ROWS = 136


def padded_2(cells, sides, width):
    for axis, dim in sides:
        count = lax.axis_size(axis)
        ends = count - 1
        head = lax.slice_in_dim(cells, 0, width, axis=dim)
        tail = lax.slice_in_dim(cells, cells.shape[dim] - width, cells.shape[dim], axis=dim)
        cells = jnp.concatenate(
            [
                lax.ppermute(tail, axis, [(i, (i + 1) % count) for i in range(ends)]),
                cells,
                lax.ppermute(head, axis, [((i + 1) % count, i) for i in range(ends)]),
            ],
            axis=dim,
        )
    return cells


def tap_lookup(offset, tap_table):
    count_taps = tap_table.shape[0]
    marks = offset[..., None] == lax.iota(jnp.int32, count_taps)
    picked = jnp.where(marks, tap_table.astype(jnp.float32), jnp.zeros((), jnp.float32))
    return jnp.sum(picked, axis=-1).astype(tap_table.dtype)


def band_matrix(tap_table, height, breadth):
    offset = lax.iota(jnp.int32, breadth)[None, :] - lax.iota(jnp.int32, height)[:, None]
    return tap_lookup(offset, tap_table)


def time_filter(chan_pass, tap_table):
    channels_here, samples = chan_pass.shape
    half = (tap_table.shape[0] - 1) // 2
    blocks = chan_pass.reshape(channels_here, samples // 128, 128)
    zeros_block = jnp.zeros_like(blocks[:, :1])
    earlier = jnp.concatenate([zeros_block, blocks[:, :-1]], axis=1)
    later = jnp.concatenate([blocks[:, 1:], zeros_block], axis=1)
    extended = jnp.concatenate([earlier, blocks, later], axis=2)
    offset = lax.iota(jnp.int32, 384)[:, None] - 128 - lax.iota(jnp.int32, 128)[None, :] + half
    weights = tap_lookup(offset, tap_table)
    result = jnp.einsum("cbr,rt->cbt", extended, weights, preferred_element_type=jnp.float32)
    return result.reshape(channels_here, samples)


def whiten(time_pass):
    power = jnp.mean(time_pass * time_pass, axis=-1, keepdims=True)
    return (time_pass * lax.rsqrt(power + 1e-06)).astype(jnp.bfloat16)


def corr_body(nb, rows, w_ref, p_ref, o_ref, s_ref):
    n = pl.program_id(0)
    k_count = p_ref.shape[0]
    lanes = 128

    @pl.when(n == 0)
    def _():
        o_ref[...] = jnp.zeros_like(o_ref)

    j_idx = lax.broadcasted_iota(jnp.int32, (rows, lanes), 0)
    r_idx = lax.broadcasted_iota(jnp.int32, (rows, lanes), 1)
    upper = r_idx >= j_idx
    for k in range(k_count):
        rolled = []
        for b in range(nb + 1):
            start = pl.multiple_of((n * nb + b) * lanes, lanes)
            chunk = p_ref[pl.ds(k, 1), pl.ds(start, lanes)]
            wide = jnp.broadcast_to(chunk, (rows, lanes))
            rolled.append(pltpu.roll(wide, 0, 1, stride=1, stride_axis=0))
        for b in range(nb):
            piece = jnp.where(upper, rolled[b + 1], rolled[b])
            s_ref[pl.ds(k * rows, rows), pl.ds(b * lanes, lanes)] = piece.astype(s_ref.dtype)
    o_ref[...] += lax.dot_general(
        s_ref[...], w_ref[...], (((1,), (1,)), ((), ())),
        preferred_element_type=jnp.float32)


def correlate_kernel(whitened, panel, nb=8):
    chans, samples = whitened.shape
    k_count = panel.shape[0]
    lanes = 128
    rows = CORR_ROWS
    padded = jnp.pad(panel.astype(jnp.float32), ((0, 0), (LAG, LAG)))
    grid = samples // (nb * lanes)
    out = pl.pallas_call(
        functools.partial(corr_body, nb, rows),
        grid=(grid,),
        in_specs=[
            pl.BlockSpec((chans, nb * lanes), lambda n: (0, n)),
            pl.BlockSpec((k_count, samples + 2 * LAG), lambda n: (0, 0)),
        ],
        out_specs=pl.BlockSpec((k_count * rows, chans), lambda n: (0, 0)),
        out_shape=jax.ShapeDtypeStruct((k_count * rows, chans), jnp.float32),
        scratch_shapes=[pltpu.VMEM((k_count * rows, nb * lanes), jnp.bfloat16)],
        compiler_params=pltpu.CompilerParams(dimension_semantics=("arbitrary",)),
        cost_estimate=pl.CostEstimate(
            flops=2 * k_count * rows * samples * chans,
            bytes_accessed=2 * chans * samples + 4 * k_count * (samples + rows * chans),
            transcendentals=0,
        ),
    )(whitened, padded)
    return out


def chan_filter(piece, tap_table):
    channels_here = piece.shape[0]
    half = (tap_table.shape[0] - 1) // 2
    widened = padded_2(piece, (("chan", 0),), half)
    total = jnp.dot(
        band_matrix(tap_table, channels_here, channels_here + 2 * half),
        widened,
        preferred_element_type=jnp.float32,
    )
    return total.astype(jnp.bfloat16)


def prep_body(section_chunk, rec_ref, lo_ref, hi_ref, blo_ref, bmid_ref, bhi_ref, tw_ref, o_ref, cp_ref, tp_ref):
    chans, samples = o_ref.shape
    lanes = 128
    cp_ref[:, pl.ds(0, lanes)] = jnp.zeros((chans, lanes), cp_ref.dtype)
    cp_ref[:, pl.ds(samples + lanes, lanes)] = jnp.zeros((chans, lanes), cp_ref.dtype)
    chunk = section_chunk

    def chan_step(i, carry):
        off = pl.multiple_of(i * chunk, chunk)
        total = jnp.dot(bmid_ref[...], rec_ref[0, :, pl.ds(off, chunk)], preferred_element_type=jnp.float32)
        total += jnp.dot(blo_ref[...], lo_ref[:, pl.ds(off, chunk)], preferred_element_type=jnp.float32)
        total += jnp.dot(bhi_ref[...], hi_ref[:, pl.ds(off, chunk)], preferred_element_type=jnp.float32)
        cp_ref[:, pl.ds(pl.multiple_of(off + lanes, lanes), chunk)] = total.astype(cp_ref.dtype)
        return carry

    lax.fori_loop(0, samples // chunk, chan_step, 0)

    group = 8

    def time_step(g, acc):
        base = g * group
        windows = [
            cp_ref[:, pl.ds(pl.multiple_of((base + q) * lanes, lanes), 3 * lanes)]
            for q in range(group)
        ]
        y = jnp.dot(jnp.concatenate(windows, axis=0), tw_ref[...], preferred_element_type=jnp.float32)
        for q in range(group):
            part = y[q * chans : (q + 1) * chans]
            tp_ref[:, pl.ds(pl.multiple_of((base + q) * lanes, lanes), lanes)] = part
            acc = acc + part * part
        return acc

    acc = lax.fori_loop(0, samples // (lanes * group), time_step, jnp.zeros((chans, lanes), jnp.float32))
    power = jnp.sum(acc, axis=1, keepdims=True) / samples
    scale = lax.rsqrt(power + 1e-06)

    def white_step(i, carry):
        off = pl.multiple_of(i * chunk, chunk)
        o_ref[:, pl.ds(off, chunk)] = (tp_ref[:, pl.ds(off, chunk)] * scale).astype(o_ref.dtype)
        return carry

    lax.fori_loop(0, samples // chunk, white_step, 0)


def prepare_kernel(record, section, lo, hi, band, time_weights):
    count_steps, chans, samples = record.shape
    half = lo.shape[0]
    lanes = 128
    chunk = 512
    blo, bmid, bhi = band[:, :half], band[:, half:half + chans], band[:, half + chans:]
    full = lambda i: (0, 0)
    return pl.pallas_call(
        functools.partial(prep_body, chunk),
        grid=(1,),
        in_specs=[
            pl.BlockSpec((1, chans, samples), lambda i: (section, 0, 0)),
            pl.BlockSpec((half, samples), full),
            pl.BlockSpec((half, samples), full),
            pl.BlockSpec((chans, half), full),
            pl.BlockSpec((chans, chans), full),
            pl.BlockSpec((chans, half), full),
            pl.BlockSpec(time_weights.shape, full),
        ],
        out_specs=pl.BlockSpec((chans, samples), full),
        out_shape=jax.ShapeDtypeStruct((chans, samples), jnp.bfloat16),
        scratch_shapes=[
            pltpu.VMEM((chans, samples + 2 * lanes), jnp.bfloat16),
            pltpu.VMEM((chans, samples), jnp.float32),
        ],
        compiler_params=pltpu.CompilerParams(vmem_limit_bytes=48 * 1024 * 1024),
        cost_estimate=pl.CostEstimate(
            flops=2 * chans * samples * (chans + 2 * half + 3 * lanes),
            bytes_accessed=2 * samples * (2 * chans + 2 * half),
            transcendentals=chans,
        ),
    )(record, lo, hi, blo, bmid, bhi, time_weights)


def xor_sum(x, axis):
    count = lax.axis_size(axis)
    if count & (count - 1):
        return lax.psum(x, axis)
    step = 1
    while step < count:
        x = x + lax.ppermute(x, axis, [(i, i ^ step) for i in range(count)])
        step *= 2
    return x


def body(record, chan_taps, time_taps, sources):
    count_steps = record.shape[0]
    channels_here = record.shape[1]
    samples = record.shape[2]
    chan_table = chan_taps.astype(jnp.bfloat16)
    time_table = time_taps.astype(jnp.bfloat16)
    first_chan = lax.axis_index("chan") * channels_here
    selector = (
        (sources - first_chan)[:, :, None] == lax.iota(jnp.int32, channels_here)[None, None, :]
    ).astype(jnp.bfloat16)
    normalizer = 1.0 / math.sqrt(samples * lax.axis_size("win"))

    half = (chan_table.shape[0] - 1) // 2
    count = lax.axis_size("chan")
    band = band_matrix(chan_table, channels_here, channels_here + 2 * half)
    offset = lax.iota(jnp.int32, 384)[:, None] - 128 - lax.iota(jnp.int32, 128)[None, :]
    time_weights = tap_lookup(offset + (time_table.shape[0] - 1) // 2, time_table)

    def prepare(whole, section):
        head = whole[section, :half]
        tail = whole[section, channels_here - half :]
        lower = lax.ppermute(tail, "chan", [(i, i + 1) for i in range(count - 1)])
        upper = lax.ppermute(head, "chan", [(i + 1, i) for i in range(count - 1)])
        whitened = prepare_kernel(whole, section, lower, upper, band, time_weights)
        term = jnp.dot(selector[section], whitened, preferred_element_type=jnp.float32)
        return whitened, xor_sum(term.astype(jnp.bfloat16), "chan")

    pieces = [record] * count_steps
    results = []
    pending = prepare(pieces[0], 0)
    for section in range(count_steps):
        upcoming = None
        if section + 1 < count_steps:
            upcoming = prepare(pieces[section + 1], section + 1)
        whitened, panel = pending
        if section >= 2:
            whitened, panel, results[section - 2] = lax.optimization_barrier(
                (whitened, panel, results[section - 2])
            )
        if section + 1 < count_steps:
            partial_corr = correlate_kernel(whitened, panel)
            if section + 2 < count_steps:
                pieces[section + 2], partial_corr = lax.optimization_barrier(
                    (pieces[section + 2], partial_corr)
                )
            results.append(xor_sum(partial_corr, "win"))
        else:
            half = panel.shape[0] // 2
            parts = [
                xor_sum(correlate_kernel(whitened, panel[:half]), "win"),
                xor_sum(correlate_kernel(whitened, panel[half:]), "win"),
            ]
            results.append(jnp.concatenate(parts, axis=0))
        pending = upcoming
    lags = 2 * LAG + 1
    shaped = [total.reshape(-1, CORR_ROWS, channels_here)[:, :lags] for total in results]
    return jnp.stack(shaped) * normalizer


def solution(mesh):
    in_specs = (P(None, "chan", "win"), P(), P(), P())
    out_specs = P(None, None, None, "chan")
    return jax.shard_map(body, mesh=mesh, in_specs=in_specs, out_specs=out_specs, check_vma=False)
```

```python
import functools
import math

import jax
import jax.numpy as jnp
from jax import lax
from jax.experimental import pallas as pl
from jax.experimental.pallas import tpu as pltpu
from jax.sharding import PartitionSpec as P

LAG = 64
CORR_ROWS = 136


def padded_2(cells, sides, width):
    for axis, dim in sides:
        count = lax.axis_size(axis)
        ends = count - 1
        head = lax.slice_in_dim(cells, 0, width, axis=dim)
        tail = lax.slice_in_dim(cells, cells.shape[dim] - width, cells.shape[dim], axis=dim)
        cells = jnp.concatenate(
            [
                lax.ppermute(tail, axis, [(i, (i + 1) % count) for i in range(ends)]),
                cells,
                lax.ppermute(head, axis, [((i + 1) % count, i) for i in range(ends)]),
            ],
            axis=dim,
        )
    return cells


def tap_lookup(offset, tap_table):
    count_taps = tap_table.shape[0]
    marks = offset[..., None] == lax.iota(jnp.int32, count_taps)
    picked = jnp.where(marks, tap_table.astype(jnp.float32), jnp.zeros((), jnp.float32))
    return jnp.sum(picked, axis=-1).astype(tap_table.dtype)


def band_matrix(tap_table, height, breadth):
    offset = lax.iota(jnp.int32, breadth)[None, :] - lax.iota(jnp.int32, height)[:, None]
    return tap_lookup(offset, tap_table)


def time_filter(chan_pass, tap_table):
    channels_here, samples = chan_pass.shape
    half = (tap_table.shape[0] - 1) // 2
    blocks = chan_pass.reshape(channels_here, samples // 128, 128)
    zeros_block = jnp.zeros_like(blocks[:, :1])
    earlier = jnp.concatenate([zeros_block, blocks[:, :-1]], axis=1)
    later = jnp.concatenate([blocks[:, 1:], zeros_block], axis=1)
    extended = jnp.concatenate([earlier, blocks, later], axis=2)
    offset = lax.iota(jnp.int32, 384)[:, None] - 128 - lax.iota(jnp.int32, 128)[None, :] + half
    weights = tap_lookup(offset, tap_table)
    result = jnp.einsum("cbr,rt->cbt", extended, weights, preferred_element_type=jnp.float32)
    return result.reshape(channels_here, samples)


def whiten(time_pass):
    power = jnp.mean(time_pass * time_pass, axis=-1, keepdims=True)
    return (time_pass * lax.rsqrt(power + 1e-06)).astype(jnp.bfloat16)


def corr_body(nb, rows, w_ref, p_ref, o_ref, s_ref):
    n = pl.program_id(0)
    k_count = p_ref.shape[0]
    lanes = 128

    @pl.when(n == 0)
    def _():
        o_ref[...] = jnp.zeros_like(o_ref)

    j_idx = lax.broadcasted_iota(jnp.int32, (rows, lanes), 0)
    r_idx = lax.broadcasted_iota(jnp.int32, (rows, lanes), 1)
    upper = r_idx >= j_idx
    for k in range(k_count):
        rolled = []
        for b in range(nb + 1):
            start = pl.multiple_of((n * nb + b) * lanes, lanes)
            chunk = p_ref[pl.ds(k, 1), pl.ds(start, lanes)]
            wide = jnp.broadcast_to(chunk, (rows, lanes))
            rolled.append(pltpu.roll(wide, 0, 1, stride=1, stride_axis=0))
        for b in range(nb):
            piece = jnp.where(upper, rolled[b + 1], rolled[b])
            s_ref[pl.ds(k * rows, rows), pl.ds(b * lanes, lanes)] = piece.astype(s_ref.dtype)
    o_ref[...] += lax.dot_general(
        s_ref[...], w_ref[...], (((1,), (1,)), ((), ())),
        preferred_element_type=jnp.float32)


def correlate_kernel(whitened, panel, nb=8):
    chans, samples = whitened.shape
    k_count = panel.shape[0]
    lanes = 128
    rows = CORR_ROWS
    padded = jnp.pad(panel.astype(jnp.float32), ((0, 0), (LAG, LAG)))
    grid = samples // (nb * lanes)
    out = pl.pallas_call(
        functools.partial(corr_body, nb, rows),
        grid=(grid,),
        in_specs=[
            pl.BlockSpec((chans, nb * lanes), lambda n: (0, n)),
            pl.BlockSpec((k_count, samples + 2 * LAG), lambda n: (0, 0)),
        ],
        out_specs=pl.BlockSpec((k_count * rows, chans), lambda n: (0, 0)),
        out_shape=jax.ShapeDtypeStruct((k_count * rows, chans), jnp.float32),
        scratch_shapes=[pltpu.VMEM((k_count * rows, nb * lanes), jnp.bfloat16)],
        compiler_params=pltpu.CompilerParams(dimension_semantics=("arbitrary",)),
        cost_estimate=pl.CostEstimate(
            flops=2 * k_count * rows * samples * chans,
            bytes_accessed=2 * chans * samples + 4 * k_count * (samples + rows * chans),
            transcendentals=0,
        ),
    )(whitened, padded)
    return out


def chan_filter(piece, tap_table):
    channels_here = piece.shape[0]
    half = (tap_table.shape[0] - 1) // 2
    widened = padded_2(piece, (("chan", 0),), half)
    total = jnp.dot(
        band_matrix(tap_table, channels_here, channels_here + 2 * half),
        widened,
        preferred_element_type=jnp.float32,
    )
    return total.astype(jnp.bfloat16)


def prep_body(section_chunk, rec_ref, lo_ref, hi_ref, blo_ref, bmid_ref, bhi_ref, tw_ref, o_ref, cp_ref, tp_ref):
    chans, samples = o_ref.shape
    lanes = 128
    cp_ref[:, pl.ds(0, lanes)] = jnp.zeros((chans, lanes), cp_ref.dtype)
    cp_ref[:, pl.ds(samples + lanes, lanes)] = jnp.zeros((chans, lanes), cp_ref.dtype)
    chunk = section_chunk

    def chan_step(i, carry):
        off = pl.multiple_of(i * chunk, chunk)
        total = jnp.dot(bmid_ref[...], rec_ref[0, :, pl.ds(off, chunk)], preferred_element_type=jnp.float32)
        total += jnp.dot(blo_ref[...], lo_ref[:, pl.ds(off, chunk)], preferred_element_type=jnp.float32)
        total += jnp.dot(bhi_ref[...], hi_ref[:, pl.ds(off, chunk)], preferred_element_type=jnp.float32)
        cp_ref[:, pl.ds(pl.multiple_of(off + lanes, lanes), chunk)] = total.astype(cp_ref.dtype)
        return carry

    lax.fori_loop(0, samples // chunk, chan_step, 0)

    group = 8

    def time_step(g, acc):
        base = g * group
        windows = [
            cp_ref[:, pl.ds(pl.multiple_of((base + q) * lanes, lanes), 3 * lanes)]
            for q in range(group)
        ]
        y = jnp.dot(jnp.concatenate(windows, axis=0), tw_ref[...], preferred_element_type=jnp.float32)
        for q in range(group):
            part = y[q * chans : (q + 1) * chans]
            tp_ref[:, pl.ds(pl.multiple_of((base + q) * lanes, lanes), lanes)] = part
            acc = acc + part * part
        return acc

    acc = lax.fori_loop(0, samples // (lanes * group), time_step, jnp.zeros((chans, lanes), jnp.float32))
    power = jnp.sum(acc, axis=1, keepdims=True) / samples
    scale = lax.rsqrt(power + 1e-06)

    def white_step(i, carry):
        off = pl.multiple_of(i * chunk, chunk)
        o_ref[:, pl.ds(off, chunk)] = (tp_ref[:, pl.ds(off, chunk)] * scale).astype(o_ref.dtype)
        return carry

    lax.fori_loop(0, samples // chunk, white_step, 0)


def prepare_kernel(record, section, lo, hi, band, time_weights):
    count_steps, chans, samples = record.shape
    half = lo.shape[0]
    lanes = 128
    chunk = 512
    blo, bmid, bhi = band[:, :half], band[:, half:half + chans], band[:, half + chans:]
    full = lambda i: (0, 0)
    return pl.pallas_call(
        functools.partial(prep_body, chunk),
        grid=(1,),
        in_specs=[
            pl.BlockSpec((1, chans, samples), lambda i: (section, 0, 0)),
            pl.BlockSpec((half, samples), full),
            pl.BlockSpec((half, samples), full),
            pl.BlockSpec((chans, half), full),
            pl.BlockSpec((chans, chans), full),
            pl.BlockSpec((chans, half), full),
            pl.BlockSpec(time_weights.shape, full),
        ],
        out_specs=pl.BlockSpec((chans, samples), full),
        out_shape=jax.ShapeDtypeStruct((chans, samples), jnp.bfloat16),
        scratch_shapes=[
            pltpu.VMEM((chans, samples + 2 * lanes), jnp.bfloat16),
            pltpu.VMEM((chans, samples), jnp.float32),
        ],
        compiler_params=pltpu.CompilerParams(vmem_limit_bytes=48 * 1024 * 1024),
        cost_estimate=pl.CostEstimate(
            flops=2 * chans * samples * (chans + 2 * half + 3 * lanes),
            bytes_accessed=2 * samples * (2 * chans + 2 * half),
            transcendentals=chans,
        ),
    )(record, lo, hi, blo, bmid, bhi, time_weights)


def xor_sum(x, axis):
    count = lax.axis_size(axis)
    if count & (count - 1):
        return lax.psum(x, axis)
    step = 1
    while step < count:
        x = x + lax.ppermute(x, axis, [(i, i ^ step) for i in range(count)])
        step *= 2
    return x


def body(record, chan_taps, time_taps, sources):
    count_steps = record.shape[0]
    channels_here = record.shape[1]
    samples = record.shape[2]
    chan_table = chan_taps.astype(jnp.bfloat16)
    time_table = time_taps.astype(jnp.bfloat16)
    first_chan = lax.axis_index("chan") * channels_here
    selector = (
        (sources - first_chan)[:, :, None] == lax.iota(jnp.int32, channels_here)[None, None, :]
    ).astype(jnp.bfloat16)
    normalizer = 1.0 / math.sqrt(samples * lax.axis_size("win"))

    half = (chan_table.shape[0] - 1) // 2
    count = lax.axis_size("chan")
    band = band_matrix(chan_table, channels_here, channels_here + 2 * half)
    offset = lax.iota(jnp.int32, 384)[:, None] - 128 - lax.iota(jnp.int32, 128)[None, :]
    time_weights = tap_lookup(offset + (time_table.shape[0] - 1) // 2, time_table)

    heads = record[:, :half]
    tails = record[:, channels_here - half :]
    lowers = lax.ppermute(tails, "chan", [(i, i + 1) for i in range(count - 1)])
    uppers = lax.ppermute(heads, "chan", [(i + 1, i) for i in range(count - 1)])

    def prepare(whole, section):
        lower, upper = lowers[section], uppers[section]
        whitened = prepare_kernel(whole, section, lower, upper, band, time_weights)
        term = jnp.dot(selector[section], whitened, preferred_element_type=jnp.float32)
        return whitened, xor_sum(term.astype(jnp.bfloat16), "chan")

    pieces = [record] * count_steps
    results = []
    pending = prepare(pieces[0], 0)
    for section in range(count_steps):
        upcoming = None
        if section + 1 < count_steps:
            upcoming = prepare(pieces[section + 1], section + 1)
        whitened, panel = pending
        if section >= 2:
            whitened, panel, results[section - 2] = lax.optimization_barrier(
                (whitened, panel, results[section - 2])
            )
        if section + 1 < count_steps:
            partial_corr = correlate_kernel(whitened, panel)
            if section + 2 < count_steps:
                pieces[section + 2], partial_corr = lax.optimization_barrier(
                    (pieces[section + 2], partial_corr)
                )
            results.append(xor_sum(partial_corr, "win"))
        else:
            half = panel.shape[0] // 2
            parts = [
                xor_sum(correlate_kernel(whitened, panel[:half]), "win"),
                xor_sum(correlate_kernel(whitened, panel[half:]), "win"),
            ]
            results.append(jnp.concatenate(parts, axis=0))
        pending = upcoming
    lags = 2 * LAG + 1
    shaped = [total.reshape(-1, CORR_ROWS, channels_here)[:, :lags] for total in results]
    return jnp.stack(shaped) * normalizer


def solution(mesh):
    in_specs = (P(None, "chan", "win"), P(), P(), P())
    out_specs = P(None, None, None, "chan")
    return jax.shard_map(body, mesh=mesh, in_specs=in_specs, out_specs=out_specs, check_vma=False)
```

```python
import functools
import math

import jax
import jax.numpy as jnp
from jax import lax
from jax.experimental import pallas as pl
from jax.experimental.pallas import tpu as pltpu
from jax.sharding import PartitionSpec as P

LAG = 64
CORR_ROWS = 136


def padded_2(cells, sides, width):
    for axis, dim in sides:
        count = lax.axis_size(axis)
        ends = count - 1
        head = lax.slice_in_dim(cells, 0, width, axis=dim)
        tail = lax.slice_in_dim(cells, cells.shape[dim] - width, cells.shape[dim], axis=dim)
        cells = jnp.concatenate(
            [
                lax.ppermute(tail, axis, [(i, (i + 1) % count) for i in range(ends)]),
                cells,
                lax.ppermute(head, axis, [((i + 1) % count, i) for i in range(ends)]),
            ],
            axis=dim,
        )
    return cells


def tap_lookup(offset, tap_table):
    count_taps = tap_table.shape[0]
    marks = offset[..., None] == lax.iota(jnp.int32, count_taps)
    picked = jnp.where(marks, tap_table.astype(jnp.float32), jnp.zeros((), jnp.float32))
    return jnp.sum(picked, axis=-1).astype(tap_table.dtype)


def band_matrix(tap_table, height, breadth):
    offset = lax.iota(jnp.int32, breadth)[None, :] - lax.iota(jnp.int32, height)[:, None]
    return tap_lookup(offset, tap_table)


def time_filter(chan_pass, tap_table):
    channels_here, samples = chan_pass.shape
    half = (tap_table.shape[0] - 1) // 2
    blocks = chan_pass.reshape(channels_here, samples // 128, 128)
    zeros_block = jnp.zeros_like(blocks[:, :1])
    earlier = jnp.concatenate([zeros_block, blocks[:, :-1]], axis=1)
    later = jnp.concatenate([blocks[:, 1:], zeros_block], axis=1)
    extended = jnp.concatenate([earlier, blocks, later], axis=2)
    offset = lax.iota(jnp.int32, 384)[:, None] - 128 - lax.iota(jnp.int32, 128)[None, :] + half
    weights = tap_lookup(offset, tap_table)
    result = jnp.einsum("cbr,rt->cbt", extended, weights, preferred_element_type=jnp.float32)
    return result.reshape(channels_here, samples)


def whiten(time_pass):
    power = jnp.mean(time_pass * time_pass, axis=-1, keepdims=True)
    return (time_pass * lax.rsqrt(power + 1e-06)).astype(jnp.bfloat16)


def corr_body(nb, rows, w_ref, p_ref, o_ref, s_ref):
    n = pl.program_id(0)
    k_count = p_ref.shape[0]
    lanes = 128

    @pl.when(n == 0)
    def _():
        o_ref[...] = jnp.zeros_like(o_ref)

    j_idx = lax.broadcasted_iota(jnp.int32, (rows, lanes), 0)
    r_idx = lax.broadcasted_iota(jnp.int32, (rows, lanes), 1)
    upper = r_idx >= j_idx
    for k in range(k_count):
        rolled = []
        for b in range(nb + 1):
            start = pl.multiple_of((n * nb + b) * lanes, lanes)
            chunk = p_ref[pl.ds(k, 1), pl.ds(start, lanes)]
            wide = jnp.broadcast_to(chunk, (rows, lanes))
            rolled.append(pltpu.roll(wide, 0, 1, stride=1, stride_axis=0))
        for b in range(nb):
            piece = jnp.where(upper, rolled[b + 1], rolled[b])
            s_ref[pl.ds(k * rows, rows), pl.ds(b * lanes, lanes)] = piece.astype(s_ref.dtype)
    o_ref[...] += lax.dot_general(
        s_ref[...], w_ref[...], (((1,), (1,)), ((), ())),
        preferred_element_type=jnp.float32)


def correlate_kernel(whitened, panel, nb=8):
    chans, samples = whitened.shape
    k_count = panel.shape[0]
    lanes = 128
    rows = CORR_ROWS
    padded = jnp.pad(panel.astype(jnp.float32), ((0, 0), (LAG, LAG)))
    grid = samples // (nb * lanes)
    out = pl.pallas_call(
        functools.partial(corr_body, nb, rows),
        grid=(grid,),
        in_specs=[
            pl.BlockSpec((chans, nb * lanes), lambda n: (0, n)),
            pl.BlockSpec((k_count, samples + 2 * LAG), lambda n: (0, 0)),
        ],
        out_specs=pl.BlockSpec((k_count * rows, chans), lambda n: (0, 0)),
        out_shape=jax.ShapeDtypeStruct((k_count * rows, chans), jnp.float32),
        scratch_shapes=[pltpu.VMEM((k_count * rows, nb * lanes), jnp.bfloat16)],
        compiler_params=pltpu.CompilerParams(dimension_semantics=("arbitrary",)),
        cost_estimate=pl.CostEstimate(
            flops=2 * k_count * rows * samples * chans,
            bytes_accessed=2 * chans * samples + 4 * k_count * (samples + rows * chans),
            transcendentals=0,
        ),
    )(whitened, padded)
    return out


def chan_filter(piece, tap_table):
    channels_here = piece.shape[0]
    half = (tap_table.shape[0] - 1) // 2
    widened = padded_2(piece, (("chan", 0),), half)
    total = jnp.dot(
        band_matrix(tap_table, channels_here, channels_here + 2 * half),
        widened,
        preferred_element_type=jnp.float32,
    )
    return total.astype(jnp.bfloat16)


def prep_body(section_chunk, rec_ref, lo_ref, hi_ref, blo_ref, bmid_ref, bhi_ref, tw_ref, o_ref, cp_ref, tp_ref):
    chans, samples = o_ref.shape
    lanes = 128
    cp_ref[:, pl.ds(0, lanes)] = jnp.zeros((chans, lanes), cp_ref.dtype)
    cp_ref[:, pl.ds(samples + lanes, lanes)] = jnp.zeros((chans, lanes), cp_ref.dtype)
    chunk = section_chunk

    def chan_step(i, carry):
        off = pl.multiple_of(i * chunk, chunk)
        total = jnp.dot(bmid_ref[...], rec_ref[0, :, pl.ds(off, chunk)], preferred_element_type=jnp.float32)
        total += jnp.dot(blo_ref[...], lo_ref[:, pl.ds(off, chunk)], preferred_element_type=jnp.float32)
        total += jnp.dot(bhi_ref[...], hi_ref[:, pl.ds(off, chunk)], preferred_element_type=jnp.float32)
        cp_ref[:, pl.ds(pl.multiple_of(off + lanes, lanes), chunk)] = total.astype(cp_ref.dtype)
        return carry

    lax.fori_loop(0, samples // chunk, chan_step, 0)

    group = 8

    def time_step(g, acc):
        base = g * group
        windows = [
            cp_ref[:, pl.ds(pl.multiple_of((base + q) * lanes, lanes), 3 * lanes)]
            for q in range(group)
        ]
        y = jnp.dot(jnp.concatenate(windows, axis=0), tw_ref[...], preferred_element_type=jnp.float32)
        for q in range(group):
            part = y[q * chans : (q + 1) * chans]
            tp_ref[:, pl.ds(pl.multiple_of((base + q) * lanes, lanes), lanes)] = part
            acc = acc + part * part
        return acc

    acc = lax.fori_loop(0, samples // (lanes * group), time_step, jnp.zeros((chans, lanes), jnp.float32))
    power = jnp.sum(acc, axis=1, keepdims=True) / samples
    scale = lax.rsqrt(power + 1e-06)

    def white_step(i, carry):
        off = pl.multiple_of(i * chunk, chunk)
        o_ref[:, pl.ds(off, chunk)] = (tp_ref[:, pl.ds(off, chunk)] * scale).astype(o_ref.dtype)
        return carry

    lax.fori_loop(0, samples // chunk, white_step, 0)


def prepare_kernel(record, section, lo, hi, band, time_weights):
    count_steps, chans, samples = record.shape
    half = lo.shape[0]
    lanes = 128
    chunk = 512
    blo, bmid, bhi = band[:, :half], band[:, half:half + chans], band[:, half + chans:]
    full = lambda i: (0, 0)
    return pl.pallas_call(
        functools.partial(prep_body, chunk),
        grid=(1,),
        in_specs=[
            pl.BlockSpec((1, chans, samples), lambda i: (section, 0, 0)),
            pl.BlockSpec((half, samples), full),
            pl.BlockSpec((half, samples), full),
            pl.BlockSpec((chans, half), full),
            pl.BlockSpec((chans, chans), full),
            pl.BlockSpec((chans, half), full),
            pl.BlockSpec(time_weights.shape, full),
        ],
        out_specs=pl.BlockSpec((chans, samples), full),
        out_shape=jax.ShapeDtypeStruct((chans, samples), jnp.bfloat16),
        scratch_shapes=[
            pltpu.VMEM((chans, samples + 2 * lanes), jnp.bfloat16),
            pltpu.VMEM((chans, samples), jnp.float32),
        ],
        compiler_params=pltpu.CompilerParams(vmem_limit_bytes=48 * 1024 * 1024),
        cost_estimate=pl.CostEstimate(
            flops=2 * chans * samples * (chans + 2 * half + 3 * lanes),
            bytes_accessed=2 * samples * (2 * chans + 2 * half),
            transcendentals=chans,
        ),
    )(record, lo, hi, blo, bmid, bhi, time_weights)


def xor_sum(x, axis):
    count = lax.axis_size(axis)
    if count & (count - 1):
        return lax.psum(x, axis)
    step = 1
    while step < count:
        x = x + lax.ppermute(x, axis, [(i, i ^ step) for i in range(count)])
        step *= 2
    return x


def body(record, chan_taps, time_taps, sources):
    count_steps = record.shape[0]
    channels_here = record.shape[1]
    samples = record.shape[2]
    chan_table = chan_taps.astype(jnp.bfloat16)
    time_table = time_taps.astype(jnp.bfloat16)
    first_chan = lax.axis_index("chan") * channels_here
    selector = (
        (sources - first_chan)[:, :, None] == lax.iota(jnp.int32, channels_here)[None, None, :]
    ).astype(jnp.bfloat16)
    normalizer = 1.0 / math.sqrt(samples * lax.axis_size("win"))

    half = (chan_table.shape[0] - 1) // 2
    count = lax.axis_size("chan")
    band = band_matrix(chan_table, channels_here, channels_here + 2 * half)
    offset = lax.iota(jnp.int32, 384)[:, None] - 128 - lax.iota(jnp.int32, 128)[None, :]
    time_weights = tap_lookup(offset + (time_table.shape[0] - 1) // 2, time_table)

    heads = record[:, :half]
    tails = record[:, channels_here - half :]
    lowers = lax.ppermute(tails, "chan", [(i, i + 1) for i in range(count - 1)])
    uppers = lax.ppermute(heads, "chan", [(i + 1, i) for i in range(count - 1)])

    active = {}

    def hold(values):
        keys = sorted(active)
        values, held = lax.optimization_barrier((values, [active[key][0] for key in keys]))
        for key, value in zip(keys, held):
            active[key][0] = value
        return values

    def advance(key):
        value, step, axis = active[key]
        value = value + lax.ppermute(value, axis, [(i, i ^ step) for i in range(lax.axis_size(axis))])
        active[key] = [value, step * 2, axis]

    def advance_all():
        for key in sorted(active):
            if active[key][1] < lax.axis_size(active[key][2]):
                advance(key)

    def finish(key):
        while active[key][1] < lax.axis_size(active[key][2]):
            advance(key)
        return active.pop(key)[0]

    def start(key, value, axis):
        if lax.axis_size(axis) & (lax.axis_size(axis) - 1):
            active[key] = [lax.psum(value, axis), lax.axis_size(axis), axis]
        else:
            active[key] = [value, 1, axis]

    whitened = []
    for section in range(count_steps):
        inputs = hold((record, lowers[section], uppers[section]))
        advance_all()
        piece = prepare_kernel(inputs[0], section, inputs[1], inputs[2], band, time_weights)
        whitened.append(piece)
        term = jnp.dot(selector[section], piece, preferred_element_type=jnp.float32)
        start(("panel", section), term.astype(jnp.bfloat16), "chan")
    results = {}
    for section in range(count_steps):
        panel = finish(("panel", section))
        quarters = [panel] if section + 1 < count_steps else [panel[: panel.shape[0] // 2], panel[panel.shape[0] // 2 :]]
        for index, part in enumerate(quarters):
            piece, part = hold((whitened[section], part))
            advance_all()
            start(("win", section, index), correlate_kernel(piece, part), "win")
    for key in sorted(active):
        results[key] = finish(key)
    outputs = []
    for section in range(count_steps):
        keys = sorted(key for key in results if key[1] == section)
        outputs.append(jnp.concatenate([results[key] for key in keys], axis=0))
    results = outputs
    lags = 2 * LAG + 1
    shaped = [total.reshape(-1, CORR_ROWS, channels_here)[:, :lags] for total in results]
    return jnp.stack(shaped) * normalizer


def solution(mesh):
    in_specs = (P(None, "chan", "win"), P(), P(), P())
    out_specs = P(None, None, None, "chan")
    return jax.shard_map(body, mesh=mesh, in_specs=in_specs, out_specs=out_specs, check_vma=False)
```

```python
import functools
import math

import jax
import jax.numpy as jnp
from jax import lax
from jax.experimental import pallas as pl
from jax.experimental.pallas import tpu as pltpu
from jax.sharding import PartitionSpec as P

LAG = 64
CORR_ROWS = 136


def padded_2(cells, sides, width):
    for axis, dim in sides:
        count = lax.axis_size(axis)
        ends = count - 1
        head = lax.slice_in_dim(cells, 0, width, axis=dim)
        tail = lax.slice_in_dim(cells, cells.shape[dim] - width, cells.shape[dim], axis=dim)
        cells = jnp.concatenate(
            [
                lax.ppermute(tail, axis, [(i, (i + 1) % count) for i in range(ends)]),
                cells,
                lax.ppermute(head, axis, [((i + 1) % count, i) for i in range(ends)]),
            ],
            axis=dim,
        )
    return cells


def tap_lookup(offset, tap_table):
    count_taps = tap_table.shape[0]
    marks = offset[..., None] == lax.iota(jnp.int32, count_taps)
    picked = jnp.where(marks, tap_table.astype(jnp.float32), jnp.zeros((), jnp.float32))
    return jnp.sum(picked, axis=-1).astype(tap_table.dtype)


def band_matrix(tap_table, height, breadth):
    offset = lax.iota(jnp.int32, breadth)[None, :] - lax.iota(jnp.int32, height)[:, None]
    return tap_lookup(offset, tap_table)


def time_filter(chan_pass, tap_table):
    channels_here, samples = chan_pass.shape
    half = (tap_table.shape[0] - 1) // 2
    blocks = chan_pass.reshape(channels_here, samples // 128, 128)
    zeros_block = jnp.zeros_like(blocks[:, :1])
    earlier = jnp.concatenate([zeros_block, blocks[:, :-1]], axis=1)
    later = jnp.concatenate([blocks[:, 1:], zeros_block], axis=1)
    extended = jnp.concatenate([earlier, blocks, later], axis=2)
    offset = lax.iota(jnp.int32, 384)[:, None] - 128 - lax.iota(jnp.int32, 128)[None, :] + half
    weights = tap_lookup(offset, tap_table)
    result = jnp.einsum("cbr,rt->cbt", extended, weights, preferred_element_type=jnp.float32)
    return result.reshape(channels_here, samples)


def whiten(time_pass):
    power = jnp.mean(time_pass * time_pass, axis=-1, keepdims=True)
    return (time_pass * lax.rsqrt(power + 1e-06)).astype(jnp.bfloat16)


def corr_body(nb, rows, w_ref, p_ref, o_ref, s_ref):
    n = pl.program_id(0)
    k_count = p_ref.shape[0]
    lanes = 128

    @pl.when(n == 0)
    def _():
        o_ref[...] = jnp.zeros_like(o_ref)

    j_idx = lax.broadcasted_iota(jnp.int32, (rows, lanes), 0)
    r_idx = lax.broadcasted_iota(jnp.int32, (rows, lanes), 1)
    upper = r_idx >= j_idx
    for k in range(k_count):
        rolled = []
        for b in range(nb + 1):
            start = pl.multiple_of((n * nb + b) * lanes, lanes)
            chunk = p_ref[pl.ds(k, 1), pl.ds(start, lanes)]
            wide = jnp.broadcast_to(chunk, (rows, lanes))
            rolled.append(pltpu.roll(wide, 0, 1, stride=1, stride_axis=0))
        for b in range(nb):
            piece = jnp.where(upper, rolled[b + 1], rolled[b])
            s_ref[pl.ds(k * rows, rows), pl.ds(b * lanes, lanes)] = piece.astype(s_ref.dtype)
    o_ref[...] += lax.dot_general(
        s_ref[...], w_ref[...], (((1,), (1,)), ((), ())),
        preferred_element_type=jnp.float32)


def correlate_kernel(whitened, panel, nb=8):
    chans, samples = whitened.shape
    k_count = panel.shape[0]
    lanes = 128
    rows = CORR_ROWS
    padded = jnp.pad(panel.astype(jnp.float32), ((0, 0), (LAG, LAG)))
    grid = samples // (nb * lanes)
    out = pl.pallas_call(
        functools.partial(corr_body, nb, rows),
        grid=(grid,),
        in_specs=[
            pl.BlockSpec((chans, nb * lanes), lambda n: (0, n)),
            pl.BlockSpec((k_count, samples + 2 * LAG), lambda n: (0, 0)),
        ],
        out_specs=pl.BlockSpec((k_count * rows, chans), lambda n: (0, 0)),
        out_shape=jax.ShapeDtypeStruct((k_count * rows, chans), jnp.float32),
        scratch_shapes=[pltpu.VMEM((k_count * rows, nb * lanes), jnp.bfloat16)],
        compiler_params=pltpu.CompilerParams(dimension_semantics=("arbitrary",)),
        cost_estimate=pl.CostEstimate(
            flops=2 * k_count * rows * samples * chans,
            bytes_accessed=2 * chans * samples + 4 * k_count * (samples + rows * chans),
            transcendentals=0,
        ),
    )(whitened, padded)
    return out


def chan_filter(piece, tap_table):
    channels_here = piece.shape[0]
    half = (tap_table.shape[0] - 1) // 2
    widened = padded_2(piece, (("chan", 0),), half)
    total = jnp.dot(
        band_matrix(tap_table, channels_here, channels_here + 2 * half),
        widened,
        preferred_element_type=jnp.float32,
    )
    return total.astype(jnp.bfloat16)


def prep_body(section_chunk, rec_ref, lo_ref, hi_ref, blo_ref, bmid_ref, bhi_ref, tw_ref, o_ref, cp_ref, tp_ref):
    chans, samples = o_ref.shape
    lanes = 128
    cp_ref[:, pl.ds(0, lanes)] = jnp.zeros((chans, lanes), cp_ref.dtype)
    cp_ref[:, pl.ds(samples + lanes, lanes)] = jnp.zeros((chans, lanes), cp_ref.dtype)
    chunk = section_chunk

    def chan_step(i, carry):
        off = pl.multiple_of(i * chunk, chunk)
        total = jnp.dot(bmid_ref[...], rec_ref[0, :, pl.ds(off, chunk)], preferred_element_type=jnp.float32)
        total += jnp.dot(blo_ref[...], lo_ref[:, pl.ds(off, chunk)], preferred_element_type=jnp.float32)
        total += jnp.dot(bhi_ref[...], hi_ref[:, pl.ds(off, chunk)], preferred_element_type=jnp.float32)
        cp_ref[:, pl.ds(pl.multiple_of(off + lanes, lanes), chunk)] = total.astype(cp_ref.dtype)
        return carry

    lax.fori_loop(0, samples // chunk, chan_step, 0)

    group = 8

    def time_step(g, acc):
        base = g * group
        windows = [
            cp_ref[:, pl.ds(pl.multiple_of((base + q) * lanes, lanes), 3 * lanes)]
            for q in range(group)
        ]
        y = jnp.dot(jnp.concatenate(windows, axis=0), tw_ref[...], preferred_element_type=jnp.float32)
        for q in range(group):
            part = y[q * chans : (q + 1) * chans]
            tp_ref[:, pl.ds(pl.multiple_of((base + q) * lanes, lanes), lanes)] = part
            acc = acc + part * part
        return acc

    acc = lax.fori_loop(0, samples // (lanes * group), time_step, jnp.zeros((chans, lanes), jnp.float32))
    power = jnp.sum(acc, axis=1, keepdims=True) / samples
    scale = lax.rsqrt(power + 1e-06)

    def white_step(i, carry):
        off = pl.multiple_of(i * chunk, chunk)
        o_ref[:, pl.ds(off, chunk)] = (tp_ref[:, pl.ds(off, chunk)] * scale).astype(o_ref.dtype)
        return carry

    lax.fori_loop(0, samples // chunk, white_step, 0)


def prepare_kernel(record, section, lo, hi, band, time_weights):
    count_steps, chans, samples = record.shape
    half = lo.shape[0]
    lanes = 128
    chunk = 512
    blo, bmid, bhi = band[:, :half], band[:, half:half + chans], band[:, half + chans:]
    full = lambda i: (0, 0)
    return pl.pallas_call(
        functools.partial(prep_body, chunk),
        grid=(1,),
        in_specs=[
            pl.BlockSpec((1, chans, samples), lambda i: (section, 0, 0)),
            pl.BlockSpec((half, samples), full),
            pl.BlockSpec((half, samples), full),
            pl.BlockSpec((chans, half), full),
            pl.BlockSpec((chans, chans), full),
            pl.BlockSpec((chans, half), full),
            pl.BlockSpec(time_weights.shape, full),
        ],
        out_specs=pl.BlockSpec((chans, samples), full),
        out_shape=jax.ShapeDtypeStruct((chans, samples), jnp.bfloat16),
        scratch_shapes=[
            pltpu.VMEM((chans, samples + 2 * lanes), jnp.bfloat16),
            pltpu.VMEM((chans, samples), jnp.float32),
        ],
        compiler_params=pltpu.CompilerParams(vmem_limit_bytes=48 * 1024 * 1024),
        cost_estimate=pl.CostEstimate(
            flops=2 * chans * samples * (chans + 2 * half + 3 * lanes),
            bytes_accessed=2 * samples * (2 * chans + 2 * half),
            transcendentals=chans,
        ),
    )(record, lo, hi, blo, bmid, bhi, time_weights)


def xor_sum(x, axis):
    count = lax.axis_size(axis)
    if count & (count - 1):
        return lax.psum(x, axis)
    step = 1
    while step < count:
        x = x + lax.ppermute(x, axis, [(i, i ^ step) for i in range(count)])
        step *= 2
    return x


def narrow_sum(x, axis):
    count = lax.axis_size(axis)
    if count & (count - 1):
        return lax.psum(x, axis)
    step = 1
    while step < count:
        sent = x.astype(jnp.bfloat16)
        got = lax.ppermute(sent, axis, [(i, i ^ step) for i in range(count)])
        x = sent.astype(jnp.float32) + got.astype(jnp.float32)
        step *= 2
    return x


def body(record, chan_taps, time_taps, sources):
    count_steps = record.shape[0]
    channels_here = record.shape[1]
    samples = record.shape[2]
    chan_table = chan_taps.astype(jnp.bfloat16)
    time_table = time_taps.astype(jnp.bfloat16)
    first_chan = lax.axis_index("chan") * channels_here
    selector = (
        (sources - first_chan)[:, :, None] == lax.iota(jnp.int32, channels_here)[None, None, :]
    ).astype(jnp.bfloat16)
    normalizer = 1.0 / math.sqrt(samples * lax.axis_size("win"))

    half = (chan_table.shape[0] - 1) // 2
    count = lax.axis_size("chan")
    band = band_matrix(chan_table, channels_here, channels_here + 2 * half)
    offset = lax.iota(jnp.int32, 384)[:, None] - 128 - lax.iota(jnp.int32, 128)[None, :]
    time_weights = tap_lookup(offset + (time_table.shape[0] - 1) // 2, time_table)

    heads = record[:, :half]
    tails = record[:, channels_here - half :]
    lowers = lax.ppermute(tails, "chan", [(i, i + 1) for i in range(count - 1)])
    uppers = lax.ppermute(heads, "chan", [(i + 1, i) for i in range(count - 1)])

    def prepare(whole, section):
        lower, upper = lowers[section], uppers[section]
        whitened = prepare_kernel(whole, section, lower, upper, band, time_weights)
        term = jnp.dot(selector[section], whitened, preferred_element_type=jnp.float32)
        return whitened, xor_sum(term.astype(jnp.bfloat16), "chan")

    pieces = [record] * count_steps
    results = []
    pending = prepare(pieces[0], 0)
    for section in range(count_steps):
        upcoming = None
        if section + 1 < count_steps:
            upcoming = prepare(pieces[section + 1], section + 1)
        whitened, panel = pending
        if section >= 2:
            whitened, panel, results[section - 2] = lax.optimization_barrier(
                (whitened, panel, results[section - 2])
            )
        if section + 1 < count_steps:
            partial_corr = correlate_kernel(whitened, panel)
            if section + 2 < count_steps:
                pieces[section + 2], partial_corr = lax.optimization_barrier(
                    (pieces[section + 2], partial_corr)
                )
            results.append(narrow_sum(partial_corr, "win"))
        else:
            half = panel.shape[0] // 2
            parts = [
                narrow_sum(correlate_kernel(whitened, panel[:half]), "win"),
                narrow_sum(correlate_kernel(whitened, panel[half:]), "win"),
            ]
            results.append(jnp.concatenate(parts, axis=0))
        pending = upcoming
    lags = 2 * LAG + 1
    shaped = [total.reshape(-1, CORR_ROWS, channels_here)[:, :lags] for total in results]
    return jnp.stack(shaped) * normalizer


def solution(mesh):
    in_specs = (P(None, "chan", "win"), P(), P(), P())
    out_specs = P(None, None, None, "chan")
    return jax.shard_map(body, mesh=mesh, in_specs=in_specs, out_specs=out_specs, check_vma=False)
```

```python
import functools
import math

import jax
import jax.numpy as jnp
from jax import lax
from jax.experimental import pallas as pl
from jax.experimental.pallas import tpu as pltpu
from jax.sharding import PartitionSpec as P

LAG = 64
CORR_ROWS = 136


def padded_2(cells, sides, width):
    for axis, dim in sides:
        count = lax.axis_size(axis)
        ends = count - 1
        head = lax.slice_in_dim(cells, 0, width, axis=dim)
        tail = lax.slice_in_dim(cells, cells.shape[dim] - width, cells.shape[dim], axis=dim)
        cells = jnp.concatenate(
            [
                lax.ppermute(tail, axis, [(i, (i + 1) % count) for i in range(ends)]),
                cells,
                lax.ppermute(head, axis, [((i + 1) % count, i) for i in range(ends)]),
            ],
            axis=dim,
        )
    return cells


def tap_lookup(offset, tap_table):
    count_taps = tap_table.shape[0]
    marks = offset[..., None] == lax.iota(jnp.int32, count_taps)
    picked = jnp.where(marks, tap_table.astype(jnp.float32), jnp.zeros((), jnp.float32))
    return jnp.sum(picked, axis=-1).astype(tap_table.dtype)


def band_matrix(tap_table, height, breadth):
    offset = lax.iota(jnp.int32, breadth)[None, :] - lax.iota(jnp.int32, height)[:, None]
    return tap_lookup(offset, tap_table)


def time_filter(chan_pass, tap_table):
    channels_here, samples = chan_pass.shape
    half = (tap_table.shape[0] - 1) // 2
    blocks = chan_pass.reshape(channels_here, samples // 128, 128)
    zeros_block = jnp.zeros_like(blocks[:, :1])
    earlier = jnp.concatenate([zeros_block, blocks[:, :-1]], axis=1)
    later = jnp.concatenate([blocks[:, 1:], zeros_block], axis=1)
    extended = jnp.concatenate([earlier, blocks, later], axis=2)
    offset = lax.iota(jnp.int32, 384)[:, None] - 128 - lax.iota(jnp.int32, 128)[None, :] + half
    weights = tap_lookup(offset, tap_table)
    result = jnp.einsum("cbr,rt->cbt", extended, weights, preferred_element_type=jnp.float32)
    return result.reshape(channels_here, samples)


def whiten(time_pass):
    power = jnp.mean(time_pass * time_pass, axis=-1, keepdims=True)
    return (time_pass * lax.rsqrt(power + 1e-06)).astype(jnp.bfloat16)


def corr_body(nb, rows, w_ref, p_ref, o_ref, s_ref):
    n = pl.program_id(0)
    k_count = p_ref.shape[0]
    lanes = 128

    @pl.when(n == 0)
    def _():
        o_ref[...] = jnp.zeros_like(o_ref)

    j_idx = lax.broadcasted_iota(jnp.int32, (rows, lanes), 0)
    r_idx = lax.broadcasted_iota(jnp.int32, (rows, lanes), 1)
    upper = r_idx >= j_idx
    for k in range(k_count):
        rolled = []
        for b in range(nb + 1):
            start = pl.multiple_of((n * nb + b) * lanes, lanes)
            chunk = p_ref[pl.ds(k, 1), pl.ds(start, lanes)]
            wide = jnp.broadcast_to(chunk, (rows, lanes))
            rolled.append(pltpu.roll(wide, 0, 1, stride=1, stride_axis=0))
        for b in range(nb):
            piece = jnp.where(upper, rolled[b + 1], rolled[b])
            s_ref[pl.ds(k * rows, rows), pl.ds(b * lanes, lanes)] = piece.astype(s_ref.dtype)
    o_ref[...] += lax.dot_general(
        s_ref[...], w_ref[...], (((1,), (1,)), ((), ())),
        preferred_element_type=jnp.float32)


def correlate_kernel(whitened, panel, nb=8):
    chans, samples = whitened.shape
    k_count = panel.shape[0]
    lanes = 128
    rows = CORR_ROWS
    padded = jnp.pad(panel.astype(jnp.float32), ((0, 0), (LAG, LAG)))
    grid = samples // (nb * lanes)
    out = pl.pallas_call(
        functools.partial(corr_body, nb, rows),
        grid=(grid,),
        in_specs=[
            pl.BlockSpec((chans, nb * lanes), lambda n: (0, n)),
            pl.BlockSpec((k_count, samples + 2 * LAG), lambda n: (0, 0)),
        ],
        out_specs=pl.BlockSpec((k_count * rows, chans), lambda n: (0, 0)),
        out_shape=jax.ShapeDtypeStruct((k_count * rows, chans), jnp.float32),
        scratch_shapes=[pltpu.VMEM((k_count * rows, nb * lanes), jnp.bfloat16)],
        compiler_params=pltpu.CompilerParams(dimension_semantics=("arbitrary",)),
        cost_estimate=pl.CostEstimate(
            flops=2 * k_count * rows * samples * chans,
            bytes_accessed=2 * chans * samples + 4 * k_count * (samples + rows * chans),
            transcendentals=0,
        ),
    )(whitened, padded)
    return out


def chan_filter(piece, tap_table):
    channels_here = piece.shape[0]
    half = (tap_table.shape[0] - 1) // 2
    widened = padded_2(piece, (("chan", 0),), half)
    total = jnp.dot(
        band_matrix(tap_table, channels_here, channels_here + 2 * half),
        widened,
        preferred_element_type=jnp.float32,
    )
    return total.astype(jnp.bfloat16)


def prep_body(section_chunk, rec_ref, lo_ref, hi_ref, blo_ref, bmid_ref, bhi_ref, tw_ref, o_ref, cp_ref, tp_ref):
    chans, samples = o_ref.shape
    lanes = 128
    cp_ref[:, pl.ds(0, lanes)] = jnp.zeros((chans, lanes), cp_ref.dtype)
    cp_ref[:, pl.ds(samples + lanes, lanes)] = jnp.zeros((chans, lanes), cp_ref.dtype)
    chunk = section_chunk

    def chan_step(i, carry):
        off = pl.multiple_of(i * chunk, chunk)
        total = jnp.dot(bmid_ref[...], rec_ref[0, :, pl.ds(off, chunk)], preferred_element_type=jnp.float32)
        total += jnp.dot(blo_ref[...], lo_ref[:, pl.ds(off, chunk)], preferred_element_type=jnp.float32)
        total += jnp.dot(bhi_ref[...], hi_ref[:, pl.ds(off, chunk)], preferred_element_type=jnp.float32)
        cp_ref[:, pl.ds(pl.multiple_of(off + lanes, lanes), chunk)] = total.astype(cp_ref.dtype)
        return carry

    lax.fori_loop(0, samples // chunk, chan_step, 0)

    group = 8

    def time_step(g, acc):
        base = g * group
        windows = [
            cp_ref[:, pl.ds(pl.multiple_of((base + q) * lanes, lanes), 3 * lanes)]
            for q in range(group)
        ]
        y = jnp.dot(jnp.concatenate(windows, axis=0), tw_ref[...], preferred_element_type=jnp.float32)
        for q in range(group):
            part = y[q * chans : (q + 1) * chans]
            tp_ref[:, pl.ds(pl.multiple_of((base + q) * lanes, lanes), lanes)] = part
            acc = acc + part * part
        return acc

    acc = lax.fori_loop(0, samples // (lanes * group), time_step, jnp.zeros((chans, lanes), jnp.float32))
    power = jnp.sum(acc, axis=1, keepdims=True) / samples
    scale = lax.rsqrt(power + 1e-06)

    def white_step(i, carry):
        off = pl.multiple_of(i * chunk, chunk)
        o_ref[:, pl.ds(off, chunk)] = (tp_ref[:, pl.ds(off, chunk)] * scale).astype(o_ref.dtype)
        return carry

    lax.fori_loop(0, samples // chunk, white_step, 0)


def prepare_kernel(record, section, lo, hi, band, time_weights):
    count_steps, chans, samples = record.shape
    half = lo.shape[0]
    lanes = 128
    chunk = 512
    blo, bmid, bhi = band[:, :half], band[:, half:half + chans], band[:, half + chans:]
    full = lambda i: (0, 0)
    return pl.pallas_call(
        functools.partial(prep_body, chunk),
        grid=(1,),
        in_specs=[
            pl.BlockSpec((1, chans, samples), lambda i: (section, 0, 0)),
            pl.BlockSpec((half, samples), full),
            pl.BlockSpec((half, samples), full),
            pl.BlockSpec((chans, half), full),
            pl.BlockSpec((chans, chans), full),
            pl.BlockSpec((chans, half), full),
            pl.BlockSpec(time_weights.shape, full),
        ],
        out_specs=pl.BlockSpec((chans, samples), full),
        out_shape=jax.ShapeDtypeStruct((chans, samples), jnp.bfloat16),
        scratch_shapes=[
            pltpu.VMEM((chans, samples + 2 * lanes), jnp.bfloat16),
            pltpu.VMEM((chans, samples), jnp.float32),
        ],
        compiler_params=pltpu.CompilerParams(vmem_limit_bytes=48 * 1024 * 1024),
        cost_estimate=pl.CostEstimate(
            flops=2 * chans * samples * (chans + 2 * half + 3 * lanes),
            bytes_accessed=2 * samples * (2 * chans + 2 * half),
            transcendentals=chans,
        ),
    )(record, lo, hi, blo, bmid, bhi, time_weights)


def xor_sum(x, axis):
    count = lax.axis_size(axis)
    if count & (count - 1):
        return lax.psum(x, axis)
    step = 1
    while step < count:
        x = x + lax.ppermute(x, axis, [(i, i ^ step) for i in range(count)])
        step *= 2
    return x


def body(record, chan_taps, time_taps, sources):
    count_steps = record.shape[0]
    channels_here = record.shape[1]
    samples = record.shape[2]
    chan_table = chan_taps.astype(jnp.bfloat16)
    time_table = time_taps.astype(jnp.bfloat16)
    first_chan = lax.axis_index("chan") * channels_here
    selector = (
        (sources - first_chan)[:, :, None] == lax.iota(jnp.int32, channels_here)[None, None, :]
    ).astype(jnp.bfloat16)
    normalizer = 1.0 / math.sqrt(samples * lax.axis_size("win"))

    half = (chan_table.shape[0] - 1) // 2
    count = lax.axis_size("chan")
    band = band_matrix(chan_table, channels_here, channels_here + 2 * half)
    offset = lax.iota(jnp.int32, 384)[:, None] - 128 - lax.iota(jnp.int32, 128)[None, :]
    time_weights = tap_lookup(offset + (time_table.shape[0] - 1) // 2, time_table)

    heads = record[:, :half]
    tails = record[:, channels_here - half :]

    def halos(first, last):
        lower = lax.ppermute(tails[first:last], "chan", [(i, i + 1) for i in range(count - 1)])
        upper = lax.ppermute(heads[first:last], "chan", [(i + 1, i) for i in range(count - 1)])
        return lower, upper

    lowers, uppers = halos(0, 1)
    if count_steps > 1:
        lowers, uppers, heads, tails = lax.optimization_barrier((lowers, uppers, heads, tails))
        rest = halos(1, count_steps)
        lowers = jnp.concatenate([lowers, rest[0]], axis=0)
        uppers = jnp.concatenate([uppers, rest[1]], axis=0)

    def prepare(whole, section):
        lower, upper = lowers[section], uppers[section]
        whitened = prepare_kernel(whole, section, lower, upper, band, time_weights)
        term = jnp.dot(selector[section], whitened, preferred_element_type=jnp.float32)
        return whitened, xor_sum(term.astype(jnp.bfloat16), "chan")

    pieces = [record] * count_steps
    results = []
    pending = prepare(pieces[0], 0)
    for section in range(count_steps):
        upcoming = None
        if section + 1 < count_steps:
            upcoming = prepare(pieces[section + 1], section + 1)
        whitened, panel = pending
        if section >= 2:
            whitened, panel, results[section - 2] = lax.optimization_barrier(
                (whitened, panel, results[section - 2])
            )
        if section + 1 < count_steps:
            partial_corr = correlate_kernel(whitened, panel)
            if section + 2 < count_steps:
                pieces[section + 2], partial_corr = lax.optimization_barrier(
                    (pieces[section + 2], partial_corr)
                )
            results.append(xor_sum(partial_corr, "win"))
        else:
            half = panel.shape[0] // 2
            parts = [
                xor_sum(correlate_kernel(whitened, panel[:half]), "win"),
                xor_sum(correlate_kernel(whitened, panel[half:]), "win"),
            ]
            results.append(jnp.concatenate(parts, axis=0))
        pending = upcoming
    lags = 2 * LAG + 1
    shaped = [total.reshape(-1, CORR_ROWS, channels_here)[:, :lags] for total in results]
    return jnp.stack(shaped) * normalizer


def solution(mesh):
    in_specs = (P(None, "chan", "win"), P(), P(), P())
    out_specs = P(None, None, None, "chan")
    return jax.shard_map(body, mesh=mesh, in_specs=in_specs, out_specs=out_specs, check_vma=False)
```

```python
import functools
import math

import jax
import jax.numpy as jnp
from jax import lax
from jax.experimental import pallas as pl
from jax.experimental.pallas import tpu as pltpu
from jax.sharding import PartitionSpec as P

LAG = 64


def padded_2(cells, sides, width):
    for axis, dim in sides:
        count = lax.axis_size(axis)
        ends = count - 1
        head = lax.slice_in_dim(cells, 0, width, axis=dim)
        tail = lax.slice_in_dim(cells, cells.shape[dim] - width, cells.shape[dim], axis=dim)
        cells = jnp.concatenate(
            [
                lax.ppermute(tail, axis, [(i, (i + 1) % count) for i in range(ends)]),
                cells,
                lax.ppermute(head, axis, [((i + 1) % count, i) for i in range(ends)]),
            ],
            axis=dim,
        )
    return cells


def tap_lookup(offset, tap_table):
    count_taps = tap_table.shape[0]
    marks = offset[..., None] == lax.iota(jnp.int32, count_taps)
    picked = jnp.where(marks, tap_table.astype(jnp.float32), jnp.zeros((), jnp.float32))
    return jnp.sum(picked, axis=-1).astype(tap_table.dtype)


def band_matrix(tap_table, height, breadth):
    offset = lax.iota(jnp.int32, breadth)[None, :] - lax.iota(jnp.int32, height)[:, None]
    return tap_lookup(offset, tap_table)


def time_filter(chan_pass, tap_table):
    channels_here, samples = chan_pass.shape
    half = (tap_table.shape[0] - 1) // 2
    blocks = chan_pass.reshape(channels_here, samples // 128, 128)
    zeros_block = jnp.zeros_like(blocks[:, :1])
    earlier = jnp.concatenate([zeros_block, blocks[:, :-1]], axis=1)
    later = jnp.concatenate([blocks[:, 1:], zeros_block], axis=1)
    extended = jnp.concatenate([earlier, blocks, later], axis=2)
    offset = lax.iota(jnp.int32, 384)[:, None] - 128 - lax.iota(jnp.int32, 128)[None, :] + half
    weights = tap_lookup(offset, tap_table)
    result = jnp.einsum("cbr,rt->cbt", extended, weights, preferred_element_type=jnp.float32)
    return result.reshape(channels_here, samples)


def whiten(time_pass):
    power = jnp.mean(time_pass * time_pass, axis=-1, keepdims=True)
    return (time_pass * lax.rsqrt(power + 1e-06)).astype(jnp.bfloat16)


def corr_body(nb, w_ref, p_ref, o_ref, s_ref):
    n = pl.program_id(0)
    k_count = p_ref.shape[0]
    lanes = 128
    blocks = p_ref.shape[1] // lanes
    tail = k_count * lanes

    @pl.when(n == 0)
    def _():
        o_ref[...] = jnp.zeros_like(o_ref)
        s_ref[pl.ds(tail, 8), :] = jnp.zeros((8, s_ref.shape[1]), s_ref.dtype)

    j_idx = lax.broadcasted_iota(jnp.int32, (lanes, lanes), 0)
    r_idx = lax.broadcasted_iota(jnp.int32, (lanes, lanes), 1)
    upper = r_idx >= j_idx
    low_half = lax.broadcasted_iota(jnp.int32, (1, lanes), 1) < LAG
    base = n * nb
    for k in range(k_count):
        raw = []
        for i in range(nb + 2):
            q = base + i - 1
            start = pl.multiple_of(jnp.clip(q, 0, blocks - 1) * lanes, lanes)
            v = p_ref[pl.ds(k, 1), pl.ds(start, lanes)].astype(jnp.float32)
            if i == 0 or i == nb + 1:
                v = jnp.where((q >= 0) & (q < blocks), v, jnp.zeros_like(v))
            raw.append(pltpu.roll(v, LAG, 1))
        rolled = []
        for b in range(nb + 1):
            chunk = jnp.where(low_half, raw[b], raw[b + 1])
            if b < nb:
                s_ref[pl.ds(tail + k, 1), pl.ds(b * lanes, lanes)] = chunk.astype(s_ref.dtype)
            wide = jnp.broadcast_to(chunk, (lanes, lanes))
            rolled.append(pltpu.roll(wide, 0, 1, stride=1, stride_axis=0))
        for b in range(nb):
            piece = jnp.where(upper, rolled[b + 1], rolled[b])
            s_ref[pl.ds(k * lanes, lanes), pl.ds(b * lanes, lanes)] = piece.astype(s_ref.dtype)
    o_ref[...] += lax.dot_general(
        s_ref[...], w_ref[...], (((1,), (1,)), ((), ())),
        preferred_element_type=jnp.float32)


def correlate_kernel(whitened, panel, nb=8):
    chans, samples = whitened.shape
    k_count = panel.shape[0]
    lanes = 128
    rows = k_count * lanes + 8
    grid = samples // (nb * lanes)
    return pl.pallas_call(
        functools.partial(corr_body, nb),
        grid=(grid,),
        in_specs=[
            pl.BlockSpec((chans, nb * lanes), lambda n: (0, n)),
            pl.BlockSpec((k_count, samples), lambda n: (0, 0)),
        ],
        out_specs=pl.BlockSpec((rows, chans), lambda n: (0, 0)),
        out_shape=jax.ShapeDtypeStruct((rows, chans), jnp.float32),
        scratch_shapes=[pltpu.VMEM((rows, nb * lanes), jnp.bfloat16)],
        compiler_params=pltpu.CompilerParams(dimension_semantics=("arbitrary",)),
        cost_estimate=pl.CostEstimate(
            flops=2 * rows * samples * chans,
            bytes_accessed=2 * chans * samples + 2 * k_count * samples + 4 * rows * chans,
            transcendentals=0,
        ),
    )(whitened, panel)


def assemble(total, k_count):
    lanes = 128
    main = total[: k_count * lanes].reshape(k_count, lanes, total.shape[-1])
    last = total[k_count * lanes : k_count * lanes + k_count][:, None, :]
    return jnp.concatenate([main, last], axis=1)


def chan_filter(piece, tap_table):
    channels_here = piece.shape[0]
    half = (tap_table.shape[0] - 1) // 2
    widened = padded_2(piece, (("chan", 0),), half)
    total = jnp.dot(
        band_matrix(tap_table, channels_here, channels_here + 2 * half),
        widened,
        preferred_element_type=jnp.float32,
    )
    return total.astype(jnp.bfloat16)


def prep_body(section_chunk, rec_ref, lo_ref, hi_ref, blo_ref, bmid_ref, bhi_ref, tw_ref, o_ref, cp_ref, tp_ref):
    chans, samples = o_ref.shape
    lanes = 128
    cp_ref[:, pl.ds(0, lanes)] = jnp.zeros((chans, lanes), cp_ref.dtype)
    cp_ref[:, pl.ds(samples + lanes, lanes)] = jnp.zeros((chans, lanes), cp_ref.dtype)
    chunk = section_chunk

    def chan_step(i, carry):
        off = pl.multiple_of(i * chunk, chunk)
        total = jnp.dot(bmid_ref[...], rec_ref[0, :, pl.ds(off, chunk)], preferred_element_type=jnp.float32)
        total += jnp.dot(blo_ref[...], lo_ref[:, pl.ds(off, chunk)], preferred_element_type=jnp.float32)
        total += jnp.dot(bhi_ref[...], hi_ref[:, pl.ds(off, chunk)], preferred_element_type=jnp.float32)
        cp_ref[:, pl.ds(pl.multiple_of(off + lanes, lanes), chunk)] = total.astype(cp_ref.dtype)
        return carry

    lax.fori_loop(0, samples // chunk, chan_step, 0)

    group = 8

    def time_step(g, acc):
        base = g * group
        windows = [
            cp_ref[:, pl.ds(pl.multiple_of((base + q) * lanes, lanes), 3 * lanes)]
            for q in range(group)
        ]
        y = jnp.dot(jnp.concatenate(windows, axis=0), tw_ref[...], preferred_element_type=jnp.float32)
        for q in range(group):
            part = y[q * chans : (q + 1) * chans]
            tp_ref[:, pl.ds(pl.multiple_of((base + q) * lanes, lanes), lanes)] = part
            acc = acc + part * part
        return acc

    acc = lax.fori_loop(0, samples // (lanes * group), time_step, jnp.zeros((chans, lanes), jnp.float32))
    power = jnp.sum(acc, axis=1, keepdims=True) / samples
    scale = lax.rsqrt(power + 1e-06)

    def white_step(i, carry):
        off = pl.multiple_of(i * chunk, chunk)
        o_ref[:, pl.ds(off, chunk)] = (tp_ref[:, pl.ds(off, chunk)] * scale).astype(o_ref.dtype)
        return carry

    lax.fori_loop(0, samples // chunk, white_step, 0)


def prepare_kernel(record, section, lo, hi, band, time_weights):
    count_steps, chans, samples = record.shape
    half = lo.shape[0]
    lanes = 128
    chunk = 512
    blo, bmid, bhi = band[:, :half], band[:, half:half + chans], band[:, half + chans:]
    full = lambda i: (0, 0)
    return pl.pallas_call(
        functools.partial(prep_body, chunk),
        grid=(1,),
        in_specs=[
            pl.BlockSpec((1, chans, samples), lambda i: (section, 0, 0)),
            pl.BlockSpec((half, samples), full),
            pl.BlockSpec((half, samples), full),
            pl.BlockSpec((chans, half), full),
            pl.BlockSpec((chans, chans), full),
            pl.BlockSpec((chans, half), full),
            pl.BlockSpec(time_weights.shape, full),
        ],
        out_specs=pl.BlockSpec((chans, samples), full),
        out_shape=jax.ShapeDtypeStruct((chans, samples), jnp.bfloat16),
        scratch_shapes=[
            pltpu.VMEM((chans, samples + 2 * lanes), jnp.bfloat16),
            pltpu.VMEM((chans, samples), jnp.float32),
        ],
        compiler_params=pltpu.CompilerParams(vmem_limit_bytes=48 * 1024 * 1024),
        cost_estimate=pl.CostEstimate(
            flops=2 * chans * samples * (chans + 2 * half + 3 * lanes),
            bytes_accessed=2 * samples * (2 * chans + 2 * half),
            transcendentals=chans,
        ),
    )(record, lo, hi, blo, bmid, bhi, time_weights)


def xor_sum(x, axis):
    count = lax.axis_size(axis)
    if count & (count - 1):
        return lax.psum(x, axis)
    step = 1
    while step < count:
        x = x + lax.ppermute(x, axis, [(i, i ^ step) for i in range(count)])
        step *= 2
    return x


def body(record, chan_taps, time_taps, sources):
    count_steps = record.shape[0]
    channels_here = record.shape[1]
    samples = record.shape[2]
    chan_table = chan_taps.astype(jnp.bfloat16)
    time_table = time_taps.astype(jnp.bfloat16)
    first_chan = lax.axis_index("chan") * channels_here
    selector = (
        (sources - first_chan)[:, :, None] == lax.iota(jnp.int32, channels_here)[None, None, :]
    ).astype(jnp.bfloat16)
    normalizer = 1.0 / math.sqrt(samples * lax.axis_size("win"))

    half = (chan_table.shape[0] - 1) // 2
    count = lax.axis_size("chan")
    band = band_matrix(chan_table, channels_here, channels_here + 2 * half)
    offset = lax.iota(jnp.int32, 384)[:, None] - 128 - lax.iota(jnp.int32, 128)[None, :]
    time_weights = tap_lookup(offset + (time_table.shape[0] - 1) // 2, time_table)

    heads = record[:, :half]
    tails = record[:, channels_here - half :]
    lowers = lax.ppermute(tails, "chan", [(i, i + 1) for i in range(count - 1)])
    uppers = lax.ppermute(heads, "chan", [(i + 1, i) for i in range(count - 1)])

    def prepare(whole, section):
        lower, upper = lowers[section], uppers[section]
        whitened = prepare_kernel(whole, section, lower, upper, band, time_weights)
        term = jnp.dot(selector[section], whitened, preferred_element_type=jnp.float32)
        return whitened, xor_sum(term.astype(jnp.bfloat16), "chan")

    pieces = [record] * count_steps
    results = []
    pending = prepare(pieces[0], 0)
    for section in range(count_steps):
        upcoming = None
        if section + 1 < count_steps:
            upcoming = prepare(pieces[section + 1], section + 1)
        whitened, panel = pending
        if section >= 2:
            whitened, panel, results[section - 2] = lax.optimization_barrier(
                (whitened, panel, results[section - 2])
            )
        if section + 1 < count_steps:
            partial_corr = correlate_kernel(whitened, panel)
            if section + 2 < count_steps:
                pieces[section + 2], partial_corr = lax.optimization_barrier(
                    (pieces[section + 2], partial_corr)
                )
            results.append(assemble(xor_sum(partial_corr, "win"), panel.shape[0]))
        else:
            half = panel.shape[0] // 2
            parts = [
                assemble(xor_sum(correlate_kernel(whitened, panel[:half]), "win"), half),
                assemble(xor_sum(correlate_kernel(whitened, panel[half:]), "win"), panel.shape[0] - half),
            ]
            results.append(jnp.concatenate(parts, axis=0))
        pending = upcoming
    return jnp.stack(results) * normalizer


def solution(mesh):
    in_specs = (P(None, "chan", "win"), P(), P(), P())
    out_specs = P(None, None, None, "chan")
    return jax.shard_map(body, mesh=mesh, in_specs=in_specs, out_specs=out_specs, check_vma=False)
```

```python
import functools
import math

import jax
import jax.numpy as jnp
from jax import lax
from jax.experimental import pallas as pl
from jax.experimental.pallas import tpu as pltpu
from jax.sharding import PartitionSpec as P

LAG = 64
CORR_ROWS = 136


def padded_2(cells, sides, width):
    for axis, dim in sides:
        count = lax.axis_size(axis)
        ends = count - 1
        head = lax.slice_in_dim(cells, 0, width, axis=dim)
        tail = lax.slice_in_dim(cells, cells.shape[dim] - width, cells.shape[dim], axis=dim)
        cells = jnp.concatenate(
            [
                lax.ppermute(tail, axis, [(i, (i + 1) % count) for i in range(ends)]),
                cells,
                lax.ppermute(head, axis, [((i + 1) % count, i) for i in range(ends)]),
            ],
            axis=dim,
        )
    return cells


def tap_lookup(offset, tap_table):
    count_taps = tap_table.shape[0]
    marks = offset[..., None] == lax.iota(jnp.int32, count_taps)
    picked = jnp.where(marks, tap_table.astype(jnp.float32), jnp.zeros((), jnp.float32))
    return jnp.sum(picked, axis=-1).astype(tap_table.dtype)


def band_matrix(tap_table, height, breadth):
    offset = lax.iota(jnp.int32, breadth)[None, :] - lax.iota(jnp.int32, height)[:, None]
    return tap_lookup(offset, tap_table)


def time_filter(chan_pass, tap_table):
    channels_here, samples = chan_pass.shape
    half = (tap_table.shape[0] - 1) // 2
    blocks = chan_pass.reshape(channels_here, samples // 128, 128)
    zeros_block = jnp.zeros_like(blocks[:, :1])
    earlier = jnp.concatenate([zeros_block, blocks[:, :-1]], axis=1)
    later = jnp.concatenate([blocks[:, 1:], zeros_block], axis=1)
    extended = jnp.concatenate([earlier, blocks, later], axis=2)
    offset = lax.iota(jnp.int32, 384)[:, None] - 128 - lax.iota(jnp.int32, 128)[None, :] + half
    weights = tap_lookup(offset, tap_table)
    result = jnp.einsum("cbr,rt->cbt", extended, weights, preferred_element_type=jnp.float32)
    return result.reshape(channels_here, samples)


def whiten(time_pass):
    power = jnp.mean(time_pass * time_pass, axis=-1, keepdims=True)
    return (time_pass * lax.rsqrt(power + 1e-06)).astype(jnp.bfloat16)


def corr_body(nb, rows, w_ref, p_ref, o_ref, s_ref):
    n = pl.program_id(0)
    k_count = p_ref.shape[0]
    lanes = 128

    @pl.when(n == 0)
    def _():
        o_ref[...] = jnp.zeros_like(o_ref)

    j_idx = lax.broadcasted_iota(jnp.int32, (rows, lanes), 0)
    r_idx = lax.broadcasted_iota(jnp.int32, (rows, lanes), 1)
    upper = r_idx >= j_idx
    for k in range(k_count):
        rolled = []
        for b in range(nb + 1):
            start = pl.multiple_of((n * nb + b) * lanes, lanes)
            chunk = p_ref[pl.ds(k, 1), pl.ds(start, lanes)]
            wide = jnp.broadcast_to(chunk, (rows, lanes))
            rolled.append(pltpu.roll(wide, 0, 1, stride=1, stride_axis=0))
        for b in range(nb):
            piece = jnp.where(upper, rolled[b + 1], rolled[b])
            s_ref[pl.ds(k * rows, rows), pl.ds(b * lanes, lanes)] = piece.astype(s_ref.dtype)
    o_ref[...] += lax.dot_general(
        s_ref[...], w_ref[...], (((1,), (1,)), ((), ())),
        preferred_element_type=jnp.float32)


def correlate_kernel(whitened, panel, nb=16):
    chans, samples = whitened.shape
    k_count = panel.shape[0]
    lanes = 128
    rows = CORR_ROWS
    padded = jnp.pad(panel.astype(jnp.float32), ((0, 0), (LAG, LAG)))
    grid = samples // (nb * lanes)
    out = pl.pallas_call(
        functools.partial(corr_body, nb, rows),
        grid=(grid,),
        in_specs=[
            pl.BlockSpec((chans, nb * lanes), lambda n: (0, n)),
            pl.BlockSpec((k_count, samples + 2 * LAG), lambda n: (0, 0)),
        ],
        out_specs=pl.BlockSpec((k_count * rows, chans), lambda n: (0, 0)),
        out_shape=jax.ShapeDtypeStruct((k_count * rows, chans), jnp.float32),
        scratch_shapes=[pltpu.VMEM((k_count * rows, nb * lanes), jnp.bfloat16)],
        compiler_params=pltpu.CompilerParams(dimension_semantics=("arbitrary",)),
        cost_estimate=pl.CostEstimate(
            flops=2 * k_count * rows * samples * chans,
            bytes_accessed=2 * chans * samples + 4 * k_count * (samples + rows * chans),
            transcendentals=0,
        ),
    )(whitened, padded)
    return out


def chan_filter(piece, tap_table):
    channels_here = piece.shape[0]
    half = (tap_table.shape[0] - 1) // 2
    widened = padded_2(piece, (("chan", 0),), half)
    total = jnp.dot(
        band_matrix(tap_table, channels_here, channels_here + 2 * half),
        widened,
        preferred_element_type=jnp.float32,
    )
    return total.astype(jnp.bfloat16)


def prep_body(section_chunk, rec_ref, lo_ref, hi_ref, blo_ref, bmid_ref, bhi_ref, tw_ref, o_ref, cp_ref, tp_ref):
    chans, samples = o_ref.shape
    lanes = 128
    cp_ref[:, pl.ds(0, lanes)] = jnp.zeros((chans, lanes), cp_ref.dtype)
    cp_ref[:, pl.ds(samples + lanes, lanes)] = jnp.zeros((chans, lanes), cp_ref.dtype)
    chunk = section_chunk

    def chan_step(i, carry):
        off = pl.multiple_of(i * chunk, chunk)
        total = jnp.dot(bmid_ref[...], rec_ref[0, :, pl.ds(off, chunk)], preferred_element_type=jnp.float32)
        total += jnp.dot(blo_ref[...], lo_ref[:, pl.ds(off, chunk)], preferred_element_type=jnp.float32)
        total += jnp.dot(bhi_ref[...], hi_ref[:, pl.ds(off, chunk)], preferred_element_type=jnp.float32)
        cp_ref[:, pl.ds(pl.multiple_of(off + lanes, lanes), chunk)] = total.astype(cp_ref.dtype)
        return carry

    lax.fori_loop(0, samples // chunk, chan_step, 0)

    group = 8

    def time_step(g, acc):
        base = g * group
        windows = [
            cp_ref[:, pl.ds(pl.multiple_of((base + q) * lanes, lanes), 3 * lanes)]
            for q in range(group)
        ]
        y = jnp.dot(jnp.concatenate(windows, axis=0), tw_ref[...], preferred_element_type=jnp.float32)
        for q in range(group):
            part = y[q * chans : (q + 1) * chans]
            tp_ref[:, pl.ds(pl.multiple_of((base + q) * lanes, lanes), lanes)] = part
            acc = acc + part * part
        return acc

    acc = lax.fori_loop(0, samples // (lanes * group), time_step, jnp.zeros((chans, lanes), jnp.float32))
    power = jnp.sum(acc, axis=1, keepdims=True) / samples
    scale = lax.rsqrt(power + 1e-06)

    def white_step(i, carry):
        off = pl.multiple_of(i * chunk, chunk)
        o_ref[:, pl.ds(off, chunk)] = (tp_ref[:, pl.ds(off, chunk)] * scale).astype(o_ref.dtype)
        return carry

    lax.fori_loop(0, samples // chunk, white_step, 0)


def prepare_kernel(record, section, lo, hi, band, time_weights):
    count_steps, chans, samples = record.shape
    half = lo.shape[0]
    lanes = 128
    chunk = 512
    blo, bmid, bhi = band[:, :half], band[:, half:half + chans], band[:, half + chans:]
    full = lambda i: (0, 0)
    return pl.pallas_call(
        functools.partial(prep_body, chunk),
        grid=(1,),
        in_specs=[
            pl.BlockSpec((1, chans, samples), lambda i: (section, 0, 0)),
            pl.BlockSpec((half, samples), full),
            pl.BlockSpec((half, samples), full),
            pl.BlockSpec((chans, half), full),
            pl.BlockSpec((chans, chans), full),
            pl.BlockSpec((chans, half), full),
            pl.BlockSpec(time_weights.shape, full),
        ],
        out_specs=pl.BlockSpec((chans, samples), full),
        out_shape=jax.ShapeDtypeStruct((chans, samples), jnp.bfloat16),
        scratch_shapes=[
            pltpu.VMEM((chans, samples + 2 * lanes), jnp.bfloat16),
            pltpu.VMEM((chans, samples), jnp.float32),
        ],
        compiler_params=pltpu.CompilerParams(vmem_limit_bytes=48 * 1024 * 1024),
        cost_estimate=pl.CostEstimate(
            flops=2 * chans * samples * (chans + 2 * half + 3 * lanes),
            bytes_accessed=2 * samples * (2 * chans + 2 * half),
            transcendentals=chans,
        ),
    )(record, lo, hi, blo, bmid, bhi, time_weights)


def xor_sum(x, axis):
    count = lax.axis_size(axis)
    if count & (count - 1):
        return lax.psum(x, axis)
    step = 1
    while step < count:
        x = x + lax.ppermute(x, axis, [(i, i ^ step) for i in range(count)])
        step *= 2
    return x


def body(record, chan_taps, time_taps, sources):
    count_steps = record.shape[0]
    channels_here = record.shape[1]
    samples = record.shape[2]
    chan_table = chan_taps.astype(jnp.bfloat16)
    time_table = time_taps.astype(jnp.bfloat16)
    first_chan = lax.axis_index("chan") * channels_here
    selector = (
        (sources - first_chan)[:, :, None] == lax.iota(jnp.int32, channels_here)[None, None, :]
    ).astype(jnp.bfloat16)
    normalizer = 1.0 / math.sqrt(samples * lax.axis_size("win"))

    half = (chan_table.shape[0] - 1) // 2
    count = lax.axis_size("chan")
    band = band_matrix(chan_table, channels_here, channels_here + 2 * half)
    offset = lax.iota(jnp.int32, 384)[:, None] - 128 - lax.iota(jnp.int32, 128)[None, :]
    time_weights = tap_lookup(offset + (time_table.shape[0] - 1) // 2, time_table)

    heads = record[:, :half]
    tails = record[:, channels_here - half :]
    lowers = lax.ppermute(tails, "chan", [(i, i + 1) for i in range(count - 1)])
    uppers = lax.ppermute(heads, "chan", [(i + 1, i) for i in range(count - 1)])

    def prepare(whole, section):
        lower, upper = lowers[section], uppers[section]
        whitened = prepare_kernel(whole, section, lower, upper, band, time_weights)
        term = jnp.dot(selector[section], whitened, preferred_element_type=jnp.float32)
        return whitened, xor_sum(term.astype(jnp.bfloat16), "chan")

    pieces = [record] * count_steps
    results = []
    pending = prepare(pieces[0], 0)
    for section in range(count_steps):
        upcoming = None
        if section + 1 < count_steps:
            upcoming = prepare(pieces[section + 1], section + 1)
        whitened, panel = pending
        if section >= 2:
            whitened, panel, results[section - 2] = lax.optimization_barrier(
                (whitened, panel, results[section - 2])
            )
        if section + 1 < count_steps:
            partial_corr = correlate_kernel(whitened, panel)
            if section + 2 < count_steps:
                pieces[section + 2], partial_corr = lax.optimization_barrier(
                    (pieces[section + 2], partial_corr)
                )
            results.append(xor_sum(partial_corr, "win"))
        else:
            half = panel.shape[0] // 2
            parts = [
                xor_sum(correlate_kernel(whitened, panel[:half]), "win"),
                xor_sum(correlate_kernel(whitened, panel[half:]), "win"),
            ]
            results.append(jnp.concatenate(parts, axis=0))
        pending = upcoming
    lags = 2 * LAG + 1
    shaped = [total.reshape(-1, CORR_ROWS, channels_here)[:, :lags] for total in results]
    return jnp.stack(shaped) * normalizer


def solution(mesh):
    in_specs = (P(None, "chan", "win"), P(), P(), P())
    out_specs = P(None, None, None, "chan")
    return jax.shard_map(body, mesh=mesh, in_specs=in_specs, out_specs=out_specs, check_vma=False)
```

```python
import functools
import math

import jax
import jax.numpy as jnp
from jax import lax
from jax.experimental import pallas as pl
from jax.experimental.pallas import tpu as pltpu
from jax.sharding import PartitionSpec as P

LAG = 64
CORR_ROWS = 136


def padded_2(cells, sides, width):
    for axis, dim in sides:
        count = lax.axis_size(axis)
        ends = count - 1
        head = lax.slice_in_dim(cells, 0, width, axis=dim)
        tail = lax.slice_in_dim(cells, cells.shape[dim] - width, cells.shape[dim], axis=dim)
        cells = jnp.concatenate(
            [
                lax.ppermute(tail, axis, [(i, (i + 1) % count) for i in range(ends)]),
                cells,
                lax.ppermute(head, axis, [((i + 1) % count, i) for i in range(ends)]),
            ],
            axis=dim,
        )
    return cells


def tap_lookup(offset, tap_table):
    count_taps = tap_table.shape[0]
    marks = offset[..., None] == lax.iota(jnp.int32, count_taps)
    picked = jnp.where(marks, tap_table.astype(jnp.float32), jnp.zeros((), jnp.float32))
    return jnp.sum(picked, axis=-1).astype(tap_table.dtype)


def band_matrix(tap_table, height, breadth):
    offset = lax.iota(jnp.int32, breadth)[None, :] - lax.iota(jnp.int32, height)[:, None]
    return tap_lookup(offset, tap_table)


def time_filter(chan_pass, tap_table):
    channels_here, samples = chan_pass.shape
    half = (tap_table.shape[0] - 1) // 2
    blocks = chan_pass.reshape(channels_here, samples // 128, 128)
    zeros_block = jnp.zeros_like(blocks[:, :1])
    earlier = jnp.concatenate([zeros_block, blocks[:, :-1]], axis=1)
    later = jnp.concatenate([blocks[:, 1:], zeros_block], axis=1)
    extended = jnp.concatenate([earlier, blocks, later], axis=2)
    offset = lax.iota(jnp.int32, 384)[:, None] - 128 - lax.iota(jnp.int32, 128)[None, :] + half
    weights = tap_lookup(offset, tap_table)
    result = jnp.einsum("cbr,rt->cbt", extended, weights, preferred_element_type=jnp.float32)
    return result.reshape(channels_here, samples)


def whiten(time_pass):
    power = jnp.mean(time_pass * time_pass, axis=-1, keepdims=True)
    return (time_pass * lax.rsqrt(power + 1e-06)).astype(jnp.bfloat16)


def corr_body(nb, rows, w_ref, p_ref, o_ref, s_ref):
    n = pl.program_id(0)
    k_count = p_ref.shape[0]
    lanes = 128

    @pl.when(n == 0)
    def _():
        o_ref[...] = jnp.zeros_like(o_ref)

    j_idx = lax.broadcasted_iota(jnp.int32, (rows, lanes), 0)
    r_idx = lax.broadcasted_iota(jnp.int32, (rows, lanes), 1)
    upper = r_idx >= j_idx
    for k in range(k_count):
        rolled = []
        for b in range(nb + 1):
            start = pl.multiple_of((n * nb + b) * lanes, lanes)
            chunk = p_ref[pl.ds(k, 1), pl.ds(start, lanes)]
            wide = jnp.broadcast_to(chunk, (rows, lanes))
            rolled.append(pltpu.roll(wide, 0, 1, stride=1, stride_axis=0))
        for b in range(nb):
            piece = jnp.where(upper, rolled[b + 1], rolled[b])
            s_ref[pl.ds(k * rows, rows), pl.ds(b * lanes, lanes)] = piece.astype(s_ref.dtype)
    o_ref[...] += lax.dot_general(
        s_ref[...], w_ref[...], (((1,), (1,)), ((), ())),
        preferred_element_type=jnp.float32)


def correlate_kernel(whitened, panel, nb=32):
    chans, samples = whitened.shape
    k_count = panel.shape[0]
    lanes = 128
    rows = CORR_ROWS
    padded = jnp.pad(panel.astype(jnp.float32), ((0, 0), (LAG, LAG)))
    grid = samples // (nb * lanes)
    out = pl.pallas_call(
        functools.partial(corr_body, nb, rows),
        grid=(grid,),
        in_specs=[
            pl.BlockSpec((chans, nb * lanes), lambda n: (0, n)),
            pl.BlockSpec((k_count, samples + 2 * LAG), lambda n: (0, 0)),
        ],
        out_specs=pl.BlockSpec((k_count * rows, chans), lambda n: (0, 0)),
        out_shape=jax.ShapeDtypeStruct((k_count * rows, chans), jnp.float32),
        scratch_shapes=[pltpu.VMEM((k_count * rows, nb * lanes), jnp.bfloat16)],
        compiler_params=pltpu.CompilerParams(dimension_semantics=("arbitrary",)),
        cost_estimate=pl.CostEstimate(
            flops=2 * k_count * rows * samples * chans,
            bytes_accessed=2 * chans * samples + 4 * k_count * (samples + rows * chans),
            transcendentals=0,
        ),
    )(whitened, padded)
    return out


def chan_filter(piece, tap_table):
    channels_here = piece.shape[0]
    half = (tap_table.shape[0] - 1) // 2
    widened = padded_2(piece, (("chan", 0),), half)
    total = jnp.dot(
        band_matrix(tap_table, channels_here, channels_here + 2 * half),
        widened,
        preferred_element_type=jnp.float32,
    )
    return total.astype(jnp.bfloat16)


def prep_body(section_chunk, rec_ref, lo_ref, hi_ref, blo_ref, bmid_ref, bhi_ref, tw_ref, o_ref, cp_ref, tp_ref):
    chans, samples = o_ref.shape
    lanes = 128
    cp_ref[:, pl.ds(0, lanes)] = jnp.zeros((chans, lanes), cp_ref.dtype)
    cp_ref[:, pl.ds(samples + lanes, lanes)] = jnp.zeros((chans, lanes), cp_ref.dtype)
    chunk = section_chunk

    def chan_step(i, carry):
        off = pl.multiple_of(i * chunk, chunk)
        total = jnp.dot(bmid_ref[...], rec_ref[0, :, pl.ds(off, chunk)], preferred_element_type=jnp.float32)
        total += jnp.dot(blo_ref[...], lo_ref[:, pl.ds(off, chunk)], preferred_element_type=jnp.float32)
        total += jnp.dot(bhi_ref[...], hi_ref[:, pl.ds(off, chunk)], preferred_element_type=jnp.float32)
        cp_ref[:, pl.ds(pl.multiple_of(off + lanes, lanes), chunk)] = total.astype(cp_ref.dtype)
        return carry

    lax.fori_loop(0, samples // chunk, chan_step, 0)

    group = 8

    def time_step(g, acc):
        base = g * group
        windows = [
            cp_ref[:, pl.ds(pl.multiple_of((base + q) * lanes, lanes), 3 * lanes)]
            for q in range(group)
        ]
        y = jnp.dot(jnp.concatenate(windows, axis=0), tw_ref[...], preferred_element_type=jnp.float32)
        for q in range(group):
            part = y[q * chans : (q + 1) * chans]
            tp_ref[:, pl.ds(pl.multiple_of((base + q) * lanes, lanes), lanes)] = part
            acc = acc + part * part
        return acc

    acc = lax.fori_loop(0, samples // (lanes * group), time_step, jnp.zeros((chans, lanes), jnp.float32))
    power = jnp.sum(acc, axis=1, keepdims=True) / samples
    scale = lax.rsqrt(power + 1e-06)

    def white_step(i, carry):
        off = pl.multiple_of(i * chunk, chunk)
        o_ref[:, pl.ds(off, chunk)] = (tp_ref[:, pl.ds(off, chunk)] * scale).astype(o_ref.dtype)
        return carry

    lax.fori_loop(0, samples // chunk, white_step, 0)


def prepare_kernel(record, section, lo, hi, band, time_weights):
    count_steps, chans, samples = record.shape
    half = lo.shape[0]
    lanes = 128
    chunk = 512
    blo, bmid, bhi = band[:, :half], band[:, half:half + chans], band[:, half + chans:]
    full = lambda i: (0, 0)
    return pl.pallas_call(
        functools.partial(prep_body, chunk),
        grid=(1,),
        in_specs=[
            pl.BlockSpec((1, chans, samples), lambda i: (section, 0, 0)),
            pl.BlockSpec((half, samples), full),
            pl.BlockSpec((half, samples), full),
            pl.BlockSpec((chans, half), full),
            pl.BlockSpec((chans, chans), full),
            pl.BlockSpec((chans, half), full),
            pl.BlockSpec(time_weights.shape, full),
        ],
        out_specs=pl.BlockSpec((chans, samples), full),
        out_shape=jax.ShapeDtypeStruct((chans, samples), jnp.bfloat16),
        scratch_shapes=[
            pltpu.VMEM((chans, samples + 2 * lanes), jnp.bfloat16),
            pltpu.VMEM((chans, samples), jnp.float32),
        ],
        compiler_params=pltpu.CompilerParams(vmem_limit_bytes=48 * 1024 * 1024),
        cost_estimate=pl.CostEstimate(
            flops=2 * chans * samples * (chans + 2 * half + 3 * lanes),
            bytes_accessed=2 * samples * (2 * chans + 2 * half),
            transcendentals=chans,
        ),
    )(record, lo, hi, blo, bmid, bhi, time_weights)


def xor_sum(x, axis):
    count = lax.axis_size(axis)
    if count & (count - 1):
        return lax.psum(x, axis)
    step = 1
    while step < count:
        x = x + lax.ppermute(x, axis, [(i, i ^ step) for i in range(count)])
        step *= 2
    return x


def body(record, chan_taps, time_taps, sources):
    count_steps = record.shape[0]
    channels_here = record.shape[1]
    samples = record.shape[2]
    chan_table = chan_taps.astype(jnp.bfloat16)
    time_table = time_taps.astype(jnp.bfloat16)
    first_chan = lax.axis_index("chan") * channels_here
    selector = (
        (sources - first_chan)[:, :, None] == lax.iota(jnp.int32, channels_here)[None, None, :]
    ).astype(jnp.bfloat16)
    normalizer = 1.0 / math.sqrt(samples * lax.axis_size("win"))

    half = (chan_table.shape[0] - 1) // 2
    count = lax.axis_size("chan")
    band = band_matrix(chan_table, channels_here, channels_here + 2 * half)
    offset = lax.iota(jnp.int32, 384)[:, None] - 128 - lax.iota(jnp.int32, 128)[None, :]
    time_weights = tap_lookup(offset + (time_table.shape[0] - 1) // 2, time_table)

    heads = record[:, :half]
    tails = record[:, channels_here - half :]
    lowers = lax.ppermute(tails, "chan", [(i, i + 1) for i in range(count - 1)])
    uppers = lax.ppermute(heads, "chan", [(i + 1, i) for i in range(count - 1)])

    def prepare(whole, section):
        lower, upper = lowers[section], uppers[section]
        whitened = prepare_kernel(whole, section, lower, upper, band, time_weights)
        term = jnp.dot(selector[section], whitened, preferred_element_type=jnp.float32)
        return whitened, xor_sum(term.astype(jnp.bfloat16), "chan")

    pieces = [record] * count_steps
    results = []
    pending = prepare(pieces[0], 0)
    for section in range(count_steps):
        upcoming = None
        if section + 1 < count_steps:
            upcoming = prepare(pieces[section + 1], section + 1)
        whitened, panel = pending
        if section >= 2:
            whitened, panel, results[section - 2] = lax.optimization_barrier(
                (whitened, panel, results[section - 2])
            )
        if section + 1 < count_steps:
            partial_corr = correlate_kernel(whitened, panel)
            if section + 2 < count_steps:
                pieces[section + 2], partial_corr = lax.optimization_barrier(
                    (pieces[section + 2], partial_corr)
                )
            results.append(xor_sum(partial_corr, "win"))
        else:
            half = panel.shape[0] // 2
            parts = [
                xor_sum(correlate_kernel(whitened, panel[:half]), "win"),
                xor_sum(correlate_kernel(whitened, panel[half:]), "win"),
            ]
            results.append(jnp.concatenate(parts, axis=0))
        pending = upcoming
    lags = 2 * LAG + 1
    shaped = [total.reshape(-1, CORR_ROWS, channels_here)[:, :lags] for total in results]
    return jnp.stack(shaped) * normalizer


def solution(mesh):
    in_specs = (P(None, "chan", "win"), P(), P(), P())
    out_specs = P(None, None, None, "chan")
    return jax.shard_map(body, mesh=mesh, in_specs=in_specs, out_specs=out_specs, check_vma=False)
```

```python
import functools
import math

import jax
import jax.numpy as jnp
from jax import lax
from jax.experimental import pallas as pl
from jax.experimental.pallas import tpu as pltpu
from jax.sharding import PartitionSpec as P

LAG = 64
CORR_ROWS = 136


def padded_2(cells, sides, width):
    for axis, dim in sides:
        count = lax.axis_size(axis)
        ends = count - 1
        head = lax.slice_in_dim(cells, 0, width, axis=dim)
        tail = lax.slice_in_dim(cells, cells.shape[dim] - width, cells.shape[dim], axis=dim)
        cells = jnp.concatenate(
            [
                lax.ppermute(tail, axis, [(i, (i + 1) % count) for i in range(ends)]),
                cells,
                lax.ppermute(head, axis, [((i + 1) % count, i) for i in range(ends)]),
            ],
            axis=dim,
        )
    return cells


def tap_lookup(offset, tap_table):
    count_taps = tap_table.shape[0]
    marks = offset[..., None] == lax.iota(jnp.int32, count_taps)
    picked = jnp.where(marks, tap_table.astype(jnp.float32), jnp.zeros((), jnp.float32))
    return jnp.sum(picked, axis=-1).astype(tap_table.dtype)


def band_matrix(tap_table, height, breadth):
    offset = lax.iota(jnp.int32, breadth)[None, :] - lax.iota(jnp.int32, height)[:, None]
    return tap_lookup(offset, tap_table)


def time_filter(chan_pass, tap_table):
    channels_here, samples = chan_pass.shape
    half = (tap_table.shape[0] - 1) // 2
    blocks = chan_pass.reshape(channels_here, samples // 128, 128)
    zeros_block = jnp.zeros_like(blocks[:, :1])
    earlier = jnp.concatenate([zeros_block, blocks[:, :-1]], axis=1)
    later = jnp.concatenate([blocks[:, 1:], zeros_block], axis=1)
    extended = jnp.concatenate([earlier, blocks, later], axis=2)
    offset = lax.iota(jnp.int32, 384)[:, None] - 128 - lax.iota(jnp.int32, 128)[None, :] + half
    weights = tap_lookup(offset, tap_table)
    result = jnp.einsum("cbr,rt->cbt", extended, weights, preferred_element_type=jnp.float32)
    return result.reshape(channels_here, samples)


def whiten(time_pass):
    power = jnp.mean(time_pass * time_pass, axis=-1, keepdims=True)
    return (time_pass * lax.rsqrt(power + 1e-06)).astype(jnp.bfloat16)


def corr_body(nb, rows, w_ref, p_ref, o_ref, s_ref):
    n = pl.program_id(0)
    k_count = p_ref.shape[0]
    lanes = 128

    @pl.when(n == 0)
    def _():
        o_ref[...] = jnp.zeros_like(o_ref)

    j_idx = lax.broadcasted_iota(jnp.int32, (rows, lanes), 0)
    r_idx = lax.broadcasted_iota(jnp.int32, (rows, lanes), 1)
    upper = r_idx >= j_idx
    for k in range(k_count):
        rolled = []
        for b in range(nb + 1):
            start = pl.multiple_of((n * nb + b) * lanes, lanes)
            chunk = p_ref[pl.ds(k, 1), pl.ds(start, lanes)]
            wide = jnp.broadcast_to(chunk, (rows, lanes))
            rolled.append(pltpu.roll(wide, 0, 1, stride=1, stride_axis=0))
        for b in range(nb):
            piece = jnp.where(upper, rolled[b + 1], rolled[b])
            s_ref[pl.ds(k * rows, rows), pl.ds(b * lanes, lanes)] = piece.astype(s_ref.dtype)
    o_ref[...] += lax.dot_general(
        s_ref[...], w_ref[...], (((1,), (1,)), ((), ())),
        preferred_element_type=jnp.float32)


def correlate_kernel(whitened, panel, nb=32):
    chans, samples = whitened.shape
    k_count = panel.shape[0]
    lanes = 128
    rows = CORR_ROWS
    padded = jnp.pad(panel.astype(jnp.float32), ((0, 0), (LAG, LAG)))
    grid = samples // (nb * lanes)
    out = pl.pallas_call(
        functools.partial(corr_body, nb, rows),
        grid=(grid,),
        in_specs=[
            pl.BlockSpec((chans, nb * lanes), lambda n: (0, n)),
            pl.BlockSpec((k_count, samples + 2 * LAG), lambda n: (0, 0)),
        ],
        out_specs=pl.BlockSpec((k_count * rows, chans), lambda n: (0, 0)),
        out_shape=jax.ShapeDtypeStruct((k_count * rows, chans), jnp.float32),
        scratch_shapes=[pltpu.VMEM((k_count * rows, nb * lanes), jnp.bfloat16)],
        compiler_params=pltpu.CompilerParams(dimension_semantics=("arbitrary",)),
        cost_estimate=pl.CostEstimate(
            flops=2 * k_count * rows * samples * chans,
            bytes_accessed=2 * chans * samples + 4 * k_count * (samples + rows * chans),
            transcendentals=0,
        ),
    )(whitened, padded)
    return out


def chan_filter(piece, tap_table):
    channels_here = piece.shape[0]
    half = (tap_table.shape[0] - 1) // 2
    widened = padded_2(piece, (("chan", 0),), half)
    total = jnp.dot(
        band_matrix(tap_table, channels_here, channels_here + 2 * half),
        widened,
        preferred_element_type=jnp.float32,
    )
    return total.astype(jnp.bfloat16)


def prep_body(section_chunk, rec_ref, lo_ref, hi_ref, blo_ref, bmid_ref, bhi_ref, tw_ref, o_ref, cp_ref, tp_ref):
    chans, samples = o_ref.shape
    lanes = 128
    cp_ref[:, pl.ds(0, lanes)] = jnp.zeros((chans, lanes), cp_ref.dtype)
    cp_ref[:, pl.ds(samples + lanes, lanes)] = jnp.zeros((chans, lanes), cp_ref.dtype)
    chunk = section_chunk

    def chan_step(i, carry):
        off = pl.multiple_of(i * chunk, chunk)
        total = jnp.dot(bmid_ref[...], rec_ref[0, :, pl.ds(off, chunk)], preferred_element_type=jnp.float32)
        total += jnp.dot(blo_ref[...], lo_ref[:, pl.ds(off, chunk)], preferred_element_type=jnp.float32)
        total += jnp.dot(bhi_ref[...], hi_ref[:, pl.ds(off, chunk)], preferred_element_type=jnp.float32)
        cp_ref[:, pl.ds(pl.multiple_of(off + lanes, lanes), chunk)] = total.astype(cp_ref.dtype)
        return carry

    lax.fori_loop(0, samples // chunk, chan_step, 0)

    group = 16

    def time_step(g, acc):
        base = g * group
        windows = [
            cp_ref[:, pl.ds(pl.multiple_of((base + q) * lanes, lanes), 3 * lanes)]
            for q in range(group)
        ]
        y = jnp.dot(jnp.concatenate(windows, axis=0), tw_ref[...], preferred_element_type=jnp.float32)
        for q in range(group):
            part = y[q * chans : (q + 1) * chans]
            tp_ref[:, pl.ds(pl.multiple_of((base + q) * lanes, lanes), lanes)] = part
            acc = acc + part * part
        return acc

    acc = lax.fori_loop(0, samples // (lanes * group), time_step, jnp.zeros((chans, lanes), jnp.float32))
    power = jnp.sum(acc, axis=1, keepdims=True) / samples
    scale = lax.rsqrt(power + 1e-06)

    def white_step(i, carry):
        off = pl.multiple_of(i * chunk, chunk)
        o_ref[:, pl.ds(off, chunk)] = (tp_ref[:, pl.ds(off, chunk)] * scale).astype(o_ref.dtype)
        return carry

    lax.fori_loop(0, samples // chunk, white_step, 0)


def prepare_kernel(record, section, lo, hi, band, time_weights):
    count_steps, chans, samples = record.shape
    half = lo.shape[0]
    lanes = 128
    chunk = 1024
    blo, bmid, bhi = band[:, :half], band[:, half:half + chans], band[:, half + chans:]
    full = lambda i: (0, 0)
    return pl.pallas_call(
        functools.partial(prep_body, chunk),
        grid=(1,),
        in_specs=[
            pl.BlockSpec((1, chans, samples), lambda i: (section, 0, 0)),
            pl.BlockSpec((half, samples), full),
            pl.BlockSpec((half, samples), full),
            pl.BlockSpec((chans, half), full),
            pl.BlockSpec((chans, chans), full),
            pl.BlockSpec((chans, half), full),
            pl.BlockSpec(time_weights.shape, full),
        ],
        out_specs=pl.BlockSpec((chans, samples), full),
        out_shape=jax.ShapeDtypeStruct((chans, samples), jnp.bfloat16),
        scratch_shapes=[
            pltpu.VMEM((chans, samples + 2 * lanes), jnp.bfloat16),
            pltpu.VMEM((chans, samples), jnp.float32),
        ],
        compiler_params=pltpu.CompilerParams(vmem_limit_bytes=48 * 1024 * 1024),
        cost_estimate=pl.CostEstimate(
            flops=2 * chans * samples * (chans + 2 * half + 3 * lanes),
            bytes_accessed=2 * samples * (2 * chans + 2 * half),
            transcendentals=chans,
        ),
    )(record, lo, hi, blo, bmid, bhi, time_weights)


def xor_sum(x, axis):
    count = lax.axis_size(axis)
    if count & (count - 1):
        return lax.psum(x, axis)
    step = 1
    while step < count:
        x = x + lax.ppermute(x, axis, [(i, i ^ step) for i in range(count)])
        step *= 2
    return x


def body(record, chan_taps, time_taps, sources):
    count_steps = record.shape[0]
    channels_here = record.shape[1]
    samples = record.shape[2]
    chan_table = chan_taps.astype(jnp.bfloat16)
    time_table = time_taps.astype(jnp.bfloat16)
    first_chan = lax.axis_index("chan") * channels_here
    selector = (
        (sources - first_chan)[:, :, None] == lax.iota(jnp.int32, channels_here)[None, None, :]
    ).astype(jnp.bfloat16)
    normalizer = 1.0 / math.sqrt(samples * lax.axis_size("win"))

    half = (chan_table.shape[0] - 1) // 2
    count = lax.axis_size("chan")
    band = band_matrix(chan_table, channels_here, channels_here + 2 * half)
    offset = lax.iota(jnp.int32, 384)[:, None] - 128 - lax.iota(jnp.int32, 128)[None, :]
    time_weights = tap_lookup(offset + (time_table.shape[0] - 1) // 2, time_table)

    heads = record[:, :half]
    tails = record[:, channels_here - half :]
    lowers = lax.ppermute(tails, "chan", [(i, i + 1) for i in range(count - 1)])
    uppers = lax.ppermute(heads, "chan", [(i + 1, i) for i in range(count - 1)])

    def prepare(whole, section):
        lower, upper = lowers[section], uppers[section]
        whitened = prepare_kernel(whole, section, lower, upper, band, time_weights)
        term = jnp.dot(selector[section], whitened, preferred_element_type=jnp.float32)
        return whitened, xor_sum(term.astype(jnp.bfloat16), "chan")

    pieces = [record] * count_steps
    results = []
    pending = prepare(pieces[0], 0)
    for section in range(count_steps):
        upcoming = None
        if section + 1 < count_steps:
            upcoming = prepare(pieces[section + 1], section + 1)
        whitened, panel = pending
        if section >= 2:
            whitened, panel, results[section - 2] = lax.optimization_barrier(
                (whitened, panel, results[section - 2])
            )
        if section + 1 < count_steps:
            partial_corr = correlate_kernel(whitened, panel)
            if section + 2 < count_steps:
                pieces[section + 2], partial_corr = lax.optimization_barrier(
                    (pieces[section + 2], partial_corr)
                )
            results.append(xor_sum(partial_corr, "win"))
        else:
            half = panel.shape[0] // 2
            parts = [
                xor_sum(correlate_kernel(whitened, panel[:half]), "win"),
                xor_sum(correlate_kernel(whitened, panel[half:]), "win"),
            ]
            results.append(jnp.concatenate(parts, axis=0))
        pending = upcoming
    lags = 2 * LAG + 1
    shaped = [total.reshape(-1, CORR_ROWS, channels_here)[:, :lags] for total in results]
    return jnp.stack(shaped) * normalizer


def solution(mesh):
    in_specs = (P(None, "chan", "win"), P(), P(), P())
    out_specs = P(None, None, None, "chan")
    return jax.shard_map(body, mesh=mesh, in_specs=in_specs, out_specs=out_specs, check_vma=False)
```

```python
import functools
import math

import jax
import jax.numpy as jnp
from jax import lax
from jax.experimental import pallas as pl
from jax.experimental.pallas import tpu as pltpu
from jax.sharding import PartitionSpec as P

LAG = 64
CORR_ROWS = 136


def padded_2(cells, sides, width):
    for axis, dim in sides:
        count = lax.axis_size(axis)
        ends = count - 1
        head = lax.slice_in_dim(cells, 0, width, axis=dim)
        tail = lax.slice_in_dim(cells, cells.shape[dim] - width, cells.shape[dim], axis=dim)
        cells = jnp.concatenate(
            [
                lax.ppermute(tail, axis, [(i, (i + 1) % count) for i in range(ends)]),
                cells,
                lax.ppermute(head, axis, [((i + 1) % count, i) for i in range(ends)]),
            ],
            axis=dim,
        )
    return cells


def tap_lookup(offset, tap_table):
    count_taps = tap_table.shape[0]
    marks = offset[..., None] == lax.iota(jnp.int32, count_taps)
    picked = jnp.where(marks, tap_table.astype(jnp.float32), jnp.zeros((), jnp.float32))
    return jnp.sum(picked, axis=-1).astype(tap_table.dtype)


def band_matrix(tap_table, height, breadth):
    offset = lax.iota(jnp.int32, breadth)[None, :] - lax.iota(jnp.int32, height)[:, None]
    return tap_lookup(offset, tap_table)


def time_filter(chan_pass, tap_table):
    channels_here, samples = chan_pass.shape
    half = (tap_table.shape[0] - 1) // 2
    blocks = chan_pass.reshape(channels_here, samples // 128, 128)
    zeros_block = jnp.zeros_like(blocks[:, :1])
    earlier = jnp.concatenate([zeros_block, blocks[:, :-1]], axis=1)
    later = jnp.concatenate([blocks[:, 1:], zeros_block], axis=1)
    extended = jnp.concatenate([earlier, blocks, later], axis=2)
    offset = lax.iota(jnp.int32, 384)[:, None] - 128 - lax.iota(jnp.int32, 128)[None, :] + half
    weights = tap_lookup(offset, tap_table)
    result = jnp.einsum("cbr,rt->cbt", extended, weights, preferred_element_type=jnp.float32)
    return result.reshape(channels_here, samples)


def whiten(time_pass):
    power = jnp.mean(time_pass * time_pass, axis=-1, keepdims=True)
    return (time_pass * lax.rsqrt(power + 1e-06)).astype(jnp.bfloat16)


def corr_body(nb, rows, w_ref, p_ref, o_ref, s_ref):
    n = pl.program_id(0)
    k_count = p_ref.shape[0]
    lanes = 128

    @pl.when(n == 0)
    def _():
        o_ref[...] = jnp.zeros_like(o_ref)

    j_idx = lax.broadcasted_iota(jnp.int32, (rows, lanes), 0)
    r_idx = lax.broadcasted_iota(jnp.int32, (rows, lanes), 1)
    upper = r_idx >= j_idx
    for k in range(k_count):
        rolled = []
        for b in range(nb + 1):
            start = pl.multiple_of((n * nb + b) * lanes, lanes)
            chunk = p_ref[pl.ds(k, 1), pl.ds(start, lanes)]
            wide = jnp.broadcast_to(chunk, (rows, lanes))
            rolled.append(pltpu.roll(wide, 0, 1, stride=1, stride_axis=0))
        for b in range(nb):
            piece = jnp.where(upper, rolled[b + 1], rolled[b])
            s_ref[pl.ds(k * rows, rows), pl.ds(b * lanes, lanes)] = piece.astype(s_ref.dtype)
    o_ref[...] += lax.dot_general(
        s_ref[...], w_ref[...], (((1,), (1,)), ((), ())),
        preferred_element_type=jnp.float32)


def correlate_kernel(whitened, panel, nb=32):
    chans, samples = whitened.shape
    k_count = panel.shape[0]
    lanes = 128
    rows = CORR_ROWS
    padded = jnp.pad(panel.astype(jnp.float32), ((0, 0), (LAG, LAG)))
    grid = samples // (nb * lanes)
    out = pl.pallas_call(
        functools.partial(corr_body, nb, rows),
        grid=(grid,),
        in_specs=[
            pl.BlockSpec((chans, nb * lanes), lambda n: (0, n)),
            pl.BlockSpec((k_count, samples + 2 * LAG), lambda n: (0, 0)),
        ],
        out_specs=pl.BlockSpec((k_count * rows, chans), lambda n: (0, 0)),
        out_shape=jax.ShapeDtypeStruct((k_count * rows, chans), jnp.float32),
        scratch_shapes=[pltpu.VMEM((k_count * rows, nb * lanes), jnp.bfloat16)],
        compiler_params=pltpu.CompilerParams(dimension_semantics=("arbitrary",)),
        cost_estimate=pl.CostEstimate(
            flops=2 * k_count * rows * samples * chans,
            bytes_accessed=2 * chans * samples + 4 * k_count * (samples + rows * chans),
            transcendentals=0,
        ),
    )(whitened, padded)
    return out


def chan_filter(piece, tap_table):
    channels_here = piece.shape[0]
    half = (tap_table.shape[0] - 1) // 2
    widened = padded_2(piece, (("chan", 0),), half)
    total = jnp.dot(
        band_matrix(tap_table, channels_here, channels_here + 2 * half),
        widened,
        preferred_element_type=jnp.float32,
    )
    return total.astype(jnp.bfloat16)


def prep_body(section_chunk, rec_ref, lo_ref, hi_ref, blo_ref, bmid_ref, bhi_ref, tw_ref, o_ref, cp_ref, tp_ref):
    chans, samples = o_ref.shape
    lanes = 128
    cp_ref[:, pl.ds(0, lanes)] = jnp.zeros((chans, lanes), cp_ref.dtype)
    cp_ref[:, pl.ds(samples + lanes, lanes)] = jnp.zeros((chans, lanes), cp_ref.dtype)
    chunk = section_chunk

    def chan_step(i, carry):
        off = pl.multiple_of(i * chunk, chunk)
        total = jnp.dot(bmid_ref[...], rec_ref[0, :, pl.ds(off, chunk)], preferred_element_type=jnp.float32)
        total += jnp.dot(blo_ref[...], lo_ref[:, pl.ds(off, chunk)], preferred_element_type=jnp.float32)
        total += jnp.dot(bhi_ref[...], hi_ref[:, pl.ds(off, chunk)], preferred_element_type=jnp.float32)
        cp_ref[:, pl.ds(pl.multiple_of(off + lanes, lanes), chunk)] = total.astype(cp_ref.dtype)
        return carry

    lax.fori_loop(0, samples // chunk, chan_step, 0)

    group = 32

    def time_step(g, acc):
        base = g * group
        windows = [
            cp_ref[:, pl.ds(pl.multiple_of((base + q) * lanes, lanes), 3 * lanes)]
            for q in range(group)
        ]
        y = jnp.dot(jnp.concatenate(windows, axis=0), tw_ref[...], preferred_element_type=jnp.float32)
        for q in range(group):
            part = y[q * chans : (q + 1) * chans]
            tp_ref[:, pl.ds(pl.multiple_of((base + q) * lanes, lanes), lanes)] = part
            acc = acc + part * part
        return acc

    acc = lax.fori_loop(0, samples // (lanes * group), time_step, jnp.zeros((chans, lanes), jnp.float32))
    power = jnp.sum(acc, axis=1, keepdims=True) / samples
    scale = lax.rsqrt(power + 1e-06)

    def white_step(i, carry):
        off = pl.multiple_of(i * chunk, chunk)
        o_ref[:, pl.ds(off, chunk)] = (tp_ref[:, pl.ds(off, chunk)] * scale).astype(o_ref.dtype)
        return carry

    lax.fori_loop(0, samples // chunk, white_step, 0)


def prepare_kernel(record, section, lo, hi, band, time_weights):
    count_steps, chans, samples = record.shape
    half = lo.shape[0]
    lanes = 128
    chunk = 2048
    blo, bmid, bhi = band[:, :half], band[:, half:half + chans], band[:, half + chans:]
    full = lambda i: (0, 0)
    return pl.pallas_call(
        functools.partial(prep_body, chunk),
        grid=(1,),
        in_specs=[
            pl.BlockSpec((1, chans, samples), lambda i: (section, 0, 0)),
            pl.BlockSpec((half, samples), full),
            pl.BlockSpec((half, samples), full),
            pl.BlockSpec((chans, half), full),
            pl.BlockSpec((chans, chans), full),
            pl.BlockSpec((chans, half), full),
            pl.BlockSpec(time_weights.shape, full),
        ],
        out_specs=pl.BlockSpec((chans, samples), full),
        out_shape=jax.ShapeDtypeStruct((chans, samples), jnp.bfloat16),
        scratch_shapes=[
            pltpu.VMEM((chans, samples + 2 * lanes), jnp.bfloat16),
            pltpu.VMEM((chans, samples), jnp.float32),
        ],
        compiler_params=pltpu.CompilerParams(vmem_limit_bytes=48 * 1024 * 1024),
        cost_estimate=pl.CostEstimate(
            flops=2 * chans * samples * (chans + 2 * half + 3 * lanes),
            bytes_accessed=2 * samples * (2 * chans + 2 * half),
            transcendentals=chans,
        ),
    )(record, lo, hi, blo, bmid, bhi, time_weights)


def xor_sum(x, axis):
    count = lax.axis_size(axis)
    if count & (count - 1):
        return lax.psum(x, axis)
    step = 1
    while step < count:
        x = x + lax.ppermute(x, axis, [(i, i ^ step) for i in range(count)])
        step *= 2
    return x


def body(record, chan_taps, time_taps, sources):
    count_steps = record.shape[0]
    channels_here = record.shape[1]
    samples = record.shape[2]
    chan_table = chan_taps.astype(jnp.bfloat16)
    time_table = time_taps.astype(jnp.bfloat16)
    first_chan = lax.axis_index("chan") * channels_here
    selector = (
        (sources - first_chan)[:, :, None] == lax.iota(jnp.int32, channels_here)[None, None, :]
    ).astype(jnp.bfloat16)
    normalizer = 1.0 / math.sqrt(samples * lax.axis_size("win"))

    half = (chan_table.shape[0] - 1) // 2
    count = lax.axis_size("chan")
    band = band_matrix(chan_table, channels_here, channels_here + 2 * half)
    offset = lax.iota(jnp.int32, 384)[:, None] - 128 - lax.iota(jnp.int32, 128)[None, :]
    time_weights = tap_lookup(offset + (time_table.shape[0] - 1) // 2, time_table)

    heads = record[:, :half]
    tails = record[:, channels_here - half :]
    lowers = lax.ppermute(tails, "chan", [(i, i + 1) for i in range(count - 1)])
    uppers = lax.ppermute(heads, "chan", [(i + 1, i) for i in range(count - 1)])

    def prepare(whole, section):
        lower, upper = lowers[section], uppers[section]
        whitened = prepare_kernel(whole, section, lower, upper, band, time_weights)
        term = jnp.dot(selector[section], whitened, preferred_element_type=jnp.float32)
        return whitened, xor_sum(term.astype(jnp.bfloat16), "chan")

    pieces = [record] * count_steps
    results = []
    pending = prepare(pieces[0], 0)
    for section in range(count_steps):
        upcoming = None
        if section + 1 < count_steps:
            upcoming = prepare(pieces[section + 1], section + 1)
        whitened, panel = pending
        if section >= 2:
            whitened, panel, results[section - 2] = lax.optimization_barrier(
                (whitened, panel, results[section - 2])
            )
        if section + 1 < count_steps:
            partial_corr = correlate_kernel(whitened, panel)
            if section + 2 < count_steps:
                pieces[section + 2], partial_corr = lax.optimization_barrier(
                    (pieces[section + 2], partial_corr)
                )
            results.append(xor_sum(partial_corr, "win"))
        else:
            half = panel.shape[0] // 2
            parts = [
                xor_sum(correlate_kernel(whitened, panel[:half]), "win"),
                xor_sum(correlate_kernel(whitened, panel[half:]), "win"),
            ]
            results.append(jnp.concatenate(parts, axis=0))
        pending = upcoming
    lags = 2 * LAG + 1
    shaped = [total.reshape(-1, CORR_ROWS, channels_here)[:, :lags] for total in results]
    return jnp.stack(shaped) * normalizer


def solution(mesh):
    in_specs = (P(None, "chan", "win"), P(), P(), P())
    out_specs = P(None, None, None, "chan")
    return jax.shard_map(body, mesh=mesh, in_specs=in_specs, out_specs=out_specs, check_vma=False)
```

```python
import functools
import math

import jax
import jax.numpy as jnp
from jax import lax
from jax.experimental import pallas as pl
from jax.experimental.pallas import tpu as pltpu
from jax.sharding import PartitionSpec as P

LAG = 64
CORR_ROWS = 136


def padded_2(cells, sides, width):
    for axis, dim in sides:
        count = lax.axis_size(axis)
        ends = count - 1
        head = lax.slice_in_dim(cells, 0, width, axis=dim)
        tail = lax.slice_in_dim(cells, cells.shape[dim] - width, cells.shape[dim], axis=dim)
        cells = jnp.concatenate(
            [
                lax.ppermute(tail, axis, [(i, (i + 1) % count) for i in range(ends)]),
                cells,
                lax.ppermute(head, axis, [((i + 1) % count, i) for i in range(ends)]),
            ],
            axis=dim,
        )
    return cells


def tap_lookup(offset, tap_table):
    count_taps = tap_table.shape[0]
    marks = offset[..., None] == lax.iota(jnp.int32, count_taps)
    picked = jnp.where(marks, tap_table.astype(jnp.float32), jnp.zeros((), jnp.float32))
    return jnp.sum(picked, axis=-1).astype(tap_table.dtype)


def band_matrix(tap_table, height, breadth):
    offset = lax.iota(jnp.int32, breadth)[None, :] - lax.iota(jnp.int32, height)[:, None]
    return tap_lookup(offset, tap_table)


def time_filter(chan_pass, tap_table):
    channels_here, samples = chan_pass.shape
    half = (tap_table.shape[0] - 1) // 2
    blocks = chan_pass.reshape(channels_here, samples // 128, 128)
    zeros_block = jnp.zeros_like(blocks[:, :1])
    earlier = jnp.concatenate([zeros_block, blocks[:, :-1]], axis=1)
    later = jnp.concatenate([blocks[:, 1:], zeros_block], axis=1)
    extended = jnp.concatenate([earlier, blocks, later], axis=2)
    offset = lax.iota(jnp.int32, 384)[:, None] - 128 - lax.iota(jnp.int32, 128)[None, :] + half
    weights = tap_lookup(offset, tap_table)
    result = jnp.einsum("cbr,rt->cbt", extended, weights, preferred_element_type=jnp.float32)
    return result.reshape(channels_here, samples)


def whiten(time_pass):
    power = jnp.mean(time_pass * time_pass, axis=-1, keepdims=True)
    return (time_pass * lax.rsqrt(power + 1e-06)).astype(jnp.bfloat16)


def corr_body(nb, rows, w_ref, p_ref, o_ref, s_ref):
    n = pl.program_id(0)
    k_count = p_ref.shape[0]
    lanes = 128

    @pl.when(n == 0)
    def _():
        o_ref[...] = jnp.zeros_like(o_ref)

    j_idx = lax.broadcasted_iota(jnp.int32, (rows, lanes), 0)
    r_idx = lax.broadcasted_iota(jnp.int32, (rows, lanes), 1)
    upper = r_idx >= j_idx
    for k in range(k_count):
        rolled = []
        for b in range(nb + 1):
            start = pl.multiple_of((n * nb + b) * lanes, lanes)
            chunk = p_ref[pl.ds(k, 1), pl.ds(start, lanes)]
            wide = jnp.broadcast_to(chunk, (rows, lanes))
            rolled.append(pltpu.roll(wide, 0, 1, stride=1, stride_axis=0))
        for b in range(nb):
            piece = jnp.where(upper, rolled[b + 1], rolled[b])
            s_ref[pl.ds(k * rows, rows), pl.ds(b * lanes, lanes)] = piece.astype(s_ref.dtype)
    o_ref[...] += lax.dot_general(
        s_ref[...], w_ref[...], (((1,), (1,)), ((), ())),
        preferred_element_type=jnp.float32)


def correlate_kernel(whitened, panel, nb=32):
    chans, samples = whitened.shape
    k_count = panel.shape[0]
    lanes = 128
    rows = CORR_ROWS
    padded = jnp.pad(panel.astype(jnp.float32), ((0, 0), (LAG, LAG)))
    grid = samples // (nb * lanes)
    out = pl.pallas_call(
        functools.partial(corr_body, nb, rows),
        grid=(grid,),
        in_specs=[
            pl.BlockSpec((chans, nb * lanes), lambda n: (0, n)),
            pl.BlockSpec((k_count, samples + 2 * LAG), lambda n: (0, 0)),
        ],
        out_specs=pl.BlockSpec((k_count * rows, chans), lambda n: (0, 0)),
        out_shape=jax.ShapeDtypeStruct((k_count * rows, chans), jnp.float32),
        scratch_shapes=[pltpu.VMEM((k_count * rows, nb * lanes), jnp.bfloat16)],
        compiler_params=pltpu.CompilerParams(dimension_semantics=("arbitrary",)),
        cost_estimate=pl.CostEstimate(
            flops=2 * k_count * rows * samples * chans,
            bytes_accessed=2 * chans * samples + 4 * k_count * (samples + rows * chans),
            transcendentals=0,
        ),
    )(whitened, padded)
    return out


def chan_filter(piece, tap_table):
    channels_here = piece.shape[0]
    half = (tap_table.shape[0] - 1) // 2
    widened = padded_2(piece, (("chan", 0),), half)
    total = jnp.dot(
        band_matrix(tap_table, channels_here, channels_here + 2 * half),
        widened,
        preferred_element_type=jnp.float32,
    )
    return total.astype(jnp.bfloat16)


def prep_body(section_chunk, rec_ref, lo_ref, hi_ref, blo_ref, bmid_ref, bhi_ref, tw_ref, o_ref, cp_ref, tp_ref):
    chans, samples = o_ref.shape
    lanes = 128
    cp_ref[:, pl.ds(0, lanes)] = jnp.zeros((chans, lanes), cp_ref.dtype)
    cp_ref[:, pl.ds(samples + lanes, lanes)] = jnp.zeros((chans, lanes), cp_ref.dtype)
    chunk = section_chunk

    def chan_step(i, carry):
        off = pl.multiple_of(i * chunk, chunk)
        total = jnp.dot(bmid_ref[...], rec_ref[0, :, pl.ds(off, chunk)], preferred_element_type=jnp.float32)
        total += jnp.dot(blo_ref[...], lo_ref[:, pl.ds(off, chunk)], preferred_element_type=jnp.float32)
        total += jnp.dot(bhi_ref[...], hi_ref[:, pl.ds(off, chunk)], preferred_element_type=jnp.float32)
        cp_ref[:, pl.ds(pl.multiple_of(off + lanes, lanes), chunk)] = total.astype(cp_ref.dtype)
        return carry

    lax.fori_loop(0, samples // chunk, chan_step, 0)

    group = 64

    def time_step(g, acc):
        base = g * group
        windows = [
            cp_ref[:, pl.ds(pl.multiple_of((base + q) * lanes, lanes), 3 * lanes)]
            for q in range(group)
        ]
        y = jnp.dot(jnp.concatenate(windows, axis=0), tw_ref[...], preferred_element_type=jnp.float32)
        for q in range(group):
            part = y[q * chans : (q + 1) * chans]
            tp_ref[:, pl.ds(pl.multiple_of((base + q) * lanes, lanes), lanes)] = part
            acc = acc + part * part
        return acc

    acc = lax.fori_loop(0, samples // (lanes * group), time_step, jnp.zeros((chans, lanes), jnp.float32))
    power = jnp.sum(acc, axis=1, keepdims=True) / samples
    scale = lax.rsqrt(power + 1e-06)

    def white_step(i, carry):
        off = pl.multiple_of(i * chunk, chunk)
        o_ref[:, pl.ds(off, chunk)] = (tp_ref[:, pl.ds(off, chunk)] * scale).astype(o_ref.dtype)
        return carry

    lax.fori_loop(0, samples // chunk, white_step, 0)


def prepare_kernel(record, section, lo, hi, band, time_weights):
    count_steps, chans, samples = record.shape
    half = lo.shape[0]
    lanes = 128
    chunk = 4096
    blo, bmid, bhi = band[:, :half], band[:, half:half + chans], band[:, half + chans:]
    full = lambda i: (0, 0)
    return pl.pallas_call(
        functools.partial(prep_body, chunk),
        grid=(1,),
        in_specs=[
            pl.BlockSpec((1, chans, samples), lambda i: (section, 0, 0)),
            pl.BlockSpec((half, samples), full),
            pl.BlockSpec((half, samples), full),
            pl.BlockSpec((chans, half), full),
            pl.BlockSpec((chans, chans), full),
            pl.BlockSpec((chans, half), full),
            pl.BlockSpec(time_weights.shape, full),
        ],
        out_specs=pl.BlockSpec((chans, samples), full),
        out_shape=jax.ShapeDtypeStruct((chans, samples), jnp.bfloat16),
        scratch_shapes=[
            pltpu.VMEM((chans, samples + 2 * lanes), jnp.bfloat16),
            pltpu.VMEM((chans, samples), jnp.float32),
        ],
        compiler_params=pltpu.CompilerParams(vmem_limit_bytes=48 * 1024 * 1024),
        cost_estimate=pl.CostEstimate(
            flops=2 * chans * samples * (chans + 2 * half + 3 * lanes),
            bytes_accessed=2 * samples * (2 * chans + 2 * half),
            transcendentals=chans,
        ),
    )(record, lo, hi, blo, bmid, bhi, time_weights)


def xor_sum(x, axis):
    count = lax.axis_size(axis)
    if count & (count - 1):
        return lax.psum(x, axis)
    step = 1
    while step < count:
        x = x + lax.ppermute(x, axis, [(i, i ^ step) for i in range(count)])
        step *= 2
    return x


def body(record, chan_taps, time_taps, sources):
    count_steps = record.shape[0]
    channels_here = record.shape[1]
    samples = record.shape[2]
    chan_table = chan_taps.astype(jnp.bfloat16)
    time_table = time_taps.astype(jnp.bfloat16)
    first_chan = lax.axis_index("chan") * channels_here
    selector = (
        (sources - first_chan)[:, :, None] == lax.iota(jnp.int32, channels_here)[None, None, :]
    ).astype(jnp.bfloat16)
    normalizer = 1.0 / math.sqrt(samples * lax.axis_size("win"))

    half = (chan_table.shape[0] - 1) // 2
    count = lax.axis_size("chan")
    band = band_matrix(chan_table, channels_here, channels_here + 2 * half)
    offset = lax.iota(jnp.int32, 384)[:, None] - 128 - lax.iota(jnp.int32, 128)[None, :]
    time_weights = tap_lookup(offset + (time_table.shape[0] - 1) // 2, time_table)

    heads = record[:, :half]
    tails = record[:, channels_here - half :]
    lowers = lax.ppermute(tails, "chan", [(i, i + 1) for i in range(count - 1)])
    uppers = lax.ppermute(heads, "chan", [(i + 1, i) for i in range(count - 1)])

    def prepare(whole, section):
        lower, upper = lowers[section], uppers[section]
        whitened = prepare_kernel(whole, section, lower, upper, band, time_weights)
        term = jnp.dot(selector[section], whitened, preferred_element_type=jnp.float32)
        return whitened, xor_sum(term.astype(jnp.bfloat16), "chan")

    pieces = [record] * count_steps
    results = []
    pending = prepare(pieces[0], 0)
    for section in range(count_steps):
        upcoming = None
        if section + 1 < count_steps:
            upcoming = prepare(pieces[section + 1], section + 1)
        whitened, panel = pending
        if section >= 2:
            whitened, panel, results[section - 2] = lax.optimization_barrier(
                (whitened, panel, results[section - 2])
            )
        if section + 1 < count_steps:
            partial_corr = correlate_kernel(whitened, panel)
            if section + 2 < count_steps:
                pieces[section + 2], partial_corr = lax.optimization_barrier(
                    (pieces[section + 2], partial_corr)
                )
            results.append(xor_sum(partial_corr, "win"))
        else:
            half = panel.shape[0] // 2
            parts = [
                xor_sum(correlate_kernel(whitened, panel[:half]), "win"),
                xor_sum(correlate_kernel(whitened, panel[half:]), "win"),
            ]
            results.append(jnp.concatenate(parts, axis=0))
        pending = upcoming
    lags = 2 * LAG + 1
    shaped = [total.reshape(-1, CORR_ROWS, channels_here)[:, :lags] for total in results]
    return jnp.stack(shaped) * normalizer


def solution(mesh):
    in_specs = (P(None, "chan", "win"), P(), P(), P())
    out_specs = P(None, None, None, "chan")
    return jax.shard_map(body, mesh=mesh, in_specs=in_specs, out_specs=out_specs, check_vma=False)
```

```python
import functools
import math

import jax
import jax.numpy as jnp
from jax import lax
from jax.experimental import pallas as pl
from jax.experimental.pallas import tpu as pltpu
from jax.sharding import PartitionSpec as P

LAG = 64
CORR_ROWS = 136


def padded_2(cells, sides, width):
    for axis, dim in sides:
        count = lax.axis_size(axis)
        ends = count - 1
        head = lax.slice_in_dim(cells, 0, width, axis=dim)
        tail = lax.slice_in_dim(cells, cells.shape[dim] - width, cells.shape[dim], axis=dim)
        cells = jnp.concatenate(
            [
                lax.ppermute(tail, axis, [(i, (i + 1) % count) for i in range(ends)]),
                cells,
                lax.ppermute(head, axis, [((i + 1) % count, i) for i in range(ends)]),
            ],
            axis=dim,
        )
    return cells


def tap_lookup(offset, tap_table):
    count_taps = tap_table.shape[0]
    marks = offset[..., None] == lax.iota(jnp.int32, count_taps)
    picked = jnp.where(marks, tap_table.astype(jnp.float32), jnp.zeros((), jnp.float32))
    return jnp.sum(picked, axis=-1).astype(tap_table.dtype)


def band_matrix(tap_table, height, breadth):
    offset = lax.iota(jnp.int32, breadth)[None, :] - lax.iota(jnp.int32, height)[:, None]
    return tap_lookup(offset, tap_table)


def time_filter(chan_pass, tap_table):
    channels_here, samples = chan_pass.shape
    half = (tap_table.shape[0] - 1) // 2
    blocks = chan_pass.reshape(channels_here, samples // 128, 128)
    zeros_block = jnp.zeros_like(blocks[:, :1])
    earlier = jnp.concatenate([zeros_block, blocks[:, :-1]], axis=1)
    later = jnp.concatenate([blocks[:, 1:], zeros_block], axis=1)
    extended = jnp.concatenate([earlier, blocks, later], axis=2)
    offset = lax.iota(jnp.int32, 384)[:, None] - 128 - lax.iota(jnp.int32, 128)[None, :] + half
    weights = tap_lookup(offset, tap_table)
    result = jnp.einsum("cbr,rt->cbt", extended, weights, preferred_element_type=jnp.float32)
    return result.reshape(channels_here, samples)


def whiten(time_pass):
    power = jnp.mean(time_pass * time_pass, axis=-1, keepdims=True)
    return (time_pass * lax.rsqrt(power + 1e-06)).astype(jnp.bfloat16)


def corr_body(nb, rows, w_ref, p_ref, o_ref, s_ref):
    n = pl.program_id(0)
    k_count = p_ref.shape[0]
    lanes = 128

    @pl.when(n == 0)
    def _():
        o_ref[...] = jnp.zeros_like(o_ref)

    j_idx = lax.broadcasted_iota(jnp.int32, (rows, lanes), 0)
    r_idx = lax.broadcasted_iota(jnp.int32, (rows, lanes), 1)
    upper = r_idx >= j_idx
    for k in range(k_count):
        rolled = []
        for b in range(nb + 1):
            start = pl.multiple_of((n * nb + b) * lanes, lanes)
            chunk = p_ref[pl.ds(k, 1), pl.ds(start, lanes)]
            wide = jnp.broadcast_to(chunk, (rows, lanes))
            rolled.append(pltpu.roll(wide, 0, 1, stride=1, stride_axis=0))
        for b in range(nb):
            piece = jnp.where(upper, rolled[b + 1], rolled[b])
            s_ref[pl.ds(k * rows, rows), pl.ds(b * lanes, lanes)] = piece.astype(s_ref.dtype)
    o_ref[...] += lax.dot_general(
        s_ref[...], w_ref[...], (((1,), (1,)), ((), ())),
        preferred_element_type=jnp.float32)


def correlate_kernel(whitened, panel, nb=32):
    chans, samples = whitened.shape
    k_count = panel.shape[0]
    lanes = 128
    rows = CORR_ROWS
    padded = jnp.pad(panel.astype(jnp.float32), ((0, 0), (LAG, LAG)))
    grid = samples // (nb * lanes)
    out = pl.pallas_call(
        functools.partial(corr_body, nb, rows),
        grid=(grid,),
        in_specs=[
            pl.BlockSpec((chans, nb * lanes), lambda n: (0, n)),
            pl.BlockSpec((k_count, samples + 2 * LAG), lambda n: (0, 0)),
        ],
        out_specs=pl.BlockSpec((k_count * rows, chans), lambda n: (0, 0)),
        out_shape=jax.ShapeDtypeStruct((k_count * rows, chans), jnp.float32),
        scratch_shapes=[pltpu.VMEM((k_count * rows, nb * lanes), jnp.bfloat16)],
        compiler_params=pltpu.CompilerParams(dimension_semantics=("arbitrary",)),
        cost_estimate=pl.CostEstimate(
            flops=2 * k_count * rows * samples * chans,
            bytes_accessed=2 * chans * samples + 4 * k_count * (samples + rows * chans),
            transcendentals=0,
        ),
    )(whitened, padded)
    return out


def chan_filter(piece, tap_table):
    channels_here = piece.shape[0]
    half = (tap_table.shape[0] - 1) // 2
    widened = padded_2(piece, (("chan", 0),), half)
    total = jnp.dot(
        band_matrix(tap_table, channels_here, channels_here + 2 * half),
        widened,
        preferred_element_type=jnp.float32,
    )
    return total.astype(jnp.bfloat16)


def prep_body(section_chunk, rec_ref, lo_ref, hi_ref, blo_ref, bmid_ref, bhi_ref, tw_ref, o_ref, cp_ref, tp_ref):
    chans, samples = o_ref.shape
    lanes = 128
    cp_ref[:, pl.ds(0, lanes)] = jnp.zeros((chans, lanes), cp_ref.dtype)
    cp_ref[:, pl.ds(samples + lanes, lanes)] = jnp.zeros((chans, lanes), cp_ref.dtype)
    chunk = section_chunk

    def chan_step(i, carry):
        off = pl.multiple_of(i * chunk, chunk)
        total = jnp.dot(bmid_ref[...], rec_ref[0, :, pl.ds(off, chunk)], preferred_element_type=jnp.float32)
        total += jnp.dot(blo_ref[...], lo_ref[:, pl.ds(off, chunk)], preferred_element_type=jnp.float32)
        total += jnp.dot(bhi_ref[...], hi_ref[:, pl.ds(off, chunk)], preferred_element_type=jnp.float32)
        cp_ref[:, pl.ds(pl.multiple_of(off + lanes, lanes), chunk)] = total.astype(cp_ref.dtype)
        return carry

    lax.fori_loop(0, samples // chunk, chan_step, 0)

    group = 64

    def time_step(g, acc):
        base = g * group
        windows = [
            cp_ref[:, pl.ds(pl.multiple_of((base + q) * lanes, lanes), 3 * lanes)]
            for q in range(group)
        ]
        y = jnp.dot(jnp.concatenate(windows, axis=0), tw_ref[...], preferred_element_type=jnp.float32)
        for q in range(group):
            part = y[q * chans : (q + 1) * chans]
            tp_ref[:, pl.ds(pl.multiple_of((base + q) * lanes, lanes), lanes)] = part
            acc = acc + part * part
        return acc

    acc = lax.fori_loop(0, samples // (lanes * group), time_step, jnp.zeros((chans, lanes), jnp.float32))
    power = jnp.sum(acc, axis=1, keepdims=True) / samples
    scale = lax.rsqrt(power + 1e-06)

    def white_step(i, carry):
        off = pl.multiple_of(i * chunk, chunk)
        o_ref[:, pl.ds(off, chunk)] = (tp_ref[:, pl.ds(off, chunk)] * scale).astype(o_ref.dtype)
        return carry

    lax.fori_loop(0, samples // chunk, white_step, 0)


def prepare_kernel(record, section, lo, hi, band, time_weights):
    count_steps, chans, samples = record.shape
    half = lo.shape[0]
    lanes = 128
    chunk = 4096
    blo, bmid, bhi = band[:, :half], band[:, half:half + chans], band[:, half + chans:]
    full = lambda i: (0, 0)
    return pl.pallas_call(
        functools.partial(prep_body, chunk),
        grid=(1,),
        in_specs=[
            pl.BlockSpec((1, chans, samples), lambda i: (section, 0, 0)),
            pl.BlockSpec((half, samples), full),
            pl.BlockSpec((half, samples), full),
            pl.BlockSpec((chans, half), full),
            pl.BlockSpec((chans, chans), full),
            pl.BlockSpec((chans, half), full),
            pl.BlockSpec(time_weights.shape, full),
        ],
        out_specs=pl.BlockSpec((chans, samples), full),
        out_shape=jax.ShapeDtypeStruct((chans, samples), jnp.bfloat16),
        scratch_shapes=[
            pltpu.VMEM((chans, samples + 2 * lanes), jnp.bfloat16),
            pltpu.VMEM((chans, samples), jnp.float32),
        ],
        compiler_params=pltpu.CompilerParams(vmem_limit_bytes=48 * 1024 * 1024),
        cost_estimate=pl.CostEstimate(
            flops=2 * chans * samples * (chans + 2 * half + 3 * lanes),
            bytes_accessed=2 * samples * (2 * chans + 2 * half),
            transcendentals=chans,
        ),
    )(record, lo, hi, blo, bmid, bhi, time_weights)


def xor_sum(x, axis):
    count = lax.axis_size(axis)
    if count & (count - 1):
        return lax.psum(x, axis)
    step = 1
    while step < count:
        x = x + lax.ppermute(x, axis, [(i, i ^ step) for i in range(count)])
        step *= 2
    return x


def body(record, chan_taps, time_taps, sources):
    count_steps = record.shape[0]
    channels_here = record.shape[1]
    samples = record.shape[2]
    chan_table = chan_taps.astype(jnp.bfloat16)
    time_table = time_taps.astype(jnp.bfloat16)
    first_chan = lax.axis_index("chan") * channels_here
    selector = (
        (sources - first_chan)[:, :, None] == lax.iota(jnp.int32, channels_here)[None, None, :]
    ).astype(jnp.bfloat16)
    normalizer = 1.0 / math.sqrt(samples * lax.axis_size("win"))

    half = (chan_table.shape[0] - 1) // 2
    count = lax.axis_size("chan")
    band = band_matrix(chan_table, channels_here, channels_here + 2 * half)
    offset = lax.iota(jnp.int32, 384)[:, None] - 128 - lax.iota(jnp.int32, 128)[None, :]
    time_weights = tap_lookup(offset + (time_table.shape[0] - 1) // 2, time_table)

    heads = record[:, :half]
    tails = record[:, channels_here - half :]
    lowers = lax.ppermute(tails, "chan", [(i, i + 1) for i in range(count - 1)])
    uppers = lax.ppermute(heads, "chan", [(i + 1, i) for i in range(count - 1)])

    def prepare(whole, section):
        lower, upper = lowers[section], uppers[section]
        whitened = prepare_kernel(whole, section, lower, upper, band, time_weights)
        term = jnp.dot(selector[section], whitened, preferred_element_type=jnp.float32)
        return whitened, xor_sum(term.astype(jnp.bfloat16), "chan")

    pieces = [record] * count_steps
    results = []
    pending = prepare(pieces[0], 0)
    for section in range(count_steps):
        upcoming = None
        if section + 1 < count_steps:
            upcoming = prepare(pieces[section + 1], section + 1)
        whitened, panel = pending
        if section >= 2:
            whitened, panel, results[section - 2] = lax.optimization_barrier(
                (whitened, panel, results[section - 2])
            )
        partial_corr = correlate_kernel(whitened, panel)
        if section + 2 < count_steps:
            pieces[section + 2], partial_corr = lax.optimization_barrier(
                (pieces[section + 2], partial_corr)
            )
        results.append(xor_sum(partial_corr, "win"))
        pending = upcoming
    lags = 2 * LAG + 1
    shaped = [total.reshape(-1, CORR_ROWS, channels_here)[:, :lags] for total in results]
    return jnp.stack(shaped) * normalizer


def solution(mesh):
    in_specs = (P(None, "chan", "win"), P(), P(), P())
    out_specs = P(None, None, None, "chan")
    return jax.shard_map(body, mesh=mesh, in_specs=in_specs, out_specs=out_specs, check_vma=False)
```

```python
import functools
import math

import jax
import jax.numpy as jnp
from jax import lax
from jax.experimental import pallas as pl
from jax.experimental.pallas import tpu as pltpu
from jax.sharding import PartitionSpec as P

LAG = 64
CORR_ROWS = 136


def padded_2(cells, sides, width):
    for axis, dim in sides:
        count = lax.axis_size(axis)
        ends = count - 1
        head = lax.slice_in_dim(cells, 0, width, axis=dim)
        tail = lax.slice_in_dim(cells, cells.shape[dim] - width, cells.shape[dim], axis=dim)
        cells = jnp.concatenate(
            [
                lax.ppermute(tail, axis, [(i, (i + 1) % count) for i in range(ends)]),
                cells,
                lax.ppermute(head, axis, [((i + 1) % count, i) for i in range(ends)]),
            ],
            axis=dim,
        )
    return cells


def tap_lookup(offset, tap_table):
    count_taps = tap_table.shape[0]
    marks = offset[..., None] == lax.iota(jnp.int32, count_taps)
    picked = jnp.where(marks, tap_table.astype(jnp.float32), jnp.zeros((), jnp.float32))
    return jnp.sum(picked, axis=-1).astype(tap_table.dtype)


def band_matrix(tap_table, height, breadth):
    offset = lax.iota(jnp.int32, breadth)[None, :] - lax.iota(jnp.int32, height)[:, None]
    return tap_lookup(offset, tap_table)


def time_filter(chan_pass, tap_table):
    channels_here, samples = chan_pass.shape
    half = (tap_table.shape[0] - 1) // 2
    blocks = chan_pass.reshape(channels_here, samples // 128, 128)
    zeros_block = jnp.zeros_like(blocks[:, :1])
    earlier = jnp.concatenate([zeros_block, blocks[:, :-1]], axis=1)
    later = jnp.concatenate([blocks[:, 1:], zeros_block], axis=1)
    extended = jnp.concatenate([earlier, blocks, later], axis=2)
    offset = lax.iota(jnp.int32, 384)[:, None] - 128 - lax.iota(jnp.int32, 128)[None, :] + half
    weights = tap_lookup(offset, tap_table)
    result = jnp.einsum("cbr,rt->cbt", extended, weights, preferred_element_type=jnp.float32)
    return result.reshape(channels_here, samples)


def whiten(time_pass):
    power = jnp.mean(time_pass * time_pass, axis=-1, keepdims=True)
    return (time_pass * lax.rsqrt(power + 1e-06)).astype(jnp.bfloat16)


def corr_body(nb, rows, w_ref, p_ref, o_ref, s_ref):
    n = pl.program_id(0)
    k_count = p_ref.shape[0]
    lanes = 128

    @pl.when(n == 0)
    def _():
        o_ref[...] = jnp.zeros_like(o_ref)

    j_idx = lax.broadcasted_iota(jnp.int32, (rows, lanes), 0)
    r_idx = lax.broadcasted_iota(jnp.int32, (rows, lanes), 1)
    upper = r_idx >= j_idx
    for k in range(k_count):
        rolled = []
        for b in range(nb + 1):
            start = pl.multiple_of((n * nb + b) * lanes, lanes)
            chunk = p_ref[pl.ds(k, 1), pl.ds(start, lanes)]
            wide = jnp.broadcast_to(chunk, (rows, lanes))
            rolled.append(pltpu.roll(wide, 0, 1, stride=1, stride_axis=0))
        for b in range(nb):
            piece = jnp.where(upper, rolled[b + 1], rolled[b])
            s_ref[pl.ds(k * rows, rows), pl.ds(b * lanes, lanes)] = piece.astype(s_ref.dtype)
    o_ref[...] += lax.dot_general(
        s_ref[...], w_ref[...], (((1,), (1,)), ((), ())),
        preferred_element_type=jnp.float32)


def correlate_kernel(whitened, panel, nb=32):
    chans, samples = whitened.shape
    k_count = panel.shape[0]
    lanes = 128
    rows = CORR_ROWS
    padded = jnp.pad(panel.astype(jnp.float32), ((0, 0), (LAG, LAG)))
    grid = samples // (nb * lanes)
    out = pl.pallas_call(
        functools.partial(corr_body, nb, rows),
        grid=(grid,),
        in_specs=[
            pl.BlockSpec((chans, nb * lanes), lambda n: (0, n)),
            pl.BlockSpec((k_count, samples + 2 * LAG), lambda n: (0, 0)),
        ],
        out_specs=pl.BlockSpec((k_count * rows, chans), lambda n: (0, 0)),
        out_shape=jax.ShapeDtypeStruct((k_count * rows, chans), jnp.float32),
        scratch_shapes=[pltpu.VMEM((k_count * rows, nb * lanes), jnp.bfloat16)],
        compiler_params=pltpu.CompilerParams(dimension_semantics=("arbitrary",)),
        cost_estimate=pl.CostEstimate(
            flops=2 * k_count * rows * samples * chans,
            bytes_accessed=2 * chans * samples + 4 * k_count * (samples + rows * chans),
            transcendentals=0,
        ),
    )(whitened, padded)
    return out


def chan_filter(piece, tap_table):
    channels_here = piece.shape[0]
    half = (tap_table.shape[0] - 1) // 2
    widened = padded_2(piece, (("chan", 0),), half)
    total = jnp.dot(
        band_matrix(tap_table, channels_here, channels_here + 2 * half),
        widened,
        preferred_element_type=jnp.float32,
    )
    return total.astype(jnp.bfloat16)


def prep_body(section_chunk, rec_ref, lo_ref, hi_ref, blo_ref, bmid_ref, bhi_ref, tw_ref, o_ref, cp_ref, tp_ref):
    chans, samples = o_ref.shape
    lanes = 128
    cp_ref[:, pl.ds(0, lanes)] = jnp.zeros((chans, lanes), cp_ref.dtype)
    cp_ref[:, pl.ds(samples + lanes, lanes)] = jnp.zeros((chans, lanes), cp_ref.dtype)
    chunk = section_chunk

    def chan_step(i, carry):
        off = pl.multiple_of(i * chunk, chunk)
        total = jnp.dot(bmid_ref[...], rec_ref[0, :, pl.ds(off, chunk)], preferred_element_type=jnp.float32)
        total += jnp.dot(blo_ref[...], lo_ref[:, pl.ds(off, chunk)], preferred_element_type=jnp.float32)
        total += jnp.dot(bhi_ref[...], hi_ref[:, pl.ds(off, chunk)], preferred_element_type=jnp.float32)
        cp_ref[:, pl.ds(pl.multiple_of(off + lanes, lanes), chunk)] = total.astype(cp_ref.dtype)
        return carry

    lax.fori_loop(0, samples // chunk, chan_step, 0)

    group = 64

    def time_step(g, acc):
        base = g * group
        windows = [
            cp_ref[:, pl.ds(pl.multiple_of((base + q) * lanes, lanes), 3 * lanes)]
            for q in range(group)
        ]
        y = jnp.dot(jnp.concatenate(windows, axis=0), tw_ref[...], preferred_element_type=jnp.float32)
        for q in range(group):
            part = y[q * chans : (q + 1) * chans]
            tp_ref[:, pl.ds(pl.multiple_of((base + q) * lanes, lanes), lanes)] = part
            acc = acc + part * part
        return acc

    acc = lax.fori_loop(0, samples // (lanes * group), time_step, jnp.zeros((chans, lanes), jnp.float32))
    power = jnp.sum(acc, axis=1, keepdims=True) / samples
    scale = lax.rsqrt(power + 1e-06)

    def white_step(i, carry):
        off = pl.multiple_of(i * chunk, chunk)
        o_ref[:, pl.ds(off, chunk)] = (tp_ref[:, pl.ds(off, chunk)] * scale).astype(o_ref.dtype)
        return carry

    lax.fori_loop(0, samples // chunk, white_step, 0)


def prepare_kernel(record, section, lo, hi, band, time_weights):
    count_steps, chans, samples = record.shape
    half = lo.shape[0]
    lanes = 128
    chunk = 4096
    blo, bmid, bhi = band[:, :half], band[:, half:half + chans], band[:, half + chans:]
    full = lambda i: (0, 0)
    return pl.pallas_call(
        functools.partial(prep_body, chunk),
        grid=(1,),
        in_specs=[
            pl.BlockSpec((1, chans, samples), lambda i: (section, 0, 0)),
            pl.BlockSpec((half, samples), full),
            pl.BlockSpec((half, samples), full),
            pl.BlockSpec((chans, half), full),
            pl.BlockSpec((chans, chans), full),
            pl.BlockSpec((chans, half), full),
            pl.BlockSpec(time_weights.shape, full),
        ],
        out_specs=pl.BlockSpec((chans, samples), full),
        out_shape=jax.ShapeDtypeStruct((chans, samples), jnp.bfloat16),
        scratch_shapes=[
            pltpu.VMEM((chans, samples + 2 * lanes), jnp.bfloat16),
            pltpu.VMEM((chans, samples), jnp.float32),
        ],
        compiler_params=pltpu.CompilerParams(vmem_limit_bytes=48 * 1024 * 1024),
        cost_estimate=pl.CostEstimate(
            flops=2 * chans * samples * (chans + 2 * half + 3 * lanes),
            bytes_accessed=2 * samples * (2 * chans + 2 * half),
            transcendentals=chans,
        ),
    )(record, lo, hi, blo, bmid, bhi, time_weights)


def xor_sum(x, axis):
    count = lax.axis_size(axis)
    if count & (count - 1):
        return lax.psum(x, axis)
    step = 1
    while step < count:
        x = x + lax.ppermute(x, axis, [(i, i ^ step) for i in range(count)])
        step *= 2
    return x


def body(record, chan_taps, time_taps, sources):
    count_steps = record.shape[0]
    channels_here = record.shape[1]
    samples = record.shape[2]
    chan_table = chan_taps.astype(jnp.bfloat16)
    time_table = time_taps.astype(jnp.bfloat16)
    first_chan = lax.axis_index("chan") * channels_here
    selector = (
        (sources - first_chan)[:, :, None] == lax.iota(jnp.int32, channels_here)[None, None, :]
    ).astype(jnp.bfloat16)
    normalizer = 1.0 / math.sqrt(samples * lax.axis_size("win"))

    half = (chan_table.shape[0] - 1) // 2
    count = lax.axis_size("chan")
    band = band_matrix(chan_table, channels_here, channels_here + 2 * half)
    offset = lax.iota(jnp.int32, 384)[:, None] - 128 - lax.iota(jnp.int32, 128)[None, :]
    time_weights = tap_lookup(offset + (time_table.shape[0] - 1) // 2, time_table)

    heads = record[:, :half]
    tails = record[:, channels_here - half :]
    lowers = lax.ppermute(tails, "chan", [(i, i + 1) for i in range(count - 1)])
    uppers = lax.ppermute(heads, "chan", [(i + 1, i) for i in range(count - 1)])

    def prepare(whole, section):
        lower, upper = lowers[section], uppers[section]
        whitened = prepare_kernel(whole, section, lower, upper, band, time_weights)
        term = jnp.dot(selector[section], whitened, preferred_element_type=jnp.float32)
        return whitened, xor_sum(term.astype(jnp.bfloat16), "chan")

    pieces = [record] * count_steps
    results = []
    pending = prepare(pieces[0], 0)
    for section in range(count_steps):
        upcoming = None
        if section + 1 < count_steps:
            upcoming = prepare(pieces[section + 1], section + 1)
        whitened, panel = pending
        if section >= 2:
            whitened, panel, results[section - 2] = lax.optimization_barrier(
                (whitened, panel, results[section - 2])
            )
        if section + 1 < count_steps:
            partial_corr = correlate_kernel(whitened, panel)
            if section + 2 < count_steps:
                pieces[section + 2], partial_corr = lax.optimization_barrier(
                    (pieces[section + 2], partial_corr)
                )
            results.append(xor_sum(partial_corr, "win"))
        else:
            parts = [
                xor_sum(correlate_kernel(whitened, panel[source : source + 1]), "win")
                for source in range(panel.shape[0])
            ]
            results.append(jnp.concatenate(parts, axis=0))
        pending = upcoming
    lags = 2 * LAG + 1
    shaped = [total.reshape(-1, CORR_ROWS, channels_here)[:, :lags] for total in results]
    return jnp.stack(shaped) * normalizer


def solution(mesh):
    in_specs = (P(None, "chan", "win"), P(), P(), P())
    out_specs = P(None, None, None, "chan")
    return jax.shard_map(body, mesh=mesh, in_specs=in_specs, out_specs=out_specs, check_vma=False)
```

```python
import functools
import math

import jax
import jax.numpy as jnp
from jax import lax
from jax.experimental import pallas as pl
from jax.experimental.pallas import tpu as pltpu
from jax.sharding import PartitionSpec as P

LAG = 64
CORR_ROWS = 136


def padded_2(cells, sides, width):
    for axis, dim in sides:
        count = lax.axis_size(axis)
        ends = count - 1
        head = lax.slice_in_dim(cells, 0, width, axis=dim)
        tail = lax.slice_in_dim(cells, cells.shape[dim] - width, cells.shape[dim], axis=dim)
        cells = jnp.concatenate(
            [
                lax.ppermute(tail, axis, [(i, (i + 1) % count) for i in range(ends)]),
                cells,
                lax.ppermute(head, axis, [((i + 1) % count, i) for i in range(ends)]),
            ],
            axis=dim,
        )
    return cells


def tap_lookup(offset, tap_table):
    count_taps = tap_table.shape[0]
    marks = offset[..., None] == lax.iota(jnp.int32, count_taps)
    picked = jnp.where(marks, tap_table.astype(jnp.float32), jnp.zeros((), jnp.float32))
    return jnp.sum(picked, axis=-1).astype(tap_table.dtype)


def band_matrix(tap_table, height, breadth):
    offset = lax.iota(jnp.int32, breadth)[None, :] - lax.iota(jnp.int32, height)[:, None]
    return tap_lookup(offset, tap_table)


def time_filter(chan_pass, tap_table):
    channels_here, samples = chan_pass.shape
    half = (tap_table.shape[0] - 1) // 2
    blocks = chan_pass.reshape(channels_here, samples // 128, 128)
    zeros_block = jnp.zeros_like(blocks[:, :1])
    earlier = jnp.concatenate([zeros_block, blocks[:, :-1]], axis=1)
    later = jnp.concatenate([blocks[:, 1:], zeros_block], axis=1)
    extended = jnp.concatenate([earlier, blocks, later], axis=2)
    offset = lax.iota(jnp.int32, 384)[:, None] - 128 - lax.iota(jnp.int32, 128)[None, :] + half
    weights = tap_lookup(offset, tap_table)
    result = jnp.einsum("cbr,rt->cbt", extended, weights, preferred_element_type=jnp.float32)
    return result.reshape(channels_here, samples)


def whiten(time_pass):
    power = jnp.mean(time_pass * time_pass, axis=-1, keepdims=True)
    return (time_pass * lax.rsqrt(power + 1e-06)).astype(jnp.bfloat16)


def corr_body(nb, rows, w_ref, p_ref, o_ref, s_ref):
    n = pl.program_id(0)
    k_count = p_ref.shape[0]
    lanes = 128

    @pl.when(n == 0)
    def _():
        o_ref[...] = jnp.zeros_like(o_ref)

    j_idx = lax.broadcasted_iota(jnp.int32, (rows, lanes), 0)
    r_idx = lax.broadcasted_iota(jnp.int32, (rows, lanes), 1)
    upper = r_idx >= j_idx
    for k in range(k_count):
        rolled = []
        for b in range(nb + 1):
            start = pl.multiple_of((n * nb + b) * lanes, lanes)
            chunk = p_ref[pl.ds(k, 1), pl.ds(start, lanes)]
            wide = jnp.broadcast_to(chunk, (rows, lanes))
            rolled.append(pltpu.roll(wide, 0, 1, stride=1, stride_axis=0))
        for b in range(nb):
            piece = jnp.where(upper, rolled[b + 1], rolled[b])
            s_ref[pl.ds(k * rows, rows), pl.ds(b * lanes, lanes)] = piece.astype(s_ref.dtype)
    o_ref[...] += lax.dot_general(
        s_ref[...], w_ref[...], (((1,), (1,)), ((), ())),
        preferred_element_type=jnp.float32)


def correlate_kernel(whitened, panel, nb=32):
    chans, samples = whitened.shape
    k_count = panel.shape[0]
    lanes = 128
    rows = CORR_ROWS
    padded = jnp.pad(panel.astype(jnp.float32), ((0, 0), (LAG, LAG)))
    grid = samples // (nb * lanes)
    out = pl.pallas_call(
        functools.partial(corr_body, nb, rows),
        grid=(grid,),
        in_specs=[
            pl.BlockSpec((chans, nb * lanes), lambda n: (0, n)),
            pl.BlockSpec((k_count, samples + 2 * LAG), lambda n: (0, 0)),
        ],
        out_specs=pl.BlockSpec((k_count * rows, chans), lambda n: (0, 0)),
        out_shape=jax.ShapeDtypeStruct((k_count * rows, chans), jnp.float32),
        scratch_shapes=[pltpu.VMEM((k_count * rows, nb * lanes), jnp.bfloat16)],
        compiler_params=pltpu.CompilerParams(dimension_semantics=("arbitrary",)),
        cost_estimate=pl.CostEstimate(
            flops=2 * k_count * rows * samples * chans,
            bytes_accessed=2 * chans * samples + 4 * k_count * (samples + rows * chans),
            transcendentals=0,
        ),
    )(whitened, padded)
    return out


def chan_filter(piece, tap_table):
    channels_here = piece.shape[0]
    half = (tap_table.shape[0] - 1) // 2
    widened = padded_2(piece, (("chan", 0),), half)
    total = jnp.dot(
        band_matrix(tap_table, channels_here, channels_here + 2 * half),
        widened,
        preferred_element_type=jnp.float32,
    )
    return total.astype(jnp.bfloat16)


def prep_body(section_chunk, rec_ref, lo_ref, hi_ref, blo_ref, bmid_ref, bhi_ref, tw_ref, o_ref, cp_ref, tp_ref):
    chans, samples = o_ref.shape
    lanes = 128
    cp_ref[:, pl.ds(0, lanes)] = jnp.zeros((chans, lanes), cp_ref.dtype)
    cp_ref[:, pl.ds(samples + lanes, lanes)] = jnp.zeros((chans, lanes), cp_ref.dtype)
    chunk = section_chunk

    def chan_step(i, carry):
        off = pl.multiple_of(i * chunk, chunk)
        total = jnp.dot(bmid_ref[...], rec_ref[0, :, pl.ds(off, chunk)], preferred_element_type=jnp.float32)
        total += jnp.dot(blo_ref[...], lo_ref[:, pl.ds(off, chunk)], preferred_element_type=jnp.float32)
        total += jnp.dot(bhi_ref[...], hi_ref[:, pl.ds(off, chunk)], preferred_element_type=jnp.float32)
        cp_ref[:, pl.ds(pl.multiple_of(off + lanes, lanes), chunk)] = total.astype(cp_ref.dtype)
        return carry

    lax.fori_loop(0, samples // chunk, chan_step, 0)

    group = 64

    def time_step(g, acc):
        base = g * group
        windows = [
            cp_ref[:, pl.ds(pl.multiple_of((base + q) * lanes, lanes), 3 * lanes)]
            for q in range(group)
        ]
        y = jnp.dot(jnp.concatenate(windows, axis=0), tw_ref[...], preferred_element_type=jnp.float32)
        for q in range(group):
            part = y[q * chans : (q + 1) * chans]
            tp_ref[:, pl.ds(pl.multiple_of((base + q) * lanes, lanes), lanes)] = part
            acc = acc + part * part
        return acc

    acc = lax.fori_loop(0, samples // (lanes * group), time_step, jnp.zeros((chans, lanes), jnp.float32))
    power = jnp.sum(acc, axis=1, keepdims=True) / samples
    scale = lax.rsqrt(power + 1e-06)

    def white_step(i, carry):
        off = pl.multiple_of(i * chunk, chunk)
        o_ref[:, pl.ds(off, chunk)] = (tp_ref[:, pl.ds(off, chunk)] * scale).astype(o_ref.dtype)
        return carry

    lax.fori_loop(0, samples // chunk, white_step, 0)


def prepare_kernel(record, section, lo, hi, band, time_weights):
    count_steps, chans, samples = record.shape
    half = lo.shape[0]
    lanes = 128
    chunk = 8192
    blo, bmid, bhi = band[:, :half], band[:, half:half + chans], band[:, half + chans:]
    full = lambda i: (0, 0)
    return pl.pallas_call(
        functools.partial(prep_body, chunk),
        grid=(1,),
        in_specs=[
            pl.BlockSpec((1, chans, samples), lambda i: (section, 0, 0)),
            pl.BlockSpec((half, samples), full),
            pl.BlockSpec((half, samples), full),
            pl.BlockSpec((chans, half), full),
            pl.BlockSpec((chans, chans), full),
            pl.BlockSpec((chans, half), full),
            pl.BlockSpec(time_weights.shape, full),
        ],
        out_specs=pl.BlockSpec((chans, samples), full),
        out_shape=jax.ShapeDtypeStruct((chans, samples), jnp.bfloat16),
        scratch_shapes=[
            pltpu.VMEM((chans, samples + 2 * lanes), jnp.bfloat16),
            pltpu.VMEM((chans, samples), jnp.float32),
        ],
        compiler_params=pltpu.CompilerParams(vmem_limit_bytes=48 * 1024 * 1024),
        cost_estimate=pl.CostEstimate(
            flops=2 * chans * samples * (chans + 2 * half + 3 * lanes),
            bytes_accessed=2 * samples * (2 * chans + 2 * half),
            transcendentals=chans,
        ),
    )(record, lo, hi, blo, bmid, bhi, time_weights)


def xor_sum(x, axis):
    count = lax.axis_size(axis)
    if count & (count - 1):
        return lax.psum(x, axis)
    step = 1
    while step < count:
        x = x + lax.ppermute(x, axis, [(i, i ^ step) for i in range(count)])
        step *= 2
    return x


def body(record, chan_taps, time_taps, sources):
    count_steps = record.shape[0]
    channels_here = record.shape[1]
    samples = record.shape[2]
    chan_table = chan_taps.astype(jnp.bfloat16)
    time_table = time_taps.astype(jnp.bfloat16)
    first_chan = lax.axis_index("chan") * channels_here
    selector = (
        (sources - first_chan)[:, :, None] == lax.iota(jnp.int32, channels_here)[None, None, :]
    ).astype(jnp.bfloat16)
    normalizer = 1.0 / math.sqrt(samples * lax.axis_size("win"))

    half = (chan_table.shape[0] - 1) // 2
    count = lax.axis_size("chan")
    band = band_matrix(chan_table, channels_here, channels_here + 2 * half)
    offset = lax.iota(jnp.int32, 384)[:, None] - 128 - lax.iota(jnp.int32, 128)[None, :]
    time_weights = tap_lookup(offset + (time_table.shape[0] - 1) // 2, time_table)

    heads = record[:, :half]
    tails = record[:, channels_here - half :]
    lowers = lax.ppermute(tails, "chan", [(i, i + 1) for i in range(count - 1)])
    uppers = lax.ppermute(heads, "chan", [(i + 1, i) for i in range(count - 1)])

    def prepare(whole, section):
        lower, upper = lowers[section], uppers[section]
        whitened = prepare_kernel(whole, section, lower, upper, band, time_weights)
        term = jnp.dot(selector[section], whitened, preferred_element_type=jnp.float32)
        return whitened, xor_sum(term.astype(jnp.bfloat16), "chan")

    pieces = [record] * count_steps
    results = []
    pending = prepare(pieces[0], 0)
    for section in range(count_steps):
        upcoming = None
        if section + 1 < count_steps:
            upcoming = prepare(pieces[section + 1], section + 1)
        whitened, panel = pending
        if section >= 2:
            whitened, panel, results[section - 2] = lax.optimization_barrier(
                (whitened, panel, results[section - 2])
            )
        if section + 1 < count_steps:
            partial_corr = correlate_kernel(whitened, panel)
            if section + 2 < count_steps:
                pieces[section + 2], partial_corr = lax.optimization_barrier(
                    (pieces[section + 2], partial_corr)
                )
            results.append(xor_sum(partial_corr, "win"))
        else:
            half = panel.shape[0] // 2
            parts = [
                xor_sum(correlate_kernel(whitened, panel[:half]), "win"),
                xor_sum(correlate_kernel(whitened, panel[half:]), "win"),
            ]
            results.append(jnp.concatenate(parts, axis=0))
        pending = upcoming
    lags = 2 * LAG + 1
    shaped = [total.reshape(-1, CORR_ROWS, channels_here)[:, :lags] for total in results]
    return jnp.stack(shaped) * normalizer


def solution(mesh):
    in_specs = (P(None, "chan", "win"), P(), P(), P())
    out_specs = P(None, None, None, "chan")
    return jax.shard_map(body, mesh=mesh, in_specs=in_specs, out_specs=out_specs, check_vma=False)
```

```python
import functools
import math

import jax
import jax.numpy as jnp
from jax import lax
from jax.experimental import pallas as pl
from jax.experimental.pallas import tpu as pltpu
from jax.sharding import PartitionSpec as P

LAG = 64
CORR_ROWS = 136


def padded_2(cells, sides, width):
    for axis, dim in sides:
        count = lax.axis_size(axis)
        ends = count - 1
        head = lax.slice_in_dim(cells, 0, width, axis=dim)
        tail = lax.slice_in_dim(cells, cells.shape[dim] - width, cells.shape[dim], axis=dim)
        cells = jnp.concatenate(
            [
                lax.ppermute(tail, axis, [(i, (i + 1) % count) for i in range(ends)]),
                cells,
                lax.ppermute(head, axis, [((i + 1) % count, i) for i in range(ends)]),
            ],
            axis=dim,
        )
    return cells


def tap_lookup(offset, tap_table):
    count_taps = tap_table.shape[0]
    marks = offset[..., None] == lax.iota(jnp.int32, count_taps)
    picked = jnp.where(marks, tap_table.astype(jnp.float32), jnp.zeros((), jnp.float32))
    return jnp.sum(picked, axis=-1).astype(tap_table.dtype)


def band_matrix(tap_table, height, breadth):
    offset = lax.iota(jnp.int32, breadth)[None, :] - lax.iota(jnp.int32, height)[:, None]
    return tap_lookup(offset, tap_table)


def time_filter(chan_pass, tap_table):
    channels_here, samples = chan_pass.shape
    half = (tap_table.shape[0] - 1) // 2
    blocks = chan_pass.reshape(channels_here, samples // 128, 128)
    zeros_block = jnp.zeros_like(blocks[:, :1])
    earlier = jnp.concatenate([zeros_block, blocks[:, :-1]], axis=1)
    later = jnp.concatenate([blocks[:, 1:], zeros_block], axis=1)
    extended = jnp.concatenate([earlier, blocks, later], axis=2)
    offset = lax.iota(jnp.int32, 384)[:, None] - 128 - lax.iota(jnp.int32, 128)[None, :] + half
    weights = tap_lookup(offset, tap_table)
    result = jnp.einsum("cbr,rt->cbt", extended, weights, preferred_element_type=jnp.float32)
    return result.reshape(channels_here, samples)


def whiten(time_pass):
    power = jnp.mean(time_pass * time_pass, axis=-1, keepdims=True)
    return (time_pass * lax.rsqrt(power + 1e-06)).astype(jnp.bfloat16)


def corr_body(nb, rows, w_ref, p_ref, o_ref, s_ref):
    n = pl.program_id(0)
    k_count = p_ref.shape[0]
    lanes = 128

    @pl.when(n == 0)
    def _():
        o_ref[...] = jnp.zeros_like(o_ref)

    j_idx = lax.broadcasted_iota(jnp.int32, (rows, lanes), 0)
    r_idx = lax.broadcasted_iota(jnp.int32, (rows, lanes), 1)
    upper = r_idx >= j_idx
    for k in range(k_count):
        rolled = []
        for b in range(nb + 1):
            start = pl.multiple_of((n * nb + b) * lanes, lanes)
            chunk = p_ref[pl.ds(k, 1), pl.ds(start, lanes)].astype(jnp.float32)
            wide = jnp.broadcast_to(chunk, (rows, lanes))
            rolled.append(pltpu.roll(wide, 0, 1, stride=1, stride_axis=0))
        for b in range(nb):
            piece = jnp.where(upper, rolled[b + 1], rolled[b])
            s_ref[pl.ds(k * rows, rows), pl.ds(b * lanes, lanes)] = piece.astype(s_ref.dtype)
    o_ref[...] += lax.dot_general(
        s_ref[...], w_ref[...], (((1,), (1,)), ((), ())),
        preferred_element_type=jnp.float32)


def correlate_kernel(whitened, panel, nb=32):
    chans, samples = whitened.shape
    k_count = panel.shape[0]
    lanes = 128
    rows = CORR_ROWS
    padded = jnp.pad(panel, ((0, 0), (LAG, LAG)))
    grid = samples // (nb * lanes)
    out = pl.pallas_call(
        functools.partial(corr_body, nb, rows),
        grid=(grid,),
        in_specs=[
            pl.BlockSpec((chans, nb * lanes), lambda n: (0, n)),
            pl.BlockSpec((k_count, samples + 2 * LAG), lambda n: (0, 0)),
        ],
        out_specs=pl.BlockSpec((k_count * rows, chans), lambda n: (0, 0)),
        out_shape=jax.ShapeDtypeStruct((k_count * rows, chans), jnp.float32),
        scratch_shapes=[pltpu.VMEM((k_count * rows, nb * lanes), jnp.bfloat16)],
        compiler_params=pltpu.CompilerParams(dimension_semantics=("arbitrary",)),
        cost_estimate=pl.CostEstimate(
            flops=2 * k_count * rows * samples * chans,
            bytes_accessed=2 * chans * samples + 2 * k_count * samples + 4 * k_count * rows * chans,
            transcendentals=0,
        ),
    )(whitened, padded)
    return out


def chan_filter(piece, tap_table):
    channels_here = piece.shape[0]
    half = (tap_table.shape[0] - 1) // 2
    widened = padded_2(piece, (("chan", 0),), half)
    total = jnp.dot(
        band_matrix(tap_table, channels_here, channels_here + 2 * half),
        widened,
        preferred_element_type=jnp.float32,
    )
    return total.astype(jnp.bfloat16)


def prep_body(section_chunk, rec_ref, lo_ref, hi_ref, blo_ref, bmid_ref, bhi_ref, tw_ref, o_ref, cp_ref, tp_ref):
    chans, samples = o_ref.shape
    lanes = 128
    cp_ref[:, pl.ds(0, lanes)] = jnp.zeros((chans, lanes), cp_ref.dtype)
    cp_ref[:, pl.ds(samples + lanes, lanes)] = jnp.zeros((chans, lanes), cp_ref.dtype)
    chunk = section_chunk

    def chan_step(i, carry):
        off = pl.multiple_of(i * chunk, chunk)
        total = jnp.dot(bmid_ref[...], rec_ref[0, :, pl.ds(off, chunk)], preferred_element_type=jnp.float32)
        total += jnp.dot(blo_ref[...], lo_ref[:, pl.ds(off, chunk)], preferred_element_type=jnp.float32)
        total += jnp.dot(bhi_ref[...], hi_ref[:, pl.ds(off, chunk)], preferred_element_type=jnp.float32)
        cp_ref[:, pl.ds(pl.multiple_of(off + lanes, lanes), chunk)] = total.astype(cp_ref.dtype)
        return carry

    lax.fori_loop(0, samples // chunk, chan_step, 0)

    group = 64

    def time_step(g, acc):
        base = g * group
        windows = [
            cp_ref[:, pl.ds(pl.multiple_of((base + q) * lanes, lanes), 3 * lanes)]
            for q in range(group)
        ]
        y = jnp.dot(jnp.concatenate(windows, axis=0), tw_ref[...], preferred_element_type=jnp.float32)
        for q in range(group):
            part = y[q * chans : (q + 1) * chans]
            tp_ref[:, pl.ds(pl.multiple_of((base + q) * lanes, lanes), lanes)] = part
            acc = acc + part * part
        return acc

    acc = lax.fori_loop(0, samples // (lanes * group), time_step, jnp.zeros((chans, lanes), jnp.float32))
    power = jnp.sum(acc, axis=1, keepdims=True) / samples
    scale = lax.rsqrt(power + 1e-06)

    def white_step(i, carry):
        off = pl.multiple_of(i * chunk, chunk)
        o_ref[:, pl.ds(off, chunk)] = (tp_ref[:, pl.ds(off, chunk)] * scale).astype(o_ref.dtype)
        return carry

    lax.fori_loop(0, samples // chunk, white_step, 0)


def prepare_kernel(record, section, lo, hi, band, time_weights):
    count_steps, chans, samples = record.shape
    half = lo.shape[0]
    lanes = 128
    chunk = 8192
    blo, bmid, bhi = band[:, :half], band[:, half:half + chans], band[:, half + chans:]
    full = lambda i: (0, 0)
    return pl.pallas_call(
        functools.partial(prep_body, chunk),
        grid=(1,),
        in_specs=[
            pl.BlockSpec((1, chans, samples), lambda i: (section, 0, 0)),
            pl.BlockSpec((half, samples), full),
            pl.BlockSpec((half, samples), full),
            pl.BlockSpec((chans, half), full),
            pl.BlockSpec((chans, chans), full),
            pl.BlockSpec((chans, half), full),
            pl.BlockSpec(time_weights.shape, full),
        ],
        out_specs=pl.BlockSpec((chans, samples), full),
        out_shape=jax.ShapeDtypeStruct((chans, samples), jnp.bfloat16),
        scratch_shapes=[
            pltpu.VMEM((chans, samples + 2 * lanes), jnp.bfloat16),
            pltpu.VMEM((chans, samples), jnp.float32),
        ],
        compiler_params=pltpu.CompilerParams(vmem_limit_bytes=48 * 1024 * 1024),
        cost_estimate=pl.CostEstimate(
            flops=2 * chans * samples * (chans + 2 * half + 3 * lanes),
            bytes_accessed=2 * samples * (2 * chans + 2 * half),
            transcendentals=chans,
        ),
    )(record, lo, hi, blo, bmid, bhi, time_weights)


def xor_sum(x, axis):
    count = lax.axis_size(axis)
    if count & (count - 1):
        return lax.psum(x, axis)
    step = 1
    while step < count:
        x = x + lax.ppermute(x, axis, [(i, i ^ step) for i in range(count)])
        step *= 2
    return x


def body(record, chan_taps, time_taps, sources):
    count_steps = record.shape[0]
    channels_here = record.shape[1]
    samples = record.shape[2]
    chan_table = chan_taps.astype(jnp.bfloat16)
    time_table = time_taps.astype(jnp.bfloat16)
    first_chan = lax.axis_index("chan") * channels_here
    selector = (
        (sources - first_chan)[:, :, None] == lax.iota(jnp.int32, channels_here)[None, None, :]
    ).astype(jnp.bfloat16)
    normalizer = 1.0 / math.sqrt(samples * lax.axis_size("win"))

    half = (chan_table.shape[0] - 1) // 2
    count = lax.axis_size("chan")
    band = band_matrix(chan_table, channels_here, channels_here + 2 * half)
    offset = lax.iota(jnp.int32, 384)[:, None] - 128 - lax.iota(jnp.int32, 128)[None, :]
    time_weights = tap_lookup(offset + (time_table.shape[0] - 1) // 2, time_table)

    heads = record[:, :half]
    tails = record[:, channels_here - half :]
    lowers = lax.ppermute(tails, "chan", [(i, i + 1) for i in range(count - 1)])
    uppers = lax.ppermute(heads, "chan", [(i + 1, i) for i in range(count - 1)])

    def prepare(whole, section):
        lower, upper = lowers[section], uppers[section]
        whitened = prepare_kernel(whole, section, lower, upper, band, time_weights)
        term = jnp.dot(selector[section], whitened, preferred_element_type=jnp.float32)
        return whitened, xor_sum(term.astype(jnp.bfloat16), "chan")

    pieces = [record] * count_steps
    results = []
    pending = prepare(pieces[0], 0)
    for section in range(count_steps):
        upcoming = None
        if section + 1 < count_steps:
            upcoming = prepare(pieces[section + 1], section + 1)
        whitened, panel = pending
        if section >= 2:
            whitened, panel, results[section - 2] = lax.optimization_barrier(
                (whitened, panel, results[section - 2])
            )
        if section + 1 < count_steps:
            partial_corr = correlate_kernel(whitened, panel)
            if section + 2 < count_steps:
                pieces[section + 2], partial_corr = lax.optimization_barrier(
                    (pieces[section + 2], partial_corr)
                )
            results.append(xor_sum(partial_corr, "win"))
        else:
            half = panel.shape[0] // 2
            parts = [
                xor_sum(correlate_kernel(whitened, panel[:half]), "win"),
                xor_sum(correlate_kernel(whitened, panel[half:]), "win"),
            ]
            results.append(jnp.concatenate(parts, axis=0))
        pending = upcoming
    lags = 2 * LAG + 1
    shaped = [total.reshape(-1, CORR_ROWS, channels_here)[:, :lags] for total in results]
    return jnp.stack(shaped) * normalizer


def solution(mesh):
    in_specs = (P(None, "chan", "win"), P(), P(), P())
    out_specs = P(None, None, None, "chan")
    return jax.shard_map(body, mesh=mesh, in_specs=in_specs, out_specs=out_specs, check_vma=False)
```

```python
import functools
import math

import jax
import jax.numpy as jnp
from jax import lax
from jax.experimental import pallas as pl
from jax.experimental.pallas import tpu as pltpu
from jax.sharding import PartitionSpec as P

LAG = 64
CORR_ROWS = 136


def padded_2(cells, sides, width):
    for axis, dim in sides:
        count = lax.axis_size(axis)
        ends = count - 1
        head = lax.slice_in_dim(cells, 0, width, axis=dim)
        tail = lax.slice_in_dim(cells, cells.shape[dim] - width, cells.shape[dim], axis=dim)
        cells = jnp.concatenate(
            [
                lax.ppermute(tail, axis, [(i, (i + 1) % count) for i in range(ends)]),
                cells,
                lax.ppermute(head, axis, [((i + 1) % count, i) for i in range(ends)]),
            ],
            axis=dim,
        )
    return cells


def tap_lookup(offset, tap_table):
    count_taps = tap_table.shape[0]
    marks = offset[..., None] == lax.iota(jnp.int32, count_taps)
    picked = jnp.where(marks, tap_table.astype(jnp.float32), jnp.zeros((), jnp.float32))
    return jnp.sum(picked, axis=-1).astype(tap_table.dtype)


def band_matrix(tap_table, height, breadth):
    offset = lax.iota(jnp.int32, breadth)[None, :] - lax.iota(jnp.int32, height)[:, None]
    return tap_lookup(offset, tap_table)


def time_filter(chan_pass, tap_table):
    channels_here, samples = chan_pass.shape
    half = (tap_table.shape[0] - 1) // 2
    blocks = chan_pass.reshape(channels_here, samples // 128, 128)
    zeros_block = jnp.zeros_like(blocks[:, :1])
    earlier = jnp.concatenate([zeros_block, blocks[:, :-1]], axis=1)
    later = jnp.concatenate([blocks[:, 1:], zeros_block], axis=1)
    extended = jnp.concatenate([earlier, blocks, later], axis=2)
    offset = lax.iota(jnp.int32, 384)[:, None] - 128 - lax.iota(jnp.int32, 128)[None, :] + half
    weights = tap_lookup(offset, tap_table)
    result = jnp.einsum("cbr,rt->cbt", extended, weights, preferred_element_type=jnp.float32)
    return result.reshape(channels_here, samples)


def whiten(time_pass):
    power = jnp.mean(time_pass * time_pass, axis=-1, keepdims=True)
    return (time_pass * lax.rsqrt(power + 1e-06)).astype(jnp.bfloat16)


def corr_body(nb, rows, w_ref, p_ref, o_ref, s_ref):
    n = pl.program_id(0)
    k_count = p_ref.shape[0]
    lanes = 128

    @pl.when(n == 0)
    def _():
        o_ref[...] = jnp.zeros_like(o_ref)

    j_idx = lax.broadcasted_iota(jnp.int32, (rows, lanes), 0)
    r_idx = lax.broadcasted_iota(jnp.int32, (rows, lanes), 1)
    upper = r_idx >= j_idx
    for k in range(k_count):
        rolled = []
        for b in range(nb + 1):
            start = pl.multiple_of((n * nb + b) * lanes, lanes)
            chunk = p_ref[pl.ds(k, 1), pl.ds(start, lanes)]
            wide = jnp.broadcast_to(chunk, (rows, lanes))
            rolled.append(pltpu.roll(wide, 0, 1, stride=1, stride_axis=0))
        for b in range(nb):
            piece = jnp.where(upper, rolled[b + 1], rolled[b])
            s_ref[pl.ds(k * rows, rows), pl.ds(b * lanes, lanes)] = piece.astype(s_ref.dtype)
    o_ref[...] += lax.dot_general(
        s_ref[...], w_ref[...], (((1,), (1,)), ((), ())),
        preferred_element_type=jnp.float32)


def correlate_kernel(whitened, panel, nb=64):
    chans, samples = whitened.shape
    k_count = panel.shape[0]
    lanes = 128
    rows = CORR_ROWS
    padded = jnp.pad(panel.astype(jnp.float32), ((0, 0), (LAG, LAG)))
    grid = samples // (nb * lanes)
    out = pl.pallas_call(
        functools.partial(corr_body, nb, rows),
        grid=(grid,),
        in_specs=[
            pl.BlockSpec((chans, nb * lanes), lambda n: (0, n)),
            pl.BlockSpec((k_count, samples + 2 * LAG), lambda n: (0, 0)),
        ],
        out_specs=pl.BlockSpec((k_count * rows, chans), lambda n: (0, 0)),
        out_shape=jax.ShapeDtypeStruct((k_count * rows, chans), jnp.float32),
        scratch_shapes=[pltpu.VMEM((k_count * rows, nb * lanes), jnp.bfloat16)],
        compiler_params=pltpu.CompilerParams(dimension_semantics=("arbitrary",)),
        cost_estimate=pl.CostEstimate(
            flops=2 * k_count * rows * samples * chans,
            bytes_accessed=2 * chans * samples + 4 * k_count * (samples + rows * chans),
            transcendentals=0,
        ),
    )(whitened, padded)
    return out


def chan_filter(piece, tap_table):
    channels_here = piece.shape[0]
    half = (tap_table.shape[0] - 1) // 2
    widened = padded_2(piece, (("chan", 0),), half)
    total = jnp.dot(
        band_matrix(tap_table, channels_here, channels_here + 2 * half),
        widened,
        preferred_element_type=jnp.float32,
    )
    return total.astype(jnp.bfloat16)


def prep_body(section_chunk, rec_ref, lo_ref, hi_ref, blo_ref, bmid_ref, bhi_ref, tw_ref, o_ref, cp_ref, tp_ref):
    chans, samples = o_ref.shape
    lanes = 128
    cp_ref[:, pl.ds(0, lanes)] = jnp.zeros((chans, lanes), cp_ref.dtype)
    cp_ref[:, pl.ds(samples + lanes, lanes)] = jnp.zeros((chans, lanes), cp_ref.dtype)
    chunk = section_chunk

    def chan_step(i, carry):
        off = pl.multiple_of(i * chunk, chunk)
        total = jnp.dot(bmid_ref[...], rec_ref[0, :, pl.ds(off, chunk)], preferred_element_type=jnp.float32)
        total += jnp.dot(blo_ref[...], lo_ref[:, pl.ds(off, chunk)], preferred_element_type=jnp.float32)
        total += jnp.dot(bhi_ref[...], hi_ref[:, pl.ds(off, chunk)], preferred_element_type=jnp.float32)
        cp_ref[:, pl.ds(pl.multiple_of(off + lanes, lanes), chunk)] = total.astype(cp_ref.dtype)
        return carry

    lax.fori_loop(0, samples // chunk, chan_step, 0)

    group = 64

    def time_step(g, acc):
        base = g * group
        windows = [
            cp_ref[:, pl.ds(pl.multiple_of((base + q) * lanes, lanes), 3 * lanes)]
            for q in range(group)
        ]
        y = jnp.dot(jnp.concatenate(windows, axis=0), tw_ref[...], preferred_element_type=jnp.float32)
        for q in range(group):
            part = y[q * chans : (q + 1) * chans]
            tp_ref[:, pl.ds(pl.multiple_of((base + q) * lanes, lanes), lanes)] = part
            acc = acc + part * part
        return acc

    acc = lax.fori_loop(0, samples // (lanes * group), time_step, jnp.zeros((chans, lanes), jnp.float32))
    power = jnp.sum(acc, axis=1, keepdims=True) / samples
    scale = lax.rsqrt(power + 1e-06)

    def white_step(i, carry):
        off = pl.multiple_of(i * chunk, chunk)
        o_ref[:, pl.ds(off, chunk)] = (tp_ref[:, pl.ds(off, chunk)] * scale).astype(o_ref.dtype)
        return carry

    lax.fori_loop(0, samples // chunk, white_step, 0)


def prepare_kernel(record, section, lo, hi, band, time_weights):
    count_steps, chans, samples = record.shape
    half = lo.shape[0]
    lanes = 128
    chunk = 8192
    blo, bmid, bhi = band[:, :half], band[:, half:half + chans], band[:, half + chans:]
    full = lambda i: (0, 0)
    return pl.pallas_call(
        functools.partial(prep_body, chunk),
        grid=(1,),
        in_specs=[
            pl.BlockSpec((1, chans, samples), lambda i: (section, 0, 0)),
            pl.BlockSpec((half, samples), full),
            pl.BlockSpec((half, samples), full),
            pl.BlockSpec((chans, half), full),
            pl.BlockSpec((chans, chans), full),
            pl.BlockSpec((chans, half), full),
            pl.BlockSpec(time_weights.shape, full),
        ],
        out_specs=pl.BlockSpec((chans, samples), full),
        out_shape=jax.ShapeDtypeStruct((chans, samples), jnp.bfloat16),
        scratch_shapes=[
            pltpu.VMEM((chans, samples + 2 * lanes), jnp.bfloat16),
            pltpu.VMEM((chans, samples), jnp.float32),
        ],
        compiler_params=pltpu.CompilerParams(vmem_limit_bytes=48 * 1024 * 1024),
        cost_estimate=pl.CostEstimate(
            flops=2 * chans * samples * (chans + 2 * half + 3 * lanes),
            bytes_accessed=2 * samples * (2 * chans + 2 * half),
            transcendentals=chans,
        ),
    )(record, lo, hi, blo, bmid, bhi, time_weights)


def xor_sum(x, axis):
    count = lax.axis_size(axis)
    if count & (count - 1):
        return lax.psum(x, axis)
    step = 1
    while step < count:
        x = x + lax.ppermute(x, axis, [(i, i ^ step) for i in range(count)])
        step *= 2
    return x


def body(record, chan_taps, time_taps, sources):
    count_steps = record.shape[0]
    channels_here = record.shape[1]
    samples = record.shape[2]
    chan_table = chan_taps.astype(jnp.bfloat16)
    time_table = time_taps.astype(jnp.bfloat16)
    first_chan = lax.axis_index("chan") * channels_here
    selector = (
        (sources - first_chan)[:, :, None] == lax.iota(jnp.int32, channels_here)[None, None, :]
    ).astype(jnp.bfloat16)
    normalizer = 1.0 / math.sqrt(samples * lax.axis_size("win"))

    half = (chan_table.shape[0] - 1) // 2
    count = lax.axis_size("chan")
    band = band_matrix(chan_table, channels_here, channels_here + 2 * half)
    offset = lax.iota(jnp.int32, 384)[:, None] - 128 - lax.iota(jnp.int32, 128)[None, :]
    time_weights = tap_lookup(offset + (time_table.shape[0] - 1) // 2, time_table)

    heads = record[:, :half]
    tails = record[:, channels_here - half :]
    lowers = lax.ppermute(tails, "chan", [(i, i + 1) for i in range(count - 1)])
    uppers = lax.ppermute(heads, "chan", [(i + 1, i) for i in range(count - 1)])

    def prepare(whole, section):
        lower, upper = lowers[section], uppers[section]
        whitened = prepare_kernel(whole, section, lower, upper, band, time_weights)
        term = jnp.dot(selector[section], whitened, preferred_element_type=jnp.float32)
        return whitened, xor_sum(term.astype(jnp.bfloat16), "chan")

    pieces = [record] * count_steps
    results = []
    pending = prepare(pieces[0], 0)
    for section in range(count_steps):
        upcoming = None
        if section + 1 < count_steps:
            upcoming = prepare(pieces[section + 1], section + 1)
        whitened, panel = pending
        if section >= 2:
            whitened, panel, results[section - 2] = lax.optimization_barrier(
                (whitened, panel, results[section - 2])
            )
        if section + 1 < count_steps:
            partial_corr = correlate_kernel(whitened, panel)
            if section + 2 < count_steps:
                pieces[section + 2], partial_corr = lax.optimization_barrier(
                    (pieces[section + 2], partial_corr)
                )
            results.append(xor_sum(partial_corr, "win"))
        else:
            half = panel.shape[0] // 2
            parts = [
                xor_sum(correlate_kernel(whitened, panel[:half]), "win"),
                xor_sum(correlate_kernel(whitened, panel[half:]), "win"),
            ]
            results.append(jnp.concatenate(parts, axis=0))
        pending = upcoming
    lags = 2 * LAG + 1
    shaped = [total.reshape(-1, CORR_ROWS, channels_here)[:, :lags] for total in results]
    return jnp.stack(shaped) * normalizer


def solution(mesh):
    in_specs = (P(None, "chan", "win"), P(), P(), P())
    out_specs = P(None, None, None, "chan")
    return jax.shard_map(body, mesh=mesh, in_specs=in_specs, out_specs=out_specs, check_vma=False)
```
